32 devices in a mesh: slab: 2 (over x), run: 2 (over core), tx: 8 (over z, y).
Axes of the slice: x: 2, y: 2, z: 4, core: 2. Of those that a mesh axis runs over, the one named last changes fastest.
Arguments:
- snapshots: bfloat16 [1024, 128, 512], P(('slab', 'tx'), None, 'run'), parts along dimension 0, may hold values from -60 to 60, as said below
- coefficient: float32 [1024, 128], P(('slab', 'tx')), parts along dimension 0, may hold values from 0.02 to 0.2
- start_first: int32 [512, 128], replicated, may hold values from -4 to 4
- start_merge: int32 [256, 128], replicated, may hold values from -4 to 4
Outputs:
- modes: float32 [1024, 128, 128], P(('slab', 'tx'), None, 'run'), parts along dimension 0
The draws below stay inside these ranges and needn't reach their ends.
There are 2 independent parts, one for each index of `slab`. The reference program is written for one: setup_inputs(seed, part) draws one part's arguments, and reference() takes and returns one part's arrays. A program takes and returns all parts, laid end to end along the dimension named above; an argument that names none is the same for every part. Nothing has to cross between parts.
Inputs may be any that keep to these rules, and one draw needn't show every extreme that they name: `snapshots`: snapshot values are real-valued and bounded.
All inputs are finite; a program needn't handle non-finite values.
Results may differ from the reference program's by a relative error of at most 0.0003.
Values may be sent and summed in bfloat16 or wider, within the bound.
No kernel may reach another device: no remote copies, remote signals or barrier semaphores. Data moves between devices by JAX's collectives and lax.ppermute only.
A program may use at most 128 MiB of HBM per device.

```python
import math
import jax
import jax.numpy as jnp
from jax import lax

S_RUN = 256
K = 128
ITERS = 2
NX = 512
NY = 128
SNAPS = 512
NCELLS = 65536
N_RUN = 2


def draw_snapshots(key, part):
    key_base = jax.random.fold_in(key, 11)
    key_cells = jax.random.fold_in(key, 12)
    key_snaps = jax.random.fold_in(key, 13)
    base_field = jax.random.truncated_normal(key_base, -4.0, 4.0, (NX, NY, SNAPS + 1), jnp.float32)
    mixed = base_field[:, :, :-1] + 0.7 * base_field[:, :, 1:]
    cell_scale = jnp.exp(jax.random.uniform(key_cells, (NX, NY, 1), jnp.float32, 0.0, math.log(4.0)))
    snap_scale = jnp.exp(jax.random.uniform(key_snaps, (1, 1, SNAPS), jnp.float32, 0.0, math.log(2.0)))
    field = mixed * cell_scale * snap_scale
    return field.astype(jnp.bfloat16)


def plant(array, key, smallest, high):
    longest = array.shape.index(max(array.shape))
    spots = []
    for shift in (0, 1):
        where = [jax.random.randint(jax.random.fold_in(key, axis), (), 0, length) for axis, length in enumerate(array.shape)]
        where[longest] = (where[longest] + shift) % array.shape[longest]
        spots.append(tuple(where))
    return array.at[spots[0]].set(smallest).at[spots[1]].set(high)


def shard_levels(own_key, dims, cuts, smallest, top_value):
    def one(position, blocks):
        heights = jax.random.uniform(jax.random.fold_in(jax.random.fold_in(own_key, 6), position), (blocks,), jnp.float32, smallest / len(cuts), top_value / len(cuts))
        return jnp.repeat(jnp.exp(heights), dims[position] // blocks).reshape((-1,) + (1,) * (len(dims) - position - 1))

    level = one(*cuts[0])
    for cut in cuts[1:]:
        level = level * one(*cut)
    return level


def setup_inputs(seed: int = 0, part: int = 0) -> dict:
    keys = jax.random.split(jax.random.key(seed), 5)
    part_keys = jax.random.split(jax.random.fold_in(keys[4], part), 5)
    return {
        "snapshots": draw_snapshots(jax.random.fold_in(jax.random.fold_in(keys[4], part), 71), part),
        "coefficient": jnp.clip(jnp.exp(math.log(0.2) - 2.3025851 * jax.random.uniform(part_keys[1], (NX, NY), jnp.float32) ** shard_levels(part_keys[1], (NX, NY), ((0, 8),), -0.2, 0.2)), 0.02, 0.2),
        "start_first": plant(jax.random.randint(keys[2], (SNAPS, K), -4, 5), jax.random.fold_in(keys[2], 1), -4, 4).astype(jnp.int32),
        "start_merge": plant(jax.random.randint(keys[3], (2 * K, K), -4, 5), jax.random.fold_in(keys[3], 1), -4, 4).astype(jnp.int32),
    }


highest = lax.Precision.HIGHEST

def fourth_order(values, axis_dim):
    length_kept = values.shape[axis_dim] - 4

    def shifted(offset):
        return lax.slice_in_dim(values, offset, offset + length_kept, axis=axis_dim)
    return (8.0 * (shifted(3) - shifted(1)) - (shifted(4) - shifted(0))) / 12.0

def fluxes(extended, coefficient):
    squared = 0.5 * jnp.square(extended.astype(jnp.float32))
    along_rows = fourth_order(squared, 0)
    padded = jnp.pad(squared[2:-2], ((0, 0), (2, 2), (0, 0)))
    along_cols = fourth_order(padded, 1)
    central = extended[2:-2].astype(jnp.float32)
    return central - coefficient[:, :, None] * (along_rows + along_cols)

def orthonormal(matrix):
    inner_gram = jnp.dot(matrix.T, matrix, precision=highest)
    factor = jnp.linalg.cholesky(inner_gram)
    return jax.scipy.linalg.solve_triangular(factor, matrix.T, lower=True).T

def iterate(gram_matrix, start_int):
    basis_set = orthonormal(start_int.astype(jnp.float32))
    for sweep_index in range(ITERS):
        basis_set = orthonormal(jnp.dot(gram_matrix, basis_set, precision=highest))
    return basis_set

def reference(snapshots, coefficient, start_first, start_merge):
    extended = jnp.pad(snapshots, ((2, 2), (0, 0), (0, 0)))
    columns = []
    for member in range(N_RUN):
        segment = extended[:, :, member * S_RUN:(member + 1) * S_RUN]
        flux_rows = fluxes(segment, coefficient).reshape(NX * NY, S_RUN)
        gram_matrix = jnp.dot(flux_rows.T, flux_rows, precision=highest) / NCELLS
        basis_set = iterate(gram_matrix, start_first[member * S_RUN:(member + 1) * S_RUN])
        columns.append(jnp.dot(flux_rows, basis_set, precision=highest))
    merged = jnp.concatenate(columns, axis=1)
    merge_gram = jnp.dot(merged.T, merged, precision=highest) / NCELLS
    rotation = iterate(merge_gram, start_merge)
    return jnp.dot(merged, rotation, precision=highest).reshape(NX, NY, K)
```

```python
import jax
import jax.numpy as jnp
from jax import lax
from jax.sharding import PartitionSpec as P

ITERS = 2


highest = lax.Precision.HIGHEST


def padded_2(block, sides, width):
    for axis, dim in sides:
        count = lax.axis_size(axis)
        forward = [(i, i + 1) for i in range(count - 1)]
        backward = [(target, source) for source, target in forward]
        low = lax.ppermute(
            lax.slice_in_dim(block, block.shape[dim] - width, None, axis=dim), axis, forward
        )
        high = lax.ppermute(lax.slice_in_dim(block, 0, width, axis=dim), axis, backward)
        block = jnp.concatenate([low, block, high], axis=dim)
    return block


def partner(block, axis, stride):
    count = lax.axis_size(axis)
    route = []
    for low in range(count):
        high = low | 1 << stride
        if high != low and high < count:
            route += [(low, high), (high, low)]
    return lax.ppermute(block, axis, route)


def tree_sum(value, axis):
    count = lax.axis_size(axis)
    if count & (count - 1):
        return lax.psum(value, axis)
    step = 1
    while step < count:
        route = [(i, i ^ step) for i in range(count)]
        value = value + lax.ppermute(value, axis, route)
        step *= 2
    return value


def fourth_order(values, axis_dim):
    length_kept = values.shape[axis_dim] - 4

    def shifted(offset):
        return lax.slice_in_dim(values, offset, offset + length_kept, axis=axis_dim)

    return (8.0 * (shifted(3) - shifted(1)) - (shifted(4) - shifted(0))) / 12.0


def fluxes(extended, coefficient):
    squared = 0.5 * jnp.square(extended.astype(jnp.float32))
    along_rows = fourth_order(squared, 0)
    padded = jnp.pad(squared[2:-2], ((0, 0), (2, 2), (0, 0)))
    along_cols = fourth_order(padded, 1)
    central = extended[2:-2].astype(jnp.float32)
    return central - coefficient[:, :, None] * (along_rows + along_cols)


def orthonormal(matrix):
    inner_gram = jnp.dot(matrix.T, matrix, precision=highest)
    factor = jnp.linalg.cholesky(inner_gram)
    return jax.scipy.linalg.solve_triangular(factor, matrix.T, lower=True).T


def iterate(gram_matrix, basis_set):
    for sweep_index in range(ITERS):
        basis_set = orthonormal(jnp.dot(gram_matrix, basis_set, precision=highest))
    return basis_set


def cross_gram(left_rows, right_rows):
    return lax.dot_general(left_rows, right_rows, (((0,), (0,)), ((), ())), precision=highest)


def on_device(snapshots, coefficient, start_first, start_merge):
    extended = padded_2(snapshots, (("tx", 0),), 2)
    rows_here = snapshots.shape[0] * snapshots.shape[1]
    order_size = snapshots.shape[2]
    modes_count = start_first.shape[1]
    share_count = modes_count // lax.axis_size("run")
    cells_total = rows_here * lax.axis_size("tx")
    member = lax.axis_index("run")
    is_first = member == 0
    own_start = lax.dynamic_slice_in_dim(start_first, member * order_size, order_size, 0)
    first_basis = orthonormal(own_start.astype(jnp.float32))
    merge_basis = orthonormal(start_merge.astype(jnp.float32))
    own_flux = fluxes(extended, coefficient).reshape(rows_here, order_size)
    own_gram = tree_sum(cross_gram(own_flux, own_flux), "tx") / cells_total
    own_basis = iterate(own_gram, first_basis)
    own_modes = jnp.dot(own_flux, own_basis, precision=highest)
    other_modes = partner(own_modes, "run", 0)
    own_block = cross_gram(own_modes, own_modes)
    half_rows = rows_here // 2
    half_start = member * half_rows
    mixed_half = cross_gram(
        lax.dynamic_slice_in_dim(own_modes, half_start, half_rows, 0),
        lax.dynamic_slice_in_dim(other_modes, half_start, half_rows, 0),
    )
    mixed_half = jnp.where(is_first, mixed_half, mixed_half.T)
    summed = tree_sum(jnp.stack([own_block, mixed_half]), "tx")
    swapped = partner(summed, "run", 0)
    own_block = summed[0] / cells_total
    other_block = swapped[0] / cells_total
    mixed_block = (summed[1] + swapped[1]) / cells_total
    first_block = jnp.where(is_first, own_block, other_block)
    last_block = jnp.where(is_first, other_block, own_block)
    merge_gram = jnp.concatenate(
        [
            jnp.concatenate([first_block, mixed_block], axis=1),
            jnp.concatenate([mixed_block.T, last_block], axis=1),
        ],
        axis=0,
    )
    rotation = iterate(merge_gram, merge_basis)
    rotation_share = lax.dynamic_slice_in_dim(rotation, member * share_count, share_count, 1)
    top_rows = rotation_share[:modes_count]
    bottom_rows = rotation_share[modes_count:]
    own_rotation = jnp.where(is_first, top_rows, bottom_rows)
    other_rotation = jnp.where(is_first, bottom_rows, top_rows)
    result = jnp.dot(own_modes, own_rotation, precision=highest) + jnp.dot(
        other_modes, other_rotation, precision=highest
    )
    return result.reshape(snapshots.shape[0], snapshots.shape[1], share_count)


def solution(mesh):
    in_specs = (P(("slab", "tx"), None, "run"), P(("slab", "tx"), None), P(), P())
    out_specs = P(("slab", "tx"), None, "run")
    return jax.shard_map(
        on_device, mesh=mesh, in_specs=in_specs, out_specs=out_specs, check_vma=False
    )
```

```python
import jax
import jax.numpy as jnp
from jax import lax
from jax.sharding import PartitionSpec as P
from jax.experimental import pallas as pl

ITERS = 2


highest = lax.Precision.HIGHEST


def padded_2(block, sides, width):
    for axis, dim in sides:
        count = lax.axis_size(axis)
        forward = [(i, i + 1) for i in range(count - 1)]
        backward = [(target, source) for source, target in forward]
        low = lax.ppermute(
            lax.slice_in_dim(block, block.shape[dim] - width, None, axis=dim), axis, forward
        )
        high = lax.ppermute(lax.slice_in_dim(block, 0, width, axis=dim), axis, backward)
        block = jnp.concatenate([low, block, high], axis=dim)
    return block


def partner(block, axis, stride):
    count = lax.axis_size(axis)
    route = []
    for low in range(count):
        high = low | 1 << stride
        if high != low and high < count:
            route += [(low, high), (high, low)]
    return lax.ppermute(block, axis, route)


def tree_sum(value, axis):
    count = lax.axis_size(axis)
    if count & (count - 1):
        return lax.psum(value, axis)
    step = 1
    while step < count:
        route = [(i, i ^ step) for i in range(count)]
        value = value + lax.ppermute(value, axis, route)
        step *= 2
    return value


def fourth_order(values, axis_dim):
    length_kept = values.shape[axis_dim] - 4

    def shifted(offset):
        return lax.slice_in_dim(values, offset, offset + length_kept, axis=axis_dim)

    return (8.0 * (shifted(3) - shifted(1)) - (shifted(4) - shifted(0))) / 12.0


def fluxes(extended, coefficient):
    squared = 0.5 * jnp.square(extended.astype(jnp.float32))
    along_rows = fourth_order(squared, 0)
    padded = jnp.pad(squared[2:-2], ((0, 0), (2, 2), (0, 0)))
    along_cols = fourth_order(padded, 1)
    central = extended[2:-2].astype(jnp.float32)
    return central - coefficient[:, :, None] * (along_rows + along_cols)


def gram_schmidt_kernel(rows_ref, out_ref):
    count, width = rows_ref.shape
    chunks = [rows_ref[i * 8:(i + 1) * 8, :] for i in range(count // 8)]
    for j in range(count):
        block, lane_row = divmod(j, 8)
        vector = chunks[block][lane_row:lane_row + 1, :]
        inverse = 1.0 / jnp.sum(vector * vector, axis=1, keepdims=True)
        for i in range(block, count // 8):
            rows = chunks[i]
            weight = jnp.sum(rows * vector, axis=1, keepdims=True) * inverse
            if i == block:
                ids = lax.broadcasted_iota(jnp.int32, weight.shape, 0)
                weight = jnp.where(ids > lane_row, weight, 0.0)
            chunks[i] = rows - weight * vector
    for i in range(count // 8):
        rows = chunks[i]
        norm = jnp.sqrt(jnp.sum(rows * rows, axis=1, keepdims=True))
        out_ref[i * 8:(i + 1) * 8, :] = rows / norm


def orthonormal(matrix):
    rows = matrix.T
    done = pl.pallas_call(
        gram_schmidt_kernel, out_shape=jax.ShapeDtypeStruct(rows.shape, jnp.float32)
    )(rows)
    return done.T


def iterate(gram_matrix, basis_set):
    for sweep_index in range(ITERS):
        basis_set = orthonormal(jnp.dot(gram_matrix, basis_set, precision=highest))
    return basis_set


def cross_gram(left_rows, right_rows):
    return lax.dot_general(left_rows, right_rows, (((0,), (0,)), ((), ())), precision=highest)


def on_device(snapshots, coefficient, start_first, start_merge):
    extended = padded_2(snapshots, (("tx", 0),), 2)
    rows_here = snapshots.shape[0] * snapshots.shape[1]
    order_size = snapshots.shape[2]
    modes_count = start_first.shape[1]
    share_count = modes_count // lax.axis_size("run")
    cells_total = rows_here * lax.axis_size("tx")
    member = lax.axis_index("run")
    is_first = member == 0
    own_start = lax.dynamic_slice_in_dim(start_first, member * order_size, order_size, 0)
    first_basis = orthonormal(own_start.astype(jnp.float32))
    merge_basis = orthonormal(start_merge.astype(jnp.float32))
    own_flux = fluxes(extended, coefficient).reshape(rows_here, order_size)
    own_gram = tree_sum(cross_gram(own_flux, own_flux), "tx") / cells_total
    own_basis = iterate(own_gram, first_basis)
    own_modes = jnp.dot(own_flux, own_basis, precision=highest)
    other_modes = partner(own_modes, "run", 0)
    own_block = cross_gram(own_modes, own_modes)
    half_rows = rows_here // 2
    half_start = member * half_rows
    mixed_half = cross_gram(
        lax.dynamic_slice_in_dim(own_modes, half_start, half_rows, 0),
        lax.dynamic_slice_in_dim(other_modes, half_start, half_rows, 0),
    )
    mixed_half = jnp.where(is_first, mixed_half, mixed_half.T)
    summed = tree_sum(jnp.stack([own_block, mixed_half]), "tx")
    swapped = partner(summed, "run", 0)
    own_block = summed[0] / cells_total
    other_block = swapped[0] / cells_total
    mixed_block = (summed[1] + swapped[1]) / cells_total
    first_block = jnp.where(is_first, own_block, other_block)
    last_block = jnp.where(is_first, other_block, own_block)
    merge_gram = jnp.concatenate(
        [
            jnp.concatenate([first_block, mixed_block], axis=1),
            jnp.concatenate([mixed_block.T, last_block], axis=1),
        ],
        axis=0,
    )
    rotation = iterate(merge_gram, merge_basis)
    rotation_share = lax.dynamic_slice_in_dim(rotation, member * share_count, share_count, 1)
    top_rows = rotation_share[:modes_count]
    bottom_rows = rotation_share[modes_count:]
    own_rotation = jnp.where(is_first, top_rows, bottom_rows)
    other_rotation = jnp.where(is_first, bottom_rows, top_rows)
    result = jnp.dot(own_modes, own_rotation, precision=highest) + jnp.dot(
        other_modes, other_rotation, precision=highest
    )
    return result.reshape(snapshots.shape[0], snapshots.shape[1], share_count)


def solution(mesh):
    in_specs = (P(("slab", "tx"), None, "run"), P(("slab", "tx"), None), P(), P())
    out_specs = P(("slab", "tx"), None, "run")
    return jax.shard_map(
        on_device, mesh=mesh, in_specs=in_specs, out_specs=out_specs, check_vma=False
    )
```

```python
import jax
import jax.numpy as jnp
from jax import lax
from jax.sharding import PartitionSpec as P
from jax.experimental import pallas as pl

ITERS = 2


highest = lax.Precision.HIGHEST
high = lax.Precision.HIGH


def padded_2(block, sides, width):
    for axis, dim in sides:
        count = lax.axis_size(axis)
        forward = [(i, i + 1) for i in range(count - 1)]
        backward = [(target, source) for source, target in forward]
        low = lax.ppermute(
            lax.slice_in_dim(block, block.shape[dim] - width, None, axis=dim), axis, forward
        )
        high = lax.ppermute(lax.slice_in_dim(block, 0, width, axis=dim), axis, backward)
        block = jnp.concatenate([low, block, high], axis=dim)
    return block


def partner(block, axis, stride):
    count = lax.axis_size(axis)
    route = []
    for low in range(count):
        high = low | 1 << stride
        if high != low and high < count:
            route += [(low, high), (high, low)]
    return lax.ppermute(block, axis, route)


def tree_sum(value, axis):
    count = lax.axis_size(axis)
    if count & (count - 1):
        return lax.psum(value, axis)
    step = 1
    while step < count:
        route = [(i, i ^ step) for i in range(count)]
        value = value + lax.ppermute(value, axis, route)
        step *= 2
    return value


def fourth_order(values, axis_dim):
    length_kept = values.shape[axis_dim] - 4

    def shifted(offset):
        return lax.slice_in_dim(values, offset, offset + length_kept, axis=axis_dim)

    return (8.0 * (shifted(3) - shifted(1)) - (shifted(4) - shifted(0))) / 12.0


def fluxes(extended, coefficient):
    squared = 0.5 * jnp.square(extended.astype(jnp.float32))
    along_rows = fourth_order(squared, 0)
    padded = jnp.pad(squared[2:-2], ((0, 0), (2, 2), (0, 0)))
    along_cols = fourth_order(padded, 1)
    central = extended[2:-2].astype(jnp.float32)
    return central - coefficient[:, :, None] * (along_rows + along_cols)


def gram_schmidt_kernel(rows_ref, out_ref):
    count, width = rows_ref.shape
    chunks = [rows_ref[i * 8:(i + 1) * 8, :] for i in range(count // 8)]
    for j in range(count):
        block, lane_row = divmod(j, 8)
        vector = chunks[block][lane_row:lane_row + 1, :]
        inverse = 1.0 / jnp.sum(vector * vector, axis=1, keepdims=True)
        for i in range(block, count // 8):
            rows = chunks[i]
            weight = jnp.sum(rows * vector, axis=1, keepdims=True) * inverse
            if i == block:
                ids = lax.broadcasted_iota(jnp.int32, weight.shape, 0)
                weight = jnp.where(ids > lane_row, weight, 0.0)
            chunks[i] = rows - weight * vector
    for i in range(count // 8):
        rows = chunks[i]
        norm = jnp.sqrt(jnp.sum(rows * rows, axis=1, keepdims=True))
        out_ref[i * 8:(i + 1) * 8, :] = rows / norm


def orthonormal(matrix):
    rows = matrix.T
    done = pl.pallas_call(
        gram_schmidt_kernel, out_shape=jax.ShapeDtypeStruct(rows.shape, jnp.float32)
    )(rows)
    return done.T


def iterate(gram_matrix, basis_set):
    for sweep_index in range(ITERS):
        basis_set = orthonormal(jnp.dot(gram_matrix, basis_set, precision=highest))
    return basis_set


def cross_gram(left_rows, right_rows):
    return lax.dot_general(left_rows, right_rows, (((0,), (0,)), ((), ())), precision=high)


def self_gram(rows):
    upper = lax.reduce_precision(rows, exponent_bits=8, mantissa_bits=7)
    lower = lax.reduce_precision(rows - upper, exponent_bits=8, mantissa_bits=7)
    missing = jnp.sum(lower * lower, axis=0)
    return cross_gram(rows, rows) + jnp.diag(missing)


def on_device(snapshots, coefficient, start_first, start_merge):
    extended = padded_2(snapshots, (("tx", 0),), 2)
    rows_here = snapshots.shape[0] * snapshots.shape[1]
    order_size = snapshots.shape[2]
    modes_count = start_first.shape[1]
    share_count = modes_count // lax.axis_size("run")
    cells_total = rows_here * lax.axis_size("tx")
    member = lax.axis_index("run")
    is_first = member == 0
    own_start = lax.dynamic_slice_in_dim(start_first, member * order_size, order_size, 0)
    first_basis = orthonormal(own_start.astype(jnp.float32))
    merge_basis = orthonormal(start_merge.astype(jnp.float32))
    own_flux = fluxes(extended, coefficient).reshape(rows_here, order_size)
    own_gram = tree_sum(self_gram(own_flux), "tx") / cells_total
    own_basis = iterate(own_gram, first_basis)
    own_modes = jnp.dot(own_flux, own_basis, precision=high)
    other_modes = partner(own_modes, "run", 0)
    own_block = self_gram(own_modes)
    half_rows = rows_here // 2
    half_start = member * half_rows
    mixed_half = cross_gram(
        lax.dynamic_slice_in_dim(own_modes, half_start, half_rows, 0),
        lax.dynamic_slice_in_dim(other_modes, half_start, half_rows, 0),
    )
    mixed_half = jnp.where(is_first, mixed_half, mixed_half.T)
    summed = tree_sum(jnp.stack([own_block, mixed_half]), "tx")
    swapped = partner(summed, "run", 0)
    own_block = summed[0] / cells_total
    other_block = swapped[0] / cells_total
    mixed_block = (summed[1] + swapped[1]) / cells_total
    first_block = jnp.where(is_first, own_block, other_block)
    last_block = jnp.where(is_first, other_block, own_block)
    merge_gram = jnp.concatenate(
        [
            jnp.concatenate([first_block, mixed_block], axis=1),
            jnp.concatenate([mixed_block.T, last_block], axis=1),
        ],
        axis=0,
    )
    rotation = iterate(merge_gram, merge_basis)
    rotation_share = lax.dynamic_slice_in_dim(rotation, member * share_count, share_count, 1)
    top_rows = rotation_share[:modes_count]
    bottom_rows = rotation_share[modes_count:]
    own_rotation = jnp.where(is_first, top_rows, bottom_rows)
    other_rotation = jnp.where(is_first, bottom_rows, top_rows)
    result = jnp.dot(own_modes, own_rotation, precision=high) + jnp.dot(
        other_modes, other_rotation, precision=high
    )
    return result.reshape(snapshots.shape[0], snapshots.shape[1], share_count)


def solution(mesh):
    in_specs = (P(("slab", "tx"), None, "run"), P(("slab", "tx"), None), P(), P())
    out_specs = P(("slab", "tx"), None, "run")
    return jax.shard_map(
        on_device, mesh=mesh, in_specs=in_specs, out_specs=out_specs, check_vma=False
    )
```

```python
import jax
import jax.numpy as jnp
from jax import lax
from jax.sharding import PartitionSpec as P
from jax.experimental import pallas as pl

ITERS = 2


highest = lax.Precision.HIGHEST
high = lax.Precision.HIGH


def padded_2(block, sides, width):
    for axis, dim in sides:
        count = lax.axis_size(axis)
        forward = [(i, i + 1) for i in range(count - 1)]
        backward = [(target, source) for source, target in forward]
        low = lax.ppermute(
            lax.slice_in_dim(block, block.shape[dim] - width, None, axis=dim), axis, forward
        )
        high = lax.ppermute(lax.slice_in_dim(block, 0, width, axis=dim), axis, backward)
        block = jnp.concatenate([low, block, high], axis=dim)
    return block


def partner(block, axis, stride):
    count = lax.axis_size(axis)
    route = []
    for low in range(count):
        high = low | 1 << stride
        if high != low and high < count:
            route += [(low, high), (high, low)]
    return lax.ppermute(block, axis, route)


def tree_sum(value, axis):
    count = lax.axis_size(axis)
    if count & (count - 1):
        return lax.psum(value, axis)
    step = 1
    while step < count:
        route = [(i, i ^ step) for i in range(count)]
        value = value + lax.ppermute(value, axis, route)
        step *= 2
    return value


def fourth_order(values, axis_dim):
    length_kept = values.shape[axis_dim] - 4

    def shifted(offset):
        return lax.slice_in_dim(values, offset, offset + length_kept, axis=axis_dim)

    return (8.0 * (shifted(3) - shifted(1)) - (shifted(4) - shifted(0))) / 12.0


def fluxes(extended, coefficient):
    squared = 0.5 * jnp.square(extended.astype(jnp.float32))
    along_rows = fourth_order(squared, 0)
    padded = jnp.pad(squared[2:-2], ((0, 0), (2, 2), (0, 0)))
    along_cols = fourth_order(padded, 1)
    central = extended[2:-2].astype(jnp.float32)
    return central - coefficient[:, :, None] * (along_rows + along_cols)


def gram_schmidt_kernel(rows_ref, out_ref):
    count, width = rows_ref.shape
    chunks = [rows_ref[i * 8:(i + 1) * 8, :] for i in range(count // 8)]
    for j in range(count):
        block, lane_row = divmod(j, 8)
        vector = chunks[block][lane_row:lane_row + 1, :]
        inverse = 1.0 / jnp.sum(vector * vector, axis=1, keepdims=True)
        for i in range(block, count // 8):
            rows = chunks[i]
            weight = jnp.sum(rows * vector, axis=1, keepdims=True) * inverse
            if i == block:
                ids = lax.broadcasted_iota(jnp.int32, weight.shape, 0)
                weight = jnp.where(ids > lane_row, weight, 0.0)
            chunks[i] = rows - weight * vector
    for i in range(count // 8):
        rows = chunks[i]
        norm = jnp.sqrt(jnp.sum(rows * rows, axis=1, keepdims=True))
        out_ref[i * 8:(i + 1) * 8, :] = rows / norm


def orthonormal(matrix):
    rows = matrix.T
    done = pl.pallas_call(
        gram_schmidt_kernel, out_shape=jax.ShapeDtypeStruct(rows.shape, jnp.float32)
    )(rows)
    return done.T


def iterate(gram_matrix, basis_set):
    for sweep_index in range(ITERS):
        basis_set = orthonormal(jnp.dot(gram_matrix, basis_set, precision=highest))
    return basis_set


def cross_gram(left_rows, right_rows):
    return lax.dot_general(left_rows, right_rows, (((0,), (0,)), ((), ())), precision=high)


def self_gram(rows):
    upper = lax.reduce_precision(rows, exponent_bits=8, mantissa_bits=7)
    lower = lax.reduce_precision(rows - upper, exponent_bits=8, mantissa_bits=7)
    missing = jnp.sum(lower * lower, axis=0)
    return cross_gram(rows, rows) + jnp.diag(missing)


def on_device(snapshots, coefficient, start_first, start_merge):
    extended = padded_2(snapshots, (("tx", 0),), 2)
    rows_here = snapshots.shape[0] * snapshots.shape[1]
    order_size = snapshots.shape[2]
    modes_count = start_first.shape[1]
    share_count = modes_count // lax.axis_size("run")
    cells_total = rows_here * lax.axis_size("tx")
    member = lax.axis_index("run")
    is_first = member == 0
    own_start = lax.dynamic_slice_in_dim(start_first, member * order_size, order_size, 0)
    own_start = own_start.astype(jnp.float32)
    merge_start = start_merge.astype(jnp.float32)
    if lax.axis_size("tx") % 2:
        first_basis = orthonormal(own_start)
        merge_basis = orthonormal(merge_start)
    else:
        is_even = lax.axis_index("tx") % 2 == 0
        mine = orthonormal(jnp.where(is_even, own_start, merge_start))
        theirs = partner(mine, "tx", 0)
        first_basis = jnp.where(is_even, mine, theirs)
        merge_basis = jnp.where(is_even, theirs, mine)
    own_flux = fluxes(extended, coefficient).reshape(rows_here, order_size)
    own_gram = tree_sum(self_gram(own_flux), "tx") / cells_total
    own_basis = iterate(own_gram, first_basis)
    own_modes = jnp.dot(own_flux, own_basis, precision=high)
    other_modes = partner(own_modes, "run", 0)
    own_block = self_gram(own_modes)
    half_rows = rows_here // 2
    half_start = member * half_rows
    mixed_half = cross_gram(
        lax.dynamic_slice_in_dim(own_modes, half_start, half_rows, 0),
        lax.dynamic_slice_in_dim(other_modes, half_start, half_rows, 0),
    )
    mixed_half = jnp.where(is_first, mixed_half, mixed_half.T)
    summed = tree_sum(jnp.stack([own_block, mixed_half]), "tx")
    swapped = partner(summed, "run", 0)
    own_block = summed[0] / cells_total
    other_block = swapped[0] / cells_total
    mixed_block = (summed[1] + swapped[1]) / cells_total
    first_block = jnp.where(is_first, own_block, other_block)
    last_block = jnp.where(is_first, other_block, own_block)
    merge_gram = jnp.concatenate(
        [
            jnp.concatenate([first_block, mixed_block], axis=1),
            jnp.concatenate([mixed_block.T, last_block], axis=1),
        ],
        axis=0,
    )
    rotation = iterate(merge_gram, merge_basis)
    rotation_share = lax.dynamic_slice_in_dim(rotation, member * share_count, share_count, 1)
    top_rows = rotation_share[:modes_count]
    bottom_rows = rotation_share[modes_count:]
    own_rotation = jnp.where(is_first, top_rows, bottom_rows)
    other_rotation = jnp.where(is_first, bottom_rows, top_rows)
    result = jnp.dot(own_modes, own_rotation, precision=high) + jnp.dot(
        other_modes, other_rotation, precision=high
    )
    return result.reshape(snapshots.shape[0], snapshots.shape[1], share_count)


def solution(mesh):
    in_specs = (P(("slab", "tx"), None, "run"), P(("slab", "tx"), None), P(), P())
    out_specs = P(("slab", "tx"), None, "run")
    return jax.shard_map(
        on_device, mesh=mesh, in_specs=in_specs, out_specs=out_specs, check_vma=False
    )
```

```python
import jax
import jax.numpy as jnp
from jax import lax
from jax.sharding import PartitionSpec as P
import functools
from jax.experimental import pallas as pl
from jax.experimental.pallas import tpu as pltpu

ITERS = 2


highest = lax.Precision.HIGHEST
high = lax.Precision.HIGH


def halos(block, axis, width):
    count = lax.axis_size(axis)
    forward = [(i, i + 1) for i in range(count - 1)]
    backward = [(target, source) for source, target in forward]
    low = lax.ppermute(lax.slice_in_dim(block, block.shape[0] - width, None, axis=0), axis, forward)
    high = lax.ppermute(lax.slice_in_dim(block, 0, width, axis=0), axis, backward)
    return low, high


def partner(block, axis, stride):
    count = lax.axis_size(axis)
    route = []
    for low in range(count):
        high = low | 1 << stride
        if high != low and high < count:
            route += [(low, high), (high, low)]
    return lax.ppermute(block, axis, route)


def tree_sum(value, axis):
    count = lax.axis_size(axis)
    if count & (count - 1):
        return lax.psum(value, axis)
    step = 1
    while step < count:
        route = [(i, i ^ step) for i in range(count)]
        value = value + lax.ppermute(value, axis, route)
        step *= 2
    return value


def fourth_order(values, axis_dim):
    length_kept = values.shape[axis_dim] - 4

    def shifted(offset):
        return lax.slice_in_dim(values, offset, offset + length_kept, axis=axis_dim)

    return (8.0 * (shifted(3) - shifted(1)) - (shifted(4) - shifted(0))) / 12.0


def flux_kernel(count, low_ref, high_ref, prev_ref, main_ref, next_ref, coef_ref, out_ref):
    i = pl.program_id(0)
    above = jnp.where(i == 0, low_ref[...], prev_ref[-2:])
    below = jnp.where(i == count - 1, high_ref[...], next_ref[:2])
    rows = jnp.concatenate([above, main_ref[...], below], axis=0).astype(jnp.float32)
    squared = 0.5 * jnp.square(rows)
    along_rows = fourth_order(squared, 0)
    mid = squared[2:-2]
    cols = mid.shape[1]
    ids = lax.broadcasted_iota(jnp.int32, mid.shape, 1)

    def shift(offset):
        moved = pltpu.roll(mid, (-offset) % cols, 1)
        inside = (ids + offset >= 0) & (ids + offset < cols)
        return jnp.where(inside, moved, 0.0)

    along_cols = (8.0 * (shift(1) - shift(-1)) - (shift(2) - shift(-2))) / 12.0
    central = rows[2:-2]
    out_ref[...] = central - coef_ref[...][:, :, None] * (along_rows + along_cols)


def fluxes(low, block, high, coefficient):
    nx, ny, ns = block.shape
    bx = 8 if nx % 8 == 0 else nx
    count = nx // bx

    def spec(index):
        return pl.BlockSpec((bx, ny, ns), index)

    return pl.pallas_call(
        functools.partial(flux_kernel, count),
        grid=(count,),
        in_specs=[
            pl.BlockSpec(low.shape, lambda i: (0, 0, 0)),
            pl.BlockSpec(high.shape, lambda i: (0, 0, 0)),
            spec(lambda i: (jnp.maximum(i - 1, 0), 0, 0)),
            spec(lambda i: (i, 0, 0)),
            spec(lambda i: (jnp.minimum(i + 1, count - 1), 0, 0)),
            pl.BlockSpec((bx, ny), lambda i: (i, 0)),
        ],
        out_specs=spec(lambda i: (i, 0, 0)),
        out_shape=jax.ShapeDtypeStruct((nx, ny, ns), jnp.float32),
    )(low, high, block, block, block, coefficient)


def gram_schmidt_kernel(rows_ref, out_ref):
    count, width = rows_ref.shape
    chunks = [rows_ref[i * 8:(i + 1) * 8, :] for i in range(count // 8)]
    for j in range(count):
        block, lane_row = divmod(j, 8)
        vector = chunks[block][lane_row:lane_row + 1, :]
        inverse = 1.0 / jnp.sum(vector * vector, axis=1, keepdims=True)
        for i in range(block, count // 8):
            rows = chunks[i]
            weight = jnp.sum(rows * vector, axis=1, keepdims=True) * inverse
            if i == block:
                ids = lax.broadcasted_iota(jnp.int32, weight.shape, 0)
                weight = jnp.where(ids > lane_row, weight, 0.0)
            chunks[i] = rows - weight * vector
    for i in range(count // 8):
        rows = chunks[i]
        norm = jnp.sqrt(jnp.sum(rows * rows, axis=1, keepdims=True))
        out_ref[i * 8:(i + 1) * 8, :] = rows / norm


def orthonormal(matrix):
    rows = matrix.T
    done = pl.pallas_call(
        gram_schmidt_kernel, out_shape=jax.ShapeDtypeStruct(rows.shape, jnp.float32)
    )(rows)
    return done.T


def iterate(gram_matrix, basis_set):
    for sweep_index in range(ITERS):
        basis_set = orthonormal(jnp.dot(gram_matrix, basis_set, precision=highest))
    return basis_set


def cross_gram(left_rows, right_rows):
    return lax.dot_general(left_rows, right_rows, (((0,), (0,)), ((), ())), precision=high)


def self_gram(rows):
    upper = lax.reduce_precision(rows, exponent_bits=8, mantissa_bits=7)
    lower = lax.reduce_precision(rows - upper, exponent_bits=8, mantissa_bits=7)
    missing = jnp.sum(lower * lower, axis=0)
    return cross_gram(rows, rows) + jnp.diag(missing)


def on_device(snapshots, coefficient, start_first, start_merge):
    halo_low, halo_high = halos(snapshots, "tx", 2)
    rows_here = snapshots.shape[0] * snapshots.shape[1]
    order_size = snapshots.shape[2]
    modes_count = start_first.shape[1]
    share_count = modes_count // lax.axis_size("run")
    cells_total = rows_here * lax.axis_size("tx")
    member = lax.axis_index("run")
    is_first = member == 0
    own_start = lax.dynamic_slice_in_dim(start_first, member * order_size, order_size, 0)
    own_start = own_start.astype(jnp.float32)
    merge_start = start_merge.astype(jnp.float32)
    if lax.axis_size("tx") % 2:
        first_basis = orthonormal(own_start)
        merge_basis = orthonormal(merge_start)
    else:
        is_even = lax.axis_index("tx") % 2 == 0
        mine = orthonormal(jnp.where(is_even, own_start, merge_start))
        theirs = partner(mine, "tx", 0)
        first_basis = jnp.where(is_even, mine, theirs)
        merge_basis = jnp.where(is_even, theirs, mine)
    own_flux = fluxes(halo_low, snapshots, halo_high, coefficient).reshape(rows_here, order_size)
    own_gram = tree_sum(self_gram(own_flux), "tx") / cells_total
    own_basis = iterate(own_gram, first_basis)
    own_modes = jnp.dot(own_flux, own_basis, precision=high)
    other_modes = partner(own_modes, "run", 0)
    own_block = self_gram(own_modes)
    half_rows = rows_here // 2
    half_start = member * half_rows
    mixed_half = cross_gram(
        lax.dynamic_slice_in_dim(own_modes, half_start, half_rows, 0),
        lax.dynamic_slice_in_dim(other_modes, half_start, half_rows, 0),
    )
    mixed_half = jnp.where(is_first, mixed_half, mixed_half.T)
    summed = tree_sum(jnp.stack([own_block, mixed_half]), "tx")
    swapped = partner(summed, "run", 0)
    own_block = summed[0] / cells_total
    other_block = swapped[0] / cells_total
    mixed_block = (summed[1] + swapped[1]) / cells_total
    first_block = jnp.where(is_first, own_block, other_block)
    last_block = jnp.where(is_first, other_block, own_block)
    merge_gram = jnp.concatenate(
        [
            jnp.concatenate([first_block, mixed_block], axis=1),
            jnp.concatenate([mixed_block.T, last_block], axis=1),
        ],
        axis=0,
    )
    rotation = iterate(merge_gram, merge_basis)
    rotation_share = lax.dynamic_slice_in_dim(rotation, member * share_count, share_count, 1)
    top_rows = rotation_share[:modes_count]
    bottom_rows = rotation_share[modes_count:]
    own_rotation = jnp.where(is_first, top_rows, bottom_rows)
    other_rotation = jnp.where(is_first, bottom_rows, top_rows)
    result = jnp.dot(own_modes, own_rotation, precision=high) + jnp.dot(
        other_modes, other_rotation, precision=high
    )
    return result.reshape(snapshots.shape[0], snapshots.shape[1], share_count)


def solution(mesh):
    in_specs = (P(("slab", "tx"), None, "run"), P(("slab", "tx"), None), P(), P())
    out_specs = P(("slab", "tx"), None, "run")
    return jax.shard_map(
        on_device, mesh=mesh, in_specs=in_specs, out_specs=out_specs, check_vma=False
    )
```

```python
import jax
import jax.numpy as jnp
from jax import lax
from jax.sharding import PartitionSpec as P
import functools
from jax.experimental import pallas as pl
from jax.experimental.pallas import tpu as pltpu

ITERS = 2


highest = lax.Precision.HIGHEST
high = lax.Precision.HIGH


def halos(block, axis, width):
    count = lax.axis_size(axis)
    forward = [(i, i + 1) for i in range(count - 1)]
    backward = [(target, source) for source, target in forward]
    low = lax.ppermute(lax.slice_in_dim(block, block.shape[0] - width, None, axis=0), axis, forward)
    high = lax.ppermute(lax.slice_in_dim(block, 0, width, axis=0), axis, backward)
    return low, high


def partner(block, axis, stride):
    count = lax.axis_size(axis)
    route = []
    for low in range(count):
        high = low | 1 << stride
        if high != low and high < count:
            route += [(low, high), (high, low)]
    return lax.ppermute(block, axis, route)


def tree_sum(value, axis):
    count = lax.axis_size(axis)
    if count & (count - 1):
        return lax.psum(value, axis)
    step = 1
    while step * 4 <= count:
        received = [
            lax.ppermute(value, axis, [(i, i ^ (step * k)) for i in range(count)]) for k in (1, 2, 3)
        ]
        value = (value + received[0]) + (received[1] + received[2])
        step *= 4
    if step < count:
        value = value + lax.ppermute(value, axis, [(i, i ^ step) for i in range(count)])
    return value


def fourth_order(values, axis_dim):
    length_kept = values.shape[axis_dim] - 4

    def shifted(offset):
        return lax.slice_in_dim(values, offset, offset + length_kept, axis=axis_dim)

    return (8.0 * (shifted(3) - shifted(1)) - (shifted(4) - shifted(0))) / 12.0


def flux_kernel(count, low_ref, high_ref, prev_ref, main_ref, next_ref, coef_ref, out_ref):
    i = pl.program_id(0)
    above = jnp.where(i == 0, low_ref[...], prev_ref[-2:])
    below = jnp.where(i == count - 1, high_ref[...], next_ref[:2])
    rows = jnp.concatenate([above, main_ref[...], below], axis=0).astype(jnp.float32)
    squared = 0.5 * jnp.square(rows)
    along_rows = fourth_order(squared, 0)
    mid = squared[2:-2]
    cols = mid.shape[1]
    ids = lax.broadcasted_iota(jnp.int32, mid.shape, 1)

    def shift(offset):
        moved = pltpu.roll(mid, (-offset) % cols, 1)
        inside = (ids + offset >= 0) & (ids + offset < cols)
        return jnp.where(inside, moved, 0.0)

    along_cols = (8.0 * (shift(1) - shift(-1)) - (shift(2) - shift(-2))) / 12.0
    central = rows[2:-2]
    out_ref[...] = central - coef_ref[...][:, :, None] * (along_rows + along_cols)


def fluxes(low, block, high, coefficient):
    nx, ny, ns = block.shape
    bx = 8 if nx % 8 == 0 else nx
    count = nx // bx

    def spec(index):
        return pl.BlockSpec((bx, ny, ns), index)

    return pl.pallas_call(
        functools.partial(flux_kernel, count),
        grid=(count,),
        in_specs=[
            pl.BlockSpec(low.shape, lambda i: (0, 0, 0)),
            pl.BlockSpec(high.shape, lambda i: (0, 0, 0)),
            spec(lambda i: (jnp.maximum(i - 1, 0), 0, 0)),
            spec(lambda i: (i, 0, 0)),
            spec(lambda i: (jnp.minimum(i + 1, count - 1), 0, 0)),
            pl.BlockSpec((bx, ny), lambda i: (i, 0)),
        ],
        out_specs=spec(lambda i: (i, 0, 0)),
        out_shape=jax.ShapeDtypeStruct((nx, ny, ns), jnp.float32),
    )(low, high, block, block, block, coefficient)


def gram_schmidt_kernel(rows_ref, out_ref):
    count, width = rows_ref.shape
    chunks = [rows_ref[i * 8:(i + 1) * 8, :] for i in range(count // 8)]
    for j in range(count):
        block, lane_row = divmod(j, 8)
        vector = chunks[block][lane_row:lane_row + 1, :]
        inverse = 1.0 / jnp.sum(vector * vector, axis=1, keepdims=True)
        for i in range(block, count // 8):
            rows = chunks[i]
            weight = jnp.sum(rows * vector, axis=1, keepdims=True) * inverse
            if i == block:
                ids = lax.broadcasted_iota(jnp.int32, weight.shape, 0)
                weight = jnp.where(ids > lane_row, weight, 0.0)
            chunks[i] = rows - weight * vector
    for i in range(count // 8):
        rows = chunks[i]
        norm = jnp.sqrt(jnp.sum(rows * rows, axis=1, keepdims=True))
        out_ref[i * 8:(i + 1) * 8, :] = rows / norm


def orthonormal(matrix):
    rows = matrix.T
    done = pl.pallas_call(
        gram_schmidt_kernel, out_shape=jax.ShapeDtypeStruct(rows.shape, jnp.float32)
    )(rows)
    return done.T


def iterate(gram_matrix, basis_set):
    for sweep_index in range(ITERS):
        basis_set = orthonormal(jnp.dot(gram_matrix, basis_set, precision=highest))
    return basis_set


def cross_gram(left_rows, right_rows):
    return lax.dot_general(left_rows, right_rows, (((0,), (0,)), ((), ())), precision=high)


def self_gram(rows):
    upper = lax.reduce_precision(rows, exponent_bits=8, mantissa_bits=7)
    lower = lax.reduce_precision(rows - upper, exponent_bits=8, mantissa_bits=7)
    missing = jnp.sum(lower * lower, axis=0)
    return cross_gram(rows, rows) + jnp.diag(missing)


def on_device(snapshots, coefficient, start_first, start_merge):
    halo_low, halo_high = halos(snapshots, "tx", 2)
    rows_here = snapshots.shape[0] * snapshots.shape[1]
    order_size = snapshots.shape[2]
    modes_count = start_first.shape[1]
    share_count = modes_count // lax.axis_size("run")
    cells_total = rows_here * lax.axis_size("tx")
    member = lax.axis_index("run")
    is_first = member == 0
    own_start = lax.dynamic_slice_in_dim(start_first, member * order_size, order_size, 0)
    own_start = own_start.astype(jnp.float32)
    merge_start = start_merge.astype(jnp.float32)
    if lax.axis_size("tx") % 2:
        first_basis = orthonormal(own_start)
        merge_basis = orthonormal(merge_start)
    else:
        is_even = lax.axis_index("tx") % 2 == 0
        mine = orthonormal(jnp.where(is_even, own_start, merge_start))
        theirs = partner(mine, "tx", 0)
        first_basis = jnp.where(is_even, mine, theirs)
        merge_basis = jnp.where(is_even, theirs, mine)
    own_flux = fluxes(halo_low, snapshots, halo_high, coefficient).reshape(rows_here, order_size)
    own_gram = tree_sum(self_gram(own_flux), "tx") / cells_total
    own_basis = iterate(own_gram, first_basis)
    own_modes = jnp.dot(own_flux, own_basis, precision=high)
    other_modes = partner(own_modes, "run", 0)
    own_block = self_gram(own_modes)
    half_rows = rows_here // 2
    half_start = member * half_rows
    mixed_half = cross_gram(
        lax.dynamic_slice_in_dim(own_modes, half_start, half_rows, 0),
        lax.dynamic_slice_in_dim(other_modes, half_start, half_rows, 0),
    )
    mixed_half = jnp.where(is_first, mixed_half, mixed_half.T)
    summed = tree_sum(jnp.stack([own_block, mixed_half]), "tx")
    swapped = partner(summed, "run", 0)
    own_block = summed[0] / cells_total
    other_block = swapped[0] / cells_total
    mixed_block = (summed[1] + swapped[1]) / cells_total
    first_block = jnp.where(is_first, own_block, other_block)
    last_block = jnp.where(is_first, other_block, own_block)
    merge_gram = jnp.concatenate(
        [
            jnp.concatenate([first_block, mixed_block], axis=1),
            jnp.concatenate([mixed_block.T, last_block], axis=1),
        ],
        axis=0,
    )
    rotation = iterate(merge_gram, merge_basis)
    rotation_share = lax.dynamic_slice_in_dim(rotation, member * share_count, share_count, 1)
    top_rows = rotation_share[:modes_count]
    bottom_rows = rotation_share[modes_count:]
    own_rotation = jnp.where(is_first, top_rows, bottom_rows)
    other_rotation = jnp.where(is_first, bottom_rows, top_rows)
    result = jnp.dot(own_modes, own_rotation, precision=high) + jnp.dot(
        other_modes, other_rotation, precision=high
    )
    return result.reshape(snapshots.shape[0], snapshots.shape[1], share_count)


def solution(mesh):
    in_specs = (P(("slab", "tx"), None, "run"), P(("slab", "tx"), None), P(), P())
    out_specs = P(("slab", "tx"), None, "run")
    return jax.shard_map(
        on_device, mesh=mesh, in_specs=in_specs, out_specs=out_specs, check_vma=False
    )
```

```python
import jax
import jax.numpy as jnp
from jax import lax
from jax.sharding import PartitionSpec as P
import functools
from jax.experimental import pallas as pl
from jax.experimental.pallas import tpu as pltpu

ITERS = 2


highest = lax.Precision.HIGHEST
high = lax.Precision.HIGH


def halos(block, axis, width):
    count = lax.axis_size(axis)
    forward = [(i, i + 1) for i in range(count - 1)]
    backward = [(target, source) for source, target in forward]
    low = lax.ppermute(lax.slice_in_dim(block, block.shape[0] - width, None, axis=0), axis, forward)
    high = lax.ppermute(lax.slice_in_dim(block, 0, width, axis=0), axis, backward)
    return low, high


def partner(block, axis, stride):
    count = lax.axis_size(axis)
    route = []
    for low in range(count):
        high = low | 1 << stride
        if high != low and high < count:
            route += [(low, high), (high, low)]
    return lax.ppermute(block, axis, route)


def tree_sum(value, axis):
    count = lax.axis_size(axis)
    if count & (count - 1):
        return lax.psum(value, axis)
    step = 1
    while step < count:
        route = [(i, i ^ step) for i in range(count)]
        value = value + lax.ppermute(value, axis, route)
        step *= 2
    return value


def fourth_order(values, axis_dim):
    length_kept = values.shape[axis_dim] - 4

    def shifted(offset):
        return lax.slice_in_dim(values, offset, offset + length_kept, axis=axis_dim)

    return (8.0 * (shifted(3) - shifted(1)) - (shifted(4) - shifted(0))) / 12.0


def flux_kernel(count, low_ref, high_ref, prev_ref, main_ref, next_ref, coef_ref, out_ref):
    i = pl.program_id(0)
    above = jnp.where(i == 0, low_ref[...], prev_ref[-2:])
    below = jnp.where(i == count - 1, high_ref[...], next_ref[:2])
    rows = jnp.concatenate([above, main_ref[...], below], axis=0).astype(jnp.float32)
    squared = 0.5 * jnp.square(rows)
    along_rows = fourth_order(squared, 0)
    mid = squared[2:-2]
    cols = mid.shape[1]
    ids = lax.broadcasted_iota(jnp.int32, mid.shape, 1)

    def shift(offset):
        moved = pltpu.roll(mid, (-offset) % cols, 1)
        inside = (ids + offset >= 0) & (ids + offset < cols)
        return jnp.where(inside, moved, 0.0)

    along_cols = (8.0 * (shift(1) - shift(-1)) - (shift(2) - shift(-2))) / 12.0
    central = rows[2:-2]
    out_ref[...] = central - coef_ref[...][:, :, None] * (along_rows + along_cols)


def fluxes(low, block, high, coefficient):
    nx, ny, ns = block.shape
    bx = 8 if nx % 8 == 0 else nx
    count = nx // bx

    def spec(index):
        return pl.BlockSpec((bx, ny, ns), index)

    return pl.pallas_call(
        functools.partial(flux_kernel, count),
        grid=(count,),
        in_specs=[
            pl.BlockSpec(low.shape, lambda i: (0, 0, 0)),
            pl.BlockSpec(high.shape, lambda i: (0, 0, 0)),
            spec(lambda i: (jnp.maximum(i - 1, 0), 0, 0)),
            spec(lambda i: (i, 0, 0)),
            spec(lambda i: (jnp.minimum(i + 1, count - 1), 0, 0)),
            pl.BlockSpec((bx, ny), lambda i: (i, 0)),
        ],
        out_specs=spec(lambda i: (i, 0, 0)),
        out_shape=jax.ShapeDtypeStruct((nx, ny, ns), jnp.float32),
    )(low, high, block, block, block, coefficient)


def gram_schmidt_kernel(rows_ref, out_ref):
    count, width = rows_ref.shape
    chunks = [rows_ref[i * 8:(i + 1) * 8, :] for i in range(count // 8)]
    for j in range(count):
        block, lane_row = divmod(j, 8)
        vector = chunks[block][lane_row:lane_row + 1, :]
        inverse = 1.0 / jnp.sum(vector * vector, axis=1, keepdims=True)
        for i in range(block, count // 8):
            rows = chunks[i]
            weight = jnp.sum(rows * vector, axis=1, keepdims=True) * inverse
            if i == block:
                ids = lax.broadcasted_iota(jnp.int32, weight.shape, 0)
                weight = jnp.where(ids > lane_row, weight, 0.0)
            chunks[i] = rows - weight * vector
    for i in range(count // 8):
        rows = chunks[i]
        norm = jnp.sqrt(jnp.sum(rows * rows, axis=1, keepdims=True))
        out_ref[i * 8:(i + 1) * 8, :] = rows / norm


def orthonormal(matrix):
    rows = matrix.T
    done = pl.pallas_call(
        gram_schmidt_kernel, out_shape=jax.ShapeDtypeStruct(rows.shape, jnp.float32)
    )(rows)
    return done.T


def iterate(gram_matrix, basis_set):
    def sweep(sweep_index, basis_set):
        return orthonormal(jnp.dot(gram_matrix, basis_set, precision=highest))

    return lax.fori_loop(0, ITERS, sweep, basis_set)


def cross_gram(left_rows, right_rows):
    return lax.dot_general(left_rows, right_rows, (((0,), (0,)), ((), ())), precision=high)


def self_gram(rows):
    upper = lax.reduce_precision(rows, exponent_bits=8, mantissa_bits=7)
    lower = lax.reduce_precision(rows - upper, exponent_bits=8, mantissa_bits=7)
    missing = jnp.sum(lower * lower, axis=0)
    return cross_gram(rows, rows) + jnp.diag(missing)


def on_device(snapshots, coefficient, start_first, start_merge):
    halo_low, halo_high = halos(snapshots, "tx", 2)
    rows_here = snapshots.shape[0] * snapshots.shape[1]
    order_size = snapshots.shape[2]
    modes_count = start_first.shape[1]
    share_count = modes_count // lax.axis_size("run")
    cells_total = rows_here * lax.axis_size("tx")
    member = lax.axis_index("run")
    is_first = member == 0
    own_start = lax.dynamic_slice_in_dim(start_first, member * order_size, order_size, 0)
    own_start = own_start.astype(jnp.float32)
    merge_start = start_merge.astype(jnp.float32)
    if lax.axis_size("tx") % 2:
        first_basis = orthonormal(own_start)
        merge_basis = orthonormal(merge_start)
    else:
        is_even = lax.axis_index("tx") % 2 == 0
        mine = orthonormal(jnp.where(is_even, own_start, merge_start))
        theirs = partner(mine, "tx", 0)
        first_basis = jnp.where(is_even, mine, theirs)
        merge_basis = jnp.where(is_even, theirs, mine)
    own_flux = fluxes(halo_low, snapshots, halo_high, coefficient).reshape(rows_here, order_size)
    own_gram = tree_sum(self_gram(own_flux), "tx") / cells_total
    own_basis = iterate(own_gram, first_basis)
    own_modes = jnp.dot(own_flux, own_basis, precision=high)
    other_modes = partner(own_modes, "run", 0)
    own_block = self_gram(own_modes)
    half_rows = rows_here // 2
    half_start = member * half_rows
    mixed_half = cross_gram(
        lax.dynamic_slice_in_dim(own_modes, half_start, half_rows, 0),
        lax.dynamic_slice_in_dim(other_modes, half_start, half_rows, 0),
    )
    mixed_half = jnp.where(is_first, mixed_half, mixed_half.T)
    summed = tree_sum(jnp.stack([own_block, mixed_half]), "tx")
    swapped = partner(summed, "run", 0)
    own_block = summed[0] / cells_total
    other_block = swapped[0] / cells_total
    mixed_block = (summed[1] + swapped[1]) / cells_total
    first_block = jnp.where(is_first, own_block, other_block)
    last_block = jnp.where(is_first, other_block, own_block)
    merge_gram = jnp.concatenate(
        [
            jnp.concatenate([first_block, mixed_block], axis=1),
            jnp.concatenate([mixed_block.T, last_block], axis=1),
        ],
        axis=0,
    )
    rotation = iterate(merge_gram, merge_basis)
    rotation_share = lax.dynamic_slice_in_dim(rotation, member * share_count, share_count, 1)
    top_rows = rotation_share[:modes_count]
    bottom_rows = rotation_share[modes_count:]
    own_rotation = jnp.where(is_first, top_rows, bottom_rows)
    other_rotation = jnp.where(is_first, bottom_rows, top_rows)
    result = jnp.dot(own_modes, own_rotation, precision=high) + jnp.dot(
        other_modes, other_rotation, precision=high
    )
    return result.reshape(snapshots.shape[0], snapshots.shape[1], share_count)


def solution(mesh):
    in_specs = (P(("slab", "tx"), None, "run"), P(("slab", "tx"), None), P(), P())
    out_specs = P(("slab", "tx"), None, "run")
    return jax.shard_map(
        on_device, mesh=mesh, in_specs=in_specs, out_specs=out_specs, check_vma=False
    )
```

```python
import jax
import jax.numpy as jnp
from jax import lax
from jax.sharding import PartitionSpec as P
import functools
from jax.experimental import pallas as pl
from jax.experimental.pallas import tpu as pltpu

ITERS = 2


highest = lax.Precision.HIGHEST
high = lax.Precision.HIGH


def halos(block, axis, width):
    count = lax.axis_size(axis)
    forward = [(i, i + 1) for i in range(count - 1)]
    backward = [(target, source) for source, target in forward]
    low = lax.ppermute(lax.slice_in_dim(block, block.shape[0] - width, None, axis=0), axis, forward)
    high = lax.ppermute(lax.slice_in_dim(block, 0, width, axis=0), axis, backward)
    return low, high


def partner(block, axis, stride):
    count = lax.axis_size(axis)
    route = []
    for low in range(count):
        high = low | 1 << stride
        if high != low and high < count:
            route += [(low, high), (high, low)]
    return lax.ppermute(block, axis, route)


def tree_sum(value, axis):
    count = lax.axis_size(axis)
    if count & (count - 1):
        return lax.psum(value, axis)
    step = 1
    while step < count:
        route = [(i, i ^ step) for i in range(count)]
        value = value + lax.ppermute(value, axis, route)
        step *= 2
    return value


def fourth_order(values, axis_dim):
    length_kept = values.shape[axis_dim] - 4

    def shifted(offset):
        return lax.slice_in_dim(values, offset, offset + length_kept, axis=axis_dim)

    return (8.0 * (shifted(3) - shifted(1)) - (shifted(4) - shifted(0))) / 12.0


def flux_kernel(count, low_ref, high_ref, prev_ref, main_ref, next_ref, coef_ref, out_ref):
    i = pl.program_id(0)
    above = jnp.where(i == 0, low_ref[...], prev_ref[-2:])
    below = jnp.where(i == count - 1, high_ref[...], next_ref[:2])
    rows = jnp.concatenate([above, main_ref[...], below], axis=0).astype(jnp.float32)
    squared = 0.5 * jnp.square(rows)
    along_rows = fourth_order(squared, 0)
    mid = squared[2:-2]
    cols = mid.shape[1]
    ids = lax.broadcasted_iota(jnp.int32, mid.shape, 1)

    def shift(offset):
        moved = pltpu.roll(mid, (-offset) % cols, 1)
        inside = (ids + offset >= 0) & (ids + offset < cols)
        return jnp.where(inside, moved, 0.0)

    along_cols = (8.0 * (shift(1) - shift(-1)) - (shift(2) - shift(-2))) / 12.0
    central = rows[2:-2]
    out_ref[...] = central - coef_ref[...][:, :, None] * (along_rows + along_cols)


def fluxes(low, block, high, coefficient):
    nx, ny, ns = block.shape
    bx = 8 if nx % 8 == 0 else nx
    count = nx // bx

    def spec(index):
        return pl.BlockSpec((bx, ny, ns), index)

    return pl.pallas_call(
        functools.partial(flux_kernel, count),
        grid=(count,),
        in_specs=[
            pl.BlockSpec(low.shape, lambda i: (0, 0, 0)),
            pl.BlockSpec(high.shape, lambda i: (0, 0, 0)),
            spec(lambda i: (jnp.maximum(i - 1, 0), 0, 0)),
            spec(lambda i: (i, 0, 0)),
            spec(lambda i: (jnp.minimum(i + 1, count - 1), 0, 0)),
            pl.BlockSpec((bx, ny), lambda i: (i, 0)),
        ],
        out_specs=spec(lambda i: (i, 0, 0)),
        out_shape=jax.ShapeDtypeStruct((nx, ny, ns), jnp.float32),
    )(low, high, block, block, block, coefficient)


def gram_schmidt_kernel(rows_ref, out_ref, work):
    count, width = rows_ref.shape
    blocks = count // 8
    group = 4 if blocks % 4 == 0 else 1
    work[...] = rows_ref[...]
    for first in range(0, blocks, group):

        def sweep(block, carry, first=first):
            base = pl.multiple_of(block * 8, 8)
            for lane_row in range(8):
                j = base + lane_row
                vector = work[pl.ds(j, 1), :]
                inverse = 1.0 / jnp.sum(vector * vector, axis=1, keepdims=True)
                for i in range(first, blocks):
                    rows = work[i * 8:(i + 1) * 8, :]
                    weight = jnp.sum(rows * vector, axis=1, keepdims=True) * inverse
                    ids = lax.broadcasted_iota(jnp.int32, weight.shape, 0) + i * 8
                    weight = jnp.where(ids > j, weight, 0.0)
                    work[i * 8:(i + 1) * 8, :] = rows - weight * vector
            return carry

        lax.fori_loop(first, first + group, sweep, 0)
    for i in range(blocks):
        rows = work[i * 8:(i + 1) * 8, :]
        norm = jnp.sqrt(jnp.sum(rows * rows, axis=1, keepdims=True))
        out_ref[i * 8:(i + 1) * 8, :] = rows / norm


def orthonormal(matrix):
    rows = matrix.T
    done = pl.pallas_call(
        gram_schmidt_kernel,
        out_shape=jax.ShapeDtypeStruct(rows.shape, jnp.float32),
        scratch_shapes=[pltpu.VMEM(rows.shape, jnp.float32)],
    )(rows)
    return done.T


def iterate(gram_matrix, basis_set):
    def sweep(sweep_index, basis_set):
        return orthonormal(jnp.dot(gram_matrix, basis_set, precision=highest))

    return lax.fori_loop(0, ITERS, sweep, basis_set)


def cross_gram(left_rows, right_rows):
    return lax.dot_general(left_rows, right_rows, (((0,), (0,)), ((), ())), precision=high)


def self_gram(rows):
    upper = lax.reduce_precision(rows, exponent_bits=8, mantissa_bits=7)
    lower = lax.reduce_precision(rows - upper, exponent_bits=8, mantissa_bits=7)
    missing = jnp.sum(lower * lower, axis=0)
    return cross_gram(rows, rows) + jnp.diag(missing)


def on_device(snapshots, coefficient, start_first, start_merge):
    halo_low, halo_high = halos(snapshots, "tx", 2)
    rows_here = snapshots.shape[0] * snapshots.shape[1]
    order_size = snapshots.shape[2]
    modes_count = start_first.shape[1]
    share_count = modes_count // lax.axis_size("run")
    cells_total = rows_here * lax.axis_size("tx")
    member = lax.axis_index("run")
    is_first = member == 0
    own_start = lax.dynamic_slice_in_dim(start_first, member * order_size, order_size, 0)
    own_start = own_start.astype(jnp.float32)
    merge_start = start_merge.astype(jnp.float32)
    if lax.axis_size("tx") % 2:
        first_basis = orthonormal(own_start)
        merge_basis = orthonormal(merge_start)
    else:
        is_even = lax.axis_index("tx") % 2 == 0
        mine = orthonormal(jnp.where(is_even, own_start, merge_start))
        theirs = partner(mine, "tx", 0)
        first_basis = jnp.where(is_even, mine, theirs)
        merge_basis = jnp.where(is_even, theirs, mine)
    own_flux = fluxes(halo_low, snapshots, halo_high, coefficient).reshape(rows_here, order_size)
    own_gram = tree_sum(self_gram(own_flux), "tx") / cells_total
    own_basis = iterate(own_gram, first_basis)
    own_modes = jnp.dot(own_flux, own_basis, precision=high)
    other_modes = partner(own_modes, "run", 0)
    own_block = self_gram(own_modes)
    half_rows = rows_here // 2
    half_start = member * half_rows
    mixed_half = cross_gram(
        lax.dynamic_slice_in_dim(own_modes, half_start, half_rows, 0),
        lax.dynamic_slice_in_dim(other_modes, half_start, half_rows, 0),
    )
    mixed_half = jnp.where(is_first, mixed_half, mixed_half.T)
    summed = tree_sum(jnp.stack([own_block, mixed_half]), "tx")
    swapped = partner(summed, "run", 0)
    own_block = summed[0] / cells_total
    other_block = swapped[0] / cells_total
    mixed_block = (summed[1] + swapped[1]) / cells_total
    first_block = jnp.where(is_first, own_block, other_block)
    last_block = jnp.where(is_first, other_block, own_block)
    merge_gram = jnp.concatenate(
        [
            jnp.concatenate([first_block, mixed_block], axis=1),
            jnp.concatenate([mixed_block.T, last_block], axis=1),
        ],
        axis=0,
    )
    rotation = iterate(merge_gram, merge_basis)
    rotation_share = lax.dynamic_slice_in_dim(rotation, member * share_count, share_count, 1)
    top_rows = rotation_share[:modes_count]
    bottom_rows = rotation_share[modes_count:]
    own_rotation = jnp.where(is_first, top_rows, bottom_rows)
    other_rotation = jnp.where(is_first, bottom_rows, top_rows)
    result = jnp.dot(own_modes, own_rotation, precision=high) + jnp.dot(
        other_modes, other_rotation, precision=high
    )
    return result.reshape(snapshots.shape[0], snapshots.shape[1], share_count)


def solution(mesh):
    in_specs = (P(("slab", "tx"), None, "run"), P(("slab", "tx"), None), P(), P())
    out_specs = P(("slab", "tx"), None, "run")
    return jax.shard_map(
        on_device, mesh=mesh, in_specs=in_specs, out_specs=out_specs, check_vma=False
    )
```

```python
import jax
import jax.numpy as jnp
from jax import lax
from jax.sharding import PartitionSpec as P
import functools
from jax.experimental import pallas as pl
from jax.experimental.pallas import tpu as pltpu

ITERS = 2


highest = lax.Precision.HIGHEST
high = lax.Precision.HIGH


def halos(block, axis, width):
    count = lax.axis_size(axis)
    forward = [(i, i + 1) for i in range(count - 1)]
    backward = [(target, source) for source, target in forward]
    low = lax.ppermute(lax.slice_in_dim(block, block.shape[0] - width, None, axis=0), axis, forward)
    high = lax.ppermute(lax.slice_in_dim(block, 0, width, axis=0), axis, backward)
    return low, high


def partner(block, axis, stride):
    count = lax.axis_size(axis)
    route = []
    for low in range(count):
        high = low | 1 << stride
        if high != low and high < count:
            route += [(low, high), (high, low)]
    return lax.ppermute(block, axis, route)


def tree_sum(value, axis):
    count = lax.axis_size(axis)
    if count & (count - 1):
        return lax.psum(value, axis)
    step = 1
    while step < count:
        route = [(i, i ^ step) for i in range(count)]
        value = value + lax.ppermute(value, axis, route)
        step *= 2
    return value


def fourth_order(values, axis_dim):
    length_kept = values.shape[axis_dim] - 4

    def shifted(offset):
        return lax.slice_in_dim(values, offset, offset + length_kept, axis=axis_dim)

    return (8.0 * (shifted(3) - shifted(1)) - (shifted(4) - shifted(0))) / 12.0


def flux_kernel(count, low_ref, high_ref, prev_ref, main_ref, next_ref, coef_ref, out_ref):
    i = pl.program_id(0)
    above = jnp.where(i == 0, low_ref[...], prev_ref[-2:])
    below = jnp.where(i == count - 1, high_ref[...], next_ref[:2])
    rows = jnp.concatenate([above, main_ref[...], below], axis=0).astype(jnp.float32)
    squared = 0.5 * jnp.square(rows)
    along_rows = fourth_order(squared, 0)
    mid = squared[2:-2]
    cols = mid.shape[1]
    ids = lax.broadcasted_iota(jnp.int32, mid.shape, 1)

    def shift(offset):
        moved = pltpu.roll(mid, (-offset) % cols, 1)
        inside = (ids + offset >= 0) & (ids + offset < cols)
        return jnp.where(inside, moved, 0.0)

    along_cols = (8.0 * (shift(1) - shift(-1)) - (shift(2) - shift(-2))) / 12.0
    central = rows[2:-2]
    out_ref[...] = central - coef_ref[...][:, :, None] * (along_rows + along_cols)


def fluxes(low, block, high, coefficient):
    nx, ny, ns = block.shape
    bx = 8 if nx % 8 == 0 else nx
    count = nx // bx

    def spec(index):
        return pl.BlockSpec((bx, ny, ns), index)

    return pl.pallas_call(
        functools.partial(flux_kernel, count),
        grid=(count,),
        in_specs=[
            pl.BlockSpec(low.shape, lambda i: (0, 0, 0)),
            pl.BlockSpec(high.shape, lambda i: (0, 0, 0)),
            spec(lambda i: (jnp.maximum(i - 1, 0), 0, 0)),
            spec(lambda i: (i, 0, 0)),
            spec(lambda i: (jnp.minimum(i + 1, count - 1), 0, 0)),
            pl.BlockSpec((bx, ny), lambda i: (i, 0)),
        ],
        out_specs=spec(lambda i: (i, 0, 0)),
        out_shape=jax.ShapeDtypeStruct((nx, ny, ns), jnp.float32),
    )(low, high, block, block, block, coefficient)


def gram_schmidt_kernel(rows_ref, out_ref, work):
    count, width = rows_ref.shape
    blocks = count // 8
    group = 4 if blocks % 4 == 0 else 1
    work[...] = rows_ref[...]
    for first in range(0, blocks, group):

        def sweep(block, carry, first=first):
            base = pl.multiple_of(block * 8, 8)
            for lane_row in range(8):
                j = base + lane_row
                vector = work[pl.ds(j, 1), :]
                inverse = 1.0 / jnp.sum(vector * vector, axis=1, keepdims=True)
                for i in range(first, blocks):
                    rows = work[i * 8:(i + 1) * 8, :]
                    weight = jnp.sum(rows * vector, axis=1, keepdims=True) * inverse
                    ids = lax.broadcasted_iota(jnp.int32, weight.shape, 0) + i * 8
                    weight = jnp.where(ids > j, weight, 0.0)
                    work[i * 8:(i + 1) * 8, :] = rows - weight * vector
            return carry

        lax.fori_loop(first, first + group, sweep, 0)
    for i in range(blocks):
        rows = work[i * 8:(i + 1) * 8, :]
        norm = jnp.sqrt(jnp.sum(rows * rows, axis=1, keepdims=True))
        out_ref[i * 8:(i + 1) * 8, :] = rows / norm


def orthonormal(matrix):
    rows = matrix.T
    done = pl.pallas_call(
        gram_schmidt_kernel,
        out_shape=jax.ShapeDtypeStruct(rows.shape, jnp.float32),
        scratch_shapes=[pltpu.VMEM(rows.shape, jnp.float32)],
    )(rows)
    return done.T


def iterate(gram_matrix, basis_set):
    def sweep(sweep_index, basis_set):
        return orthonormal(jnp.dot(gram_matrix, basis_set, precision=highest))

    return lax.fori_loop(0, ITERS, sweep, basis_set)


def cross_gram(left_rows, right_rows):
    return lax.dot_general(left_rows, right_rows, (((0,), (0,)), ((), ())), precision=high)


def self_gram(rows):
    upper = lax.reduce_precision(rows, exponent_bits=8, mantissa_bits=7)
    lower = lax.reduce_precision(rows - upper, exponent_bits=8, mantissa_bits=7)
    missing = jnp.sum(lower * lower, axis=0)
    return cross_gram(rows, rows) + jnp.diag(missing)


def on_device(snapshots, coefficient, start_first, start_merge):
    halo_low, halo_high = halos(snapshots, "tx", 2)
    rows_here = snapshots.shape[0] * snapshots.shape[1]
    order_size = snapshots.shape[2]
    modes_count = start_first.shape[1]
    share_count = modes_count // lax.axis_size("run")
    cells_total = rows_here * lax.axis_size("tx")
    member = lax.axis_index("run")
    is_first = member == 0
    own_start = lax.dynamic_slice_in_dim(start_first, member * order_size, order_size, 0)
    own_start = own_start.astype(jnp.float32)
    merge_start = start_merge.astype(jnp.float32)
    if lax.axis_size("tx") % 2:
        first_basis = orthonormal(own_start)
        merge_basis = orthonormal(merge_start)
    else:
        is_even = lax.axis_index("tx") % 2 == 0
        mine = orthonormal(jnp.where(is_even, own_start, merge_start))
        theirs = partner(mine, "tx", 0)
        first_basis = jnp.where(is_even, mine, theirs)
        merge_basis = jnp.where(is_even, theirs, mine)
    own_flux = fluxes(halo_low, snapshots, halo_high, coefficient).reshape(rows_here, order_size)
    half_rows = rows_here // 2
    half_start = member * half_rows
    sent_rows = lax.dynamic_slice_in_dim(own_flux, (1 - member) * half_rows, half_rows, 0)
    other_rows = partner(sent_rows, "run", 0)
    mixed_half = cross_gram(
        lax.dynamic_slice_in_dim(own_flux, half_start, half_rows, 0), other_rows
    )
    mixed_half = jnp.where(is_first, mixed_half, mixed_half.T)
    summed = tree_sum(jnp.stack([self_gram(own_flux), mixed_half]), "tx")
    own_gram = summed[0] / cells_total
    mixed_gram = summed[1] + partner(summed[1], "run", 0)
    own_basis = iterate(own_gram, first_basis)
    own_modes = jnp.dot(own_flux, own_basis, precision=high)
    other_modes = partner(own_modes, "run", 0)
    own_block = jnp.dot(own_basis.T, jnp.dot(own_gram, own_basis, precision=highest), precision=highest)
    other_block, other_basis = partner((own_block, own_basis), "run", 0)
    first_basis_set = jnp.where(is_first, own_basis, other_basis)
    last_basis_set = jnp.where(is_first, other_basis, own_basis)
    mixed_block = jnp.dot(
        first_basis_set.T,
        jnp.dot(mixed_gram / cells_total, last_basis_set, precision=highest),
        precision=highest,
    )
    first_block = jnp.where(is_first, own_block, other_block)
    last_block = jnp.where(is_first, other_block, own_block)
    merge_gram = jnp.concatenate(
        [
            jnp.concatenate([first_block, mixed_block], axis=1),
            jnp.concatenate([mixed_block.T, last_block], axis=1),
        ],
        axis=0,
    )
    rotation = iterate(merge_gram, merge_basis)
    rotation_share = lax.dynamic_slice_in_dim(rotation, member * share_count, share_count, 1)
    top_rows = rotation_share[:modes_count]
    bottom_rows = rotation_share[modes_count:]
    own_rotation = jnp.where(is_first, top_rows, bottom_rows)
    other_rotation = jnp.where(is_first, bottom_rows, top_rows)
    result = jnp.dot(own_modes, own_rotation, precision=high) + jnp.dot(
        other_modes, other_rotation, precision=high
    )
    return result.reshape(snapshots.shape[0], snapshots.shape[1], share_count)


def solution(mesh):
    in_specs = (P(("slab", "tx"), None, "run"), P(("slab", "tx"), None), P(), P())
    out_specs = P(("slab", "tx"), None, "run")
    return jax.shard_map(
        on_device, mesh=mesh, in_specs=in_specs, out_specs=out_specs, check_vma=False
    )
```

```python
import jax
import jax.numpy as jnp
from jax import lax
from jax.sharding import PartitionSpec as P
import functools
from jax.experimental import pallas as pl
from jax.experimental.pallas import tpu as pltpu

ITERS = 2


highest = lax.Precision.HIGHEST
high = lax.Precision.HIGH


def halos(block, axis, width):
    count = lax.axis_size(axis)
    forward = [(i, i + 1) for i in range(count - 1)]
    backward = [(target, source) for source, target in forward]
    low = lax.ppermute(lax.slice_in_dim(block, block.shape[0] - width, None, axis=0), axis, forward)
    high = lax.ppermute(lax.slice_in_dim(block, 0, width, axis=0), axis, backward)
    return low, high


def partner(block, axis, stride):
    count = lax.axis_size(axis)
    route = []
    for low in range(count):
        high = low | 1 << stride
        if high != low and high < count:
            route += [(low, high), (high, low)]
    return lax.ppermute(block, axis, route)


def tree_sum(value, axis):
    count = lax.axis_size(axis)
    if count & (count - 1):
        return lax.psum(value, axis)
    step = 1
    while step < count:
        route = [(i, i ^ step) for i in range(count)]
        value = value + lax.ppermute(value, axis, route)
        step *= 2
    return value


def butterfly_steps(axis):
    count = lax.axis_size(axis)
    assert count & (count - 1) == 0
    routes = []
    step = 1
    while step < count:
        routes.append([(i, i ^ step) for i in range(count)])
        step *= 2
    return routes


def fourth_order(values, axis_dim):
    length_kept = values.shape[axis_dim] - 4

    def shifted(offset):
        return lax.slice_in_dim(values, offset, offset + length_kept, axis=axis_dim)

    return (8.0 * (shifted(3) - shifted(1)) - (shifted(4) - shifted(0))) / 12.0


def flux_kernel(count, low_ref, high_ref, prev_ref, main_ref, next_ref, coef_ref, out_ref):
    i = pl.program_id(0)
    above = jnp.where(i == 0, low_ref[...], prev_ref[-2:])
    below = jnp.where(i == count - 1, high_ref[...], next_ref[:2])
    rows = jnp.concatenate([above, main_ref[...], below], axis=0).astype(jnp.float32)
    squared = 0.5 * jnp.square(rows)
    along_rows = fourth_order(squared, 0)
    mid = squared[2:-2]
    cols = mid.shape[1]
    ids = lax.broadcasted_iota(jnp.int32, mid.shape, 1)

    def shift(offset):
        moved = pltpu.roll(mid, (-offset) % cols, 1)
        inside = (ids + offset >= 0) & (ids + offset < cols)
        return jnp.where(inside, moved, 0.0)

    along_cols = (8.0 * (shift(1) - shift(-1)) - (shift(2) - shift(-2))) / 12.0
    central = rows[2:-2]
    out_ref[...] = central - coef_ref[...][:, :, None] * (along_rows + along_cols)


def fluxes(low, block, high, coefficient):
    nx, ny, ns = block.shape
    bx = 8 if nx % 8 == 0 else nx
    count = nx // bx

    def spec(index):
        return pl.BlockSpec((bx, ny, ns), index)

    return pl.pallas_call(
        functools.partial(flux_kernel, count),
        grid=(count,),
        in_specs=[
            pl.BlockSpec(low.shape, lambda i: (0, 0, 0)),
            pl.BlockSpec(high.shape, lambda i: (0, 0, 0)),
            spec(lambda i: (jnp.maximum(i - 1, 0), 0, 0)),
            spec(lambda i: (i, 0, 0)),
            spec(lambda i: (jnp.minimum(i + 1, count - 1), 0, 0)),
            pl.BlockSpec((bx, ny), lambda i: (i, 0)),
        ],
        out_specs=spec(lambda i: (i, 0, 0)),
        out_shape=jax.ShapeDtypeStruct((nx, ny, ns), jnp.float32),
    )(low, high, block, block, block, coefficient)


def gram_schmidt_kernel(rows_ref, out_ref, work):
    count, width = rows_ref.shape
    blocks = count // 8
    group = 4 if blocks % 4 == 0 else 1
    work[...] = rows_ref[...]
    for first in range(0, blocks, group):

        def sweep(block, carry, first=first):
            base = pl.multiple_of(block * 8, 8)
            for lane_row in range(8):
                j = base + lane_row
                vector = work[pl.ds(j, 1), :]
                inverse = 1.0 / jnp.sum(vector * vector, axis=1, keepdims=True)
                for i in range(first, blocks):
                    rows = work[i * 8:(i + 1) * 8, :]
                    weight = jnp.sum(rows * vector, axis=1, keepdims=True) * inverse
                    ids = lax.broadcasted_iota(jnp.int32, weight.shape, 0) + i * 8
                    weight = jnp.where(ids > j, weight, 0.0)
                    work[i * 8:(i + 1) * 8, :] = rows - weight * vector
            return carry

        lax.fori_loop(first, first + group, sweep, 0)
    for i in range(blocks):
        rows = work[i * 8:(i + 1) * 8, :]
        norm = jnp.sqrt(jnp.sum(rows * rows, axis=1, keepdims=True))
        out_ref[i * 8:(i + 1) * 8, :] = rows / norm


def orthonormal(matrix):
    rows = matrix.T
    done = pl.pallas_call(
        gram_schmidt_kernel,
        out_shape=jax.ShapeDtypeStruct(rows.shape, jnp.float32),
        scratch_shapes=[pltpu.VMEM(rows.shape, jnp.float32)],
    )(rows)
    return done.T


def iterate(gram_matrix, basis_set):
    for sweep_index in range(ITERS):
        basis_set = orthonormal(jnp.dot(gram_matrix, basis_set, precision=highest))
    return basis_set


def cross_gram(left_rows, right_rows):
    return lax.dot_general(left_rows, right_rows, (((0,), (0,)), ((), ())), precision=high)


def self_gram(rows):
    upper = lax.reduce_precision(rows, exponent_bits=8, mantissa_bits=7)
    lower = lax.reduce_precision(rows - upper, exponent_bits=8, mantissa_bits=7)
    missing = jnp.sum(lower * lower, axis=0)
    return cross_gram(rows, rows) + jnp.diag(missing)


def on_device(snapshots, coefficient, start_first, start_merge):
    halo_low, halo_high = halos(snapshots, "tx", 2)
    rows_here = snapshots.shape[0] * snapshots.shape[1]
    order_size = snapshots.shape[2]
    modes_count = start_first.shape[1]
    share_count = modes_count // lax.axis_size("run")
    cells_total = rows_here * lax.axis_size("tx")
    member = lax.axis_index("run")
    is_first = member == 0
    own_start = lax.dynamic_slice_in_dim(start_first, member * order_size, order_size, 0)
    own_start = own_start.astype(jnp.float32)
    merge_start = start_merge.astype(jnp.float32)
    if lax.axis_size("tx") % 2:
        first_basis = orthonormal(own_start)
        merge_basis = orthonormal(merge_start)
    else:
        is_even = lax.axis_index("tx") % 2 == 0
        mine = orthonormal(jnp.where(is_even, own_start, merge_start))
        theirs = partner(mine, "tx", 0)
        first_basis = jnp.where(is_even, mine, theirs)
        merge_basis = jnp.where(is_even, theirs, mine)
    own_flux = fluxes(halo_low, snapshots, halo_high, coefficient).reshape(rows_here, order_size)
    half_rows = rows_here // 2
    half_start = member * half_rows
    sent_rows = lax.dynamic_slice_in_dim(own_flux, (1 - member) * half_rows, half_rows, 0)
    other_rows = partner(sent_rows, "run", 0)
    mixed_half = cross_gram(
        lax.dynamic_slice_in_dim(own_flux, half_start, half_rows, 0), other_rows
    )
    mixed_half = jnp.where(is_first, mixed_half, mixed_half.T)
    own_gram = tree_sum(self_gram(own_flux), "tx") / cells_total
    own_gram, mixed_sum = lax.optimization_barrier((own_gram, mixed_half))
    hops = butterfly_steps("tx")
    own_basis = first_basis
    for sweep_index in range(ITERS):
        product = jnp.dot(own_gram, own_basis, precision=highest)
        if hops:
            received = lax.ppermute(mixed_sum, "tx", hops.pop(0))
            own_basis = orthonormal(product)
            own_basis, received = lax.optimization_barrier((own_basis, received))
            mixed_sum = mixed_sum + received
        else:
            own_basis = orthonormal(product)
    for route in hops:
        mixed_sum = mixed_sum + lax.ppermute(mixed_sum, "tx", route)
    own_modes = jnp.dot(own_flux, own_basis, precision=high)
    mixed_gram = mixed_sum + partner(mixed_sum, "run", 0)
    other_modes = partner(own_modes, "run", 0)
    own_block = jnp.dot(own_basis.T, jnp.dot(own_gram, own_basis, precision=highest), precision=highest)
    other_block, other_basis = partner((own_block, own_basis), "run", 0)
    first_basis_set = jnp.where(is_first, own_basis, other_basis)
    last_basis_set = jnp.where(is_first, other_basis, own_basis)
    mixed_block = jnp.dot(
        first_basis_set.T,
        jnp.dot(mixed_gram / cells_total, last_basis_set, precision=highest),
        precision=highest,
    )
    first_block = jnp.where(is_first, own_block, other_block)
    last_block = jnp.where(is_first, other_block, own_block)
    merge_gram = jnp.concatenate(
        [
            jnp.concatenate([first_block, mixed_block], axis=1),
            jnp.concatenate([mixed_block.T, last_block], axis=1),
        ],
        axis=0,
    )
    rotation = iterate(merge_gram, merge_basis)
    rotation_share = lax.dynamic_slice_in_dim(rotation, member * share_count, share_count, 1)
    top_rows = rotation_share[:modes_count]
    bottom_rows = rotation_share[modes_count:]
    own_rotation = jnp.where(is_first, top_rows, bottom_rows)
    other_rotation = jnp.where(is_first, bottom_rows, top_rows)
    result = jnp.dot(own_modes, own_rotation, precision=high) + jnp.dot(
        other_modes, other_rotation, precision=high
    )
    return result.reshape(snapshots.shape[0], snapshots.shape[1], share_count)


def solution(mesh):
    in_specs = (P(("slab", "tx"), None, "run"), P(("slab", "tx"), None), P(), P())
    out_specs = P(("slab", "tx"), None, "run")
    return jax.shard_map(
        on_device, mesh=mesh, in_specs=in_specs, out_specs=out_specs, check_vma=False
    )
```

```python
import jax
import jax.numpy as jnp
from jax import lax
from jax.sharding import PartitionSpec as P
import functools
from jax.experimental import pallas as pl
from jax.experimental.pallas import tpu as pltpu

ITERS = 2


highest = lax.Precision.HIGHEST
high = lax.Precision.HIGH


def halos(block, axis, width):
    count = lax.axis_size(axis)
    forward = [(i, i + 1) for i in range(count - 1)]
    backward = [(target, source) for source, target in forward]
    low = lax.ppermute(lax.slice_in_dim(block, block.shape[0] - width, None, axis=0), axis, forward)
    high = lax.ppermute(lax.slice_in_dim(block, 0, width, axis=0), axis, backward)
    return low, high


def partner(block, axis, stride):
    count = lax.axis_size(axis)
    route = []
    for low in range(count):
        high = low | 1 << stride
        if high != low and high < count:
            route += [(low, high), (high, low)]
    return lax.ppermute(block, axis, route)


def tree_sum(value, axis):
    count = lax.axis_size(axis)
    if count & (count - 1):
        return lax.psum(value, axis)
    step = 1
    while step < count:
        route = [(i, i ^ step) for i in range(count)]
        value = value + lax.ppermute(value, axis, route)
        step *= 2
    return value


def butterfly_steps(axis):
    count = lax.axis_size(axis)
    assert count & (count - 1) == 0
    routes = []
    step = 1
    while step < count:
        routes.append([(i, i ^ step) for i in range(count)])
        step *= 2
    return routes


def fourth_order(values, axis_dim):
    length_kept = values.shape[axis_dim] - 4

    def shifted(offset):
        return lax.slice_in_dim(values, offset, offset + length_kept, axis=axis_dim)

    return (8.0 * (shifted(3) - shifted(1)) - (shifted(4) - shifted(0))) / 12.0


def flux_kernel(count, low_ref, high_ref, prev_ref, main_ref, next_ref, coef_ref, out_ref):
    i = pl.program_id(0)
    above = jnp.where(i == 0, low_ref[...], prev_ref[-2:])
    below = jnp.where(i == count - 1, high_ref[...], next_ref[:2])
    rows = jnp.concatenate([above, main_ref[...], below], axis=0).astype(jnp.float32)
    squared = 0.5 * jnp.square(rows)
    along_rows = fourth_order(squared, 0)
    mid = squared[2:-2]
    cols = mid.shape[1]
    ids = lax.broadcasted_iota(jnp.int32, mid.shape, 1)

    def shift(offset):
        moved = pltpu.roll(mid, (-offset) % cols, 1)
        inside = (ids + offset >= 0) & (ids + offset < cols)
        return jnp.where(inside, moved, 0.0)

    along_cols = (8.0 * (shift(1) - shift(-1)) - (shift(2) - shift(-2))) / 12.0
    central = rows[2:-2]
    out_ref[...] = central - coef_ref[...][:, :, None] * (along_rows + along_cols)


def fluxes(low, block, high, coefficient):
    nx, ny, ns = block.shape
    bx = 8 if nx % 8 == 0 else nx
    count = nx // bx

    def spec(index):
        return pl.BlockSpec((bx, ny, ns), index)

    return pl.pallas_call(
        functools.partial(flux_kernel, count),
        grid=(count,),
        in_specs=[
            pl.BlockSpec(low.shape, lambda i: (0, 0, 0)),
            pl.BlockSpec(high.shape, lambda i: (0, 0, 0)),
            spec(lambda i: (jnp.maximum(i - 1, 0), 0, 0)),
            spec(lambda i: (i, 0, 0)),
            spec(lambda i: (jnp.minimum(i + 1, count - 1), 0, 0)),
            pl.BlockSpec((bx, ny), lambda i: (i, 0)),
        ],
        out_specs=spec(lambda i: (i, 0, 0)),
        out_shape=jax.ShapeDtypeStruct((nx, ny, ns), jnp.float32),
    )(low, high, block, block, block, coefficient)


def gram_schmidt_kernel(rows_ref, out_ref, work):
    count, width = rows_ref.shape
    blocks = count // 8
    group = 4 if blocks % 4 == 0 else 1
    work[...] = rows_ref[...]
    for first in range(0, blocks, group):

        def sweep(block, carry, first=first):
            base = pl.multiple_of(block * 8, 8)
            for lane_row in range(8):
                j = base + lane_row
                vector = work[pl.ds(j, 1), :]
                inverse = 1.0 / jnp.sum(vector * vector, axis=1, keepdims=True)
                for i in range(first, blocks):
                    rows = work[i * 8:(i + 1) * 8, :]
                    weight = jnp.sum(rows * vector, axis=1, keepdims=True) * inverse
                    ids = lax.broadcasted_iota(jnp.int32, weight.shape, 0) + i * 8
                    weight = jnp.where(ids > j, weight, 0.0)
                    work[i * 8:(i + 1) * 8, :] = rows - weight * vector
            return carry

        lax.fori_loop(first, first + group, sweep, 0)
    for i in range(blocks):
        rows = work[i * 8:(i + 1) * 8, :]
        norm = jnp.sqrt(jnp.sum(rows * rows, axis=1, keepdims=True))
        out_ref[i * 8:(i + 1) * 8, :] = rows / norm


def orthonormal(matrix):
    rows = matrix.T
    done = pl.pallas_call(
        gram_schmidt_kernel,
        out_shape=jax.ShapeDtypeStruct(rows.shape, jnp.float32),
        scratch_shapes=[pltpu.VMEM(rows.shape, jnp.float32)],
    )(rows)
    return done.T


def iterate(gram_matrix, basis_set):
    for sweep_index in range(ITERS):
        basis_set = orthonormal(jnp.dot(gram_matrix, basis_set, precision=highest))
    return basis_set


def cross_gram(left_rows, right_rows):
    return lax.dot_general(left_rows, right_rows, (((0,), (0,)), ((), ())), precision=high)


def self_gram(rows):
    upper = lax.reduce_precision(rows, exponent_bits=8, mantissa_bits=7)
    lower = lax.reduce_precision(rows - upper, exponent_bits=8, mantissa_bits=7)
    missing = jnp.sum(lower * lower, axis=0)
    return cross_gram(rows, rows) + jnp.diag(missing)


def on_device(snapshots, coefficient, start_first, start_merge):
    halo_low, halo_high = halos(snapshots, "tx", 2)
    rows_here = snapshots.shape[0] * snapshots.shape[1]
    order_size = snapshots.shape[2]
    modes_count = start_first.shape[1]
    share_count = modes_count // lax.axis_size("run")
    cells_total = rows_here * lax.axis_size("tx")
    member = lax.axis_index("run")
    is_first = member == 0
    own_start = lax.dynamic_slice_in_dim(start_first, member * order_size, order_size, 0)
    own_start = own_start.astype(jnp.float32)
    merge_start = start_merge.astype(jnp.float32)
    if lax.axis_size("tx") % 2:
        first_basis = orthonormal(own_start)
        merge_basis = orthonormal(merge_start)
    else:
        is_even = lax.axis_index("tx") % 2 == 0
        mine = orthonormal(jnp.where(is_even, own_start, merge_start))
        theirs = partner(mine, "tx", 0)
        first_basis = jnp.where(is_even, mine, theirs)
        merge_basis = jnp.where(is_even, theirs, mine)
    own_flux = fluxes(halo_low, snapshots, halo_high, coefficient).reshape(rows_here, order_size)
    half_rows = rows_here // 2
    half_start = member * half_rows
    sent_rows = lax.dynamic_slice_in_dim(own_flux, (1 - member) * half_rows, half_rows, 0)
    other_rows = partner(sent_rows, "run", 0)
    mixed_half = cross_gram(
        lax.dynamic_slice_in_dim(own_flux, half_start, half_rows, 0), other_rows
    )
    mixed_half = jnp.where(is_first, mixed_half, mixed_half.T)
    own_gram = tree_sum(self_gram(own_flux), "tx") / cells_total
    own_gram, mixed_sum = lax.optimization_barrier((own_gram, mixed_half))
    hops = butterfly_steps("tx")
    own_basis = first_basis
    for sweep_index in range(ITERS):
        product = jnp.dot(own_gram, own_basis, precision=highest)
        if hops:
            received = lax.ppermute(mixed_sum, "tx", hops.pop(0))
            own_basis = orthonormal(product)
            own_basis, received = lax.optimization_barrier((own_basis, received))
            mixed_sum = mixed_sum + received
        else:
            own_basis = orthonormal(product)
    if hops:
        received = lax.ppermute(mixed_sum, "tx", hops.pop(0))
        own_modes = jnp.dot(own_flux, own_basis, precision=high)
        own_modes, received = lax.optimization_barrier((own_modes, received))
        mixed_sum = mixed_sum + received
    else:
        own_modes = jnp.dot(own_flux, own_basis, precision=high)
    for route in hops:
        mixed_sum = mixed_sum + lax.ppermute(mixed_sum, "tx", route)
    mixed_gram = mixed_sum + partner(mixed_sum, "run", 0)
    own_block = jnp.dot(own_basis.T, jnp.dot(own_gram, own_basis, precision=highest), precision=highest)
    other_block, other_basis = partner((own_block, own_basis), "run", 0)
    own_modes, mixed_gram, other_block, other_basis = lax.optimization_barrier(
        (own_modes, mixed_gram, other_block, other_basis)
    )
    other_modes = partner(own_modes, "run", 0)
    first_basis_set = jnp.where(is_first, own_basis, other_basis)
    last_basis_set = jnp.where(is_first, other_basis, own_basis)
    mixed_block = jnp.dot(
        first_basis_set.T,
        jnp.dot(mixed_gram / cells_total, last_basis_set, precision=highest),
        precision=highest,
    )
    first_block = jnp.where(is_first, own_block, other_block)
    last_block = jnp.where(is_first, other_block, own_block)
    merge_gram = jnp.concatenate(
        [
            jnp.concatenate([first_block, mixed_block], axis=1),
            jnp.concatenate([mixed_block.T, last_block], axis=1),
        ],
        axis=0,
    )
    rotation = iterate(merge_gram, merge_basis)
    rotation_share = lax.dynamic_slice_in_dim(rotation, member * share_count, share_count, 1)
    top_rows = rotation_share[:modes_count]
    bottom_rows = rotation_share[modes_count:]
    own_rotation = jnp.where(is_first, top_rows, bottom_rows)
    other_rotation = jnp.where(is_first, bottom_rows, top_rows)
    result = jnp.dot(own_modes, own_rotation, precision=high) + jnp.dot(
        other_modes, other_rotation, precision=high
    )
    return result.reshape(snapshots.shape[0], snapshots.shape[1], share_count)


def solution(mesh):
    in_specs = (P(("slab", "tx"), None, "run"), P(("slab", "tx"), None), P(), P())
    out_specs = P(("slab", "tx"), None, "run")
    return jax.shard_map(
        on_device, mesh=mesh, in_specs=in_specs, out_specs=out_specs, check_vma=False
    )
```

```python
import jax
import jax.numpy as jnp
from jax import lax
from jax.sharding import PartitionSpec as P
import functools
from jax.experimental import pallas as pl
from jax.experimental.pallas import tpu as pltpu

ITERS = 2


highest = lax.Precision.HIGHEST
high = lax.Precision.HIGH


def halos(block, axis, width):
    count = lax.axis_size(axis)
    forward = [(i, i + 1) for i in range(count - 1)]
    backward = [(target, source) for source, target in forward]
    low = lax.ppermute(lax.slice_in_dim(block, block.shape[0] - width, None, axis=0), axis, forward)
    high = lax.ppermute(lax.slice_in_dim(block, 0, width, axis=0), axis, backward)
    return low, high


def partner(block, axis, stride):
    count = lax.axis_size(axis)
    route = []
    for low in range(count):
        high = low | 1 << stride
        if high != low and high < count:
            route += [(low, high), (high, low)]
    return lax.ppermute(block, axis, route)


def tree_sum(value, axis):
    count = lax.axis_size(axis)
    if count & (count - 1):
        return lax.psum(value, axis)
    step = 1
    while step < count:
        route = [(i, i ^ step) for i in range(count)]
        value = value + lax.ppermute(value, axis, route)
        step *= 2
    return value


def butterfly_steps(axis):
    count = lax.axis_size(axis)
    assert count & (count - 1) == 0
    routes = []
    step = 1
    while step < count:
        routes.append([(i, i ^ step) for i in range(count)])
        step *= 2
    return routes


def fourth_order(values, axis_dim):
    length_kept = values.shape[axis_dim] - 4

    def shifted(offset):
        return lax.slice_in_dim(values, offset, offset + length_kept, axis=axis_dim)

    return (8.0 * (shifted(3) - shifted(1)) - (shifted(4) - shifted(0))) / 12.0


def flux_kernel(count, low_ref, high_ref, prev_ref, main_ref, next_ref, coef_ref, out_ref):
    i = pl.program_id(0)
    above = jnp.where(i == 0, low_ref[...], prev_ref[-2:])
    below = jnp.where(i == count - 1, high_ref[...], next_ref[:2])
    rows = jnp.concatenate([above, main_ref[...], below], axis=0).astype(jnp.float32)
    squared = 0.5 * jnp.square(rows)
    along_rows = fourth_order(squared, 0)
    mid = squared[2:-2]
    cols = mid.shape[1]
    ids = lax.broadcasted_iota(jnp.int32, mid.shape, 1)

    def shift(offset):
        moved = pltpu.roll(mid, (-offset) % cols, 1)
        inside = (ids + offset >= 0) & (ids + offset < cols)
        return jnp.where(inside, moved, 0.0)

    along_cols = (8.0 * (shift(1) - shift(-1)) - (shift(2) - shift(-2))) / 12.0
    central = rows[2:-2]
    out_ref[...] = central - coef_ref[...][:, :, None] * (along_rows + along_cols)


def fluxes(low, block, high, coefficient):
    nx, ny, ns = block.shape
    bx = 8 if nx % 8 == 0 else nx
    count = nx // bx

    def spec(index):
        return pl.BlockSpec((bx, ny, ns), index)

    return pl.pallas_call(
        functools.partial(flux_kernel, count),
        grid=(count,),
        in_specs=[
            pl.BlockSpec(low.shape, lambda i: (0, 0, 0)),
            pl.BlockSpec(high.shape, lambda i: (0, 0, 0)),
            spec(lambda i: (jnp.maximum(i - 1, 0), 0, 0)),
            spec(lambda i: (i, 0, 0)),
            spec(lambda i: (jnp.minimum(i + 1, count - 1), 0, 0)),
            pl.BlockSpec((bx, ny), lambda i: (i, 0)),
        ],
        out_specs=spec(lambda i: (i, 0, 0)),
        out_shape=jax.ShapeDtypeStruct((nx, ny, ns), jnp.float32),
    )(low, high, block, block, block, coefficient)


def gram_schmidt_kernel(rows_ref, out_ref, work):
    count, width = rows_ref.shape
    blocks = count // 8
    group = 4 if blocks % 4 == 0 else 1
    work[...] = rows_ref[...]
    for first in range(0, blocks, group):

        def sweep(block, carry, first=first):
            base = pl.multiple_of(block * 8, 8)
            for lane_row in range(8):
                j = base + lane_row
                vector = work[pl.ds(j, 1), :]
                inverse = 1.0 / jnp.sum(vector * vector, axis=1, keepdims=True)
                for i in range(first, blocks):
                    rows = work[i * 8:(i + 1) * 8, :]
                    weight = jnp.sum(rows * vector, axis=1, keepdims=True) * inverse
                    ids = lax.broadcasted_iota(jnp.int32, weight.shape, 0) + i * 8
                    weight = jnp.where(ids > j, weight, 0.0)
                    work[i * 8:(i + 1) * 8, :] = rows - weight * vector
            return carry

        lax.fori_loop(first, first + group, sweep, 0)
    for i in range(blocks):
        rows = work[i * 8:(i + 1) * 8, :]
        norm = jnp.sqrt(jnp.sum(rows * rows, axis=1, keepdims=True))
        out_ref[i * 8:(i + 1) * 8, :] = rows / norm


def orthonormal(matrix):
    rows = matrix.T
    done = pl.pallas_call(
        gram_schmidt_kernel,
        out_shape=jax.ShapeDtypeStruct(rows.shape, jnp.float32),
        scratch_shapes=[pltpu.VMEM(rows.shape, jnp.float32)],
    )(rows)
    return done.T


def iterate(gram_matrix, basis_set):
    for sweep_index in range(ITERS):
        basis_set = orthonormal(jnp.dot(gram_matrix, basis_set, precision=highest))
    return basis_set


def cross_gram(left_rows, right_rows):
    return lax.dot_general(left_rows, right_rows, (((0,), (0,)), ((), ())), precision=high)


def self_gram(rows):
    upper = lax.reduce_precision(rows, exponent_bits=8, mantissa_bits=7)
    lower = lax.reduce_precision(rows - upper, exponent_bits=8, mantissa_bits=7)
    missing = jnp.sum(lower * lower, axis=0)
    return cross_gram(rows, rows) + jnp.diag(missing)


def on_device(snapshots, coefficient, start_first, start_merge):
    halo_low, halo_high = halos(snapshots, "tx", 2)
    rows_here = snapshots.shape[0] * snapshots.shape[1]
    order_size = snapshots.shape[2]
    modes_count = start_first.shape[1]
    share_count = modes_count // lax.axis_size("run")
    cells_total = rows_here * lax.axis_size("tx")
    member = lax.axis_index("run")
    is_first = member == 0
    own_start = lax.dynamic_slice_in_dim(start_first, member * order_size, order_size, 0)
    own_start = own_start.astype(jnp.float32)
    merge_start = start_merge.astype(jnp.float32)
    if lax.axis_size("tx") % 2:
        first_basis = orthonormal(own_start)
        merge_basis = orthonormal(merge_start)
    else:
        is_even = lax.axis_index("tx") % 2 == 0
        mine = orthonormal(jnp.where(is_even, own_start, merge_start))
        theirs = partner(mine, "tx", 0)
        first_basis = jnp.where(is_even, mine, theirs)
        merge_basis = jnp.where(is_even, theirs, mine)
    own_flux = fluxes(halo_low, snapshots, halo_high, coefficient).reshape(rows_here, order_size)
    half_rows = rows_here // 2
    half_start = member * half_rows
    other_flux = partner(own_flux, "run", 0)
    mixed_half = cross_gram(
        lax.dynamic_slice_in_dim(own_flux, half_start, half_rows, 0),
        lax.dynamic_slice_in_dim(other_flux, half_start, half_rows, 0),
    )
    mixed_half = jnp.where(is_first, mixed_half, mixed_half.T)
    own_gram = tree_sum(self_gram(own_flux), "tx") / cells_total
    own_gram, mixed_sum = lax.optimization_barrier((own_gram, mixed_half))
    hops = butterfly_steps("tx")
    own_basis = first_basis
    for sweep_index in range(ITERS):
        product = jnp.dot(own_gram, own_basis, precision=highest)
        if hops:
            received = lax.ppermute(mixed_sum, "tx", hops.pop(0))
            own_basis = orthonormal(product)
            own_basis, received = lax.optimization_barrier((own_basis, received))
            mixed_sum = mixed_sum + received
        else:
            own_basis = orthonormal(product)
    if hops:
        received = lax.ppermute(mixed_sum, "tx", hops.pop(0))
        own_modes = jnp.dot(own_flux, own_basis, precision=high)
        own_modes, received = lax.optimization_barrier((own_modes, received))
        mixed_sum = mixed_sum + received
    else:
        own_modes = jnp.dot(own_flux, own_basis, precision=high)
    for route in hops:
        mixed_sum = mixed_sum + lax.ppermute(mixed_sum, "tx", route)
    mixed_gram = mixed_sum + partner(mixed_sum, "run", 0)
    own_block = jnp.dot(own_basis.T, jnp.dot(own_gram, own_basis, precision=highest), precision=highest)
    other_block, other_basis = partner((own_block, own_basis), "run", 0)
    own_modes, mixed_gram, other_block, other_basis = lax.optimization_barrier(
        (own_modes, mixed_gram, other_block, other_basis)
    )
    other_modes = partner(own_modes, "run", 0)
    first_basis_set = jnp.where(is_first, own_basis, other_basis)
    last_basis_set = jnp.where(is_first, other_basis, own_basis)
    mixed_block = jnp.dot(
        first_basis_set.T,
        jnp.dot(mixed_gram / cells_total, last_basis_set, precision=highest),
        precision=highest,
    )
    first_block = jnp.where(is_first, own_block, other_block)
    last_block = jnp.where(is_first, other_block, own_block)
    merge_gram = jnp.concatenate(
        [
            jnp.concatenate([first_block, mixed_block], axis=1),
            jnp.concatenate([mixed_block.T, last_block], axis=1),
        ],
        axis=0,
    )
    rotation = iterate(merge_gram, merge_basis)
    rotation_share = lax.dynamic_slice_in_dim(rotation, member * share_count, share_count, 1)
    top_rows = rotation_share[:modes_count]
    bottom_rows = rotation_share[modes_count:]
    own_rotation = jnp.where(is_first, top_rows, bottom_rows)
    other_rotation = jnp.where(is_first, bottom_rows, top_rows)
    result = jnp.dot(own_modes, own_rotation, precision=high) + jnp.dot(
        other_modes, other_rotation, precision=high
    )
    return result.reshape(snapshots.shape[0], snapshots.shape[1], share_count)


def solution(mesh):
    in_specs = (P(("slab", "tx"), None, "run"), P(("slab", "tx"), None), P(), P())
    out_specs = P(("slab", "tx"), None, "run")
    return jax.shard_map(
        on_device, mesh=mesh, in_specs=in_specs, out_specs=out_specs, check_vma=False
    )
```

```python
import jax
import jax.numpy as jnp
from jax import lax
from jax.sharding import PartitionSpec as P
import functools
from jax.experimental import pallas as pl
from jax.experimental.pallas import tpu as pltpu

ITERS = 2


highest = lax.Precision.HIGHEST
high = lax.Precision.HIGH


def halos(block, axis, width):
    count = lax.axis_size(axis)
    forward = [(i, i + 1) for i in range(count - 1)]
    backward = [(target, source) for source, target in forward]
    low = lax.ppermute(lax.slice_in_dim(block, block.shape[0] - width, None, axis=0), axis, forward)
    high = lax.ppermute(lax.slice_in_dim(block, 0, width, axis=0), axis, backward)
    return low, high


def partner(block, axis, stride):
    count = lax.axis_size(axis)
    route = []
    for low in range(count):
        high = low | 1 << stride
        if high != low and high < count:
            route += [(low, high), (high, low)]
    return lax.ppermute(block, axis, route)


def tree_sum(value, axis):
    count = lax.axis_size(axis)
    if count & (count - 1):
        return lax.psum(value, axis)
    step = 1
    while step < count:
        route = [(i, i ^ step) for i in range(count)]
        value = value + lax.ppermute(value, axis, route)
        step *= 2
    return value


def butterfly_steps(axis):
    count = lax.axis_size(axis)
    assert count & (count - 1) == 0
    routes = []
    step = 1
    while step < count:
        routes.append([(i, i ^ step) for i in range(count)])
        step *= 2
    return routes


def fourth_order(values, axis_dim):
    length_kept = values.shape[axis_dim] - 4

    def shifted(offset):
        return lax.slice_in_dim(values, offset, offset + length_kept, axis=axis_dim)

    return (8.0 * (shifted(3) - shifted(1)) - (shifted(4) - shifted(0))) / 12.0


def flux_kernel(count, low_ref, high_ref, prev_ref, main_ref, next_ref, coef_ref, out_ref):
    i = pl.program_id(0)
    above = jnp.where(i == 0, low_ref[...], prev_ref[-2:])
    below = jnp.where(i == count - 1, high_ref[...], next_ref[:2])
    rows = jnp.concatenate([above, main_ref[...], below], axis=0).astype(jnp.float32)
    squared = 0.5 * jnp.square(rows)
    along_rows = fourth_order(squared, 0)
    mid = squared[2:-2]
    cols = mid.shape[1]
    ids = lax.broadcasted_iota(jnp.int32, mid.shape, 1)

    def shift(offset):
        moved = pltpu.roll(mid, (-offset) % cols, 1)
        inside = (ids + offset >= 0) & (ids + offset < cols)
        return jnp.where(inside, moved, 0.0)

    along_cols = (8.0 * (shift(1) - shift(-1)) - (shift(2) - shift(-2))) / 12.0
    central = rows[2:-2]
    out_ref[...] = central - coef_ref[...][:, :, None] * (along_rows + along_cols)


def fluxes(low, block, high, coefficient):
    nx, ny, ns = block.shape
    bx = 8 if nx % 8 == 0 else nx
    count = nx // bx

    def spec(index):
        return pl.BlockSpec((bx, ny, ns), index)

    return pl.pallas_call(
        functools.partial(flux_kernel, count),
        grid=(count,),
        in_specs=[
            pl.BlockSpec(low.shape, lambda i: (0, 0, 0)),
            pl.BlockSpec(high.shape, lambda i: (0, 0, 0)),
            spec(lambda i: (jnp.maximum(i - 1, 0), 0, 0)),
            spec(lambda i: (i, 0, 0)),
            spec(lambda i: (jnp.minimum(i + 1, count - 1), 0, 0)),
            pl.BlockSpec((bx, ny), lambda i: (i, 0)),
        ],
        out_specs=spec(lambda i: (i, 0, 0)),
        out_shape=jax.ShapeDtypeStruct((nx, ny, ns), jnp.float32),
    )(low, high, block, block, block, coefficient)


def gram_schmidt_kernel(rows_ref, out_ref, work):
    count, width = rows_ref.shape
    blocks = count // 8
    group = 4 if blocks % 4 == 0 else 1
    work[...] = rows_ref[...]
    for first in range(0, blocks, group):

        def sweep(block, carry, first=first):
            base = pl.multiple_of(block * 8, 8)
            for lane_row in range(8):
                j = base + lane_row
                vector = work[pl.ds(j, 1), :]
                inverse = 1.0 / jnp.sum(vector * vector, axis=1, keepdims=True)
                for i in range(first, blocks):
                    rows = work[i * 8:(i + 1) * 8, :]
                    weight = jnp.sum(rows * vector, axis=1, keepdims=True) * inverse
                    ids = lax.broadcasted_iota(jnp.int32, weight.shape, 0) + i * 8
                    weight = jnp.where(ids > j, weight, 0.0)
                    work[i * 8:(i + 1) * 8, :] = rows - weight * vector
            return carry

        lax.fori_loop(first, first + group, sweep, 0)
    for i in range(blocks):
        rows = work[i * 8:(i + 1) * 8, :]
        norm = jnp.sqrt(jnp.sum(rows * rows, axis=1, keepdims=True))
        out_ref[i * 8:(i + 1) * 8, :] = rows / norm


def orthonormal(matrix):
    rows = matrix.T
    done = pl.pallas_call(
        gram_schmidt_kernel,
        out_shape=jax.ShapeDtypeStruct(rows.shape, jnp.float32),
        scratch_shapes=[pltpu.VMEM(rows.shape, jnp.float32)],
    )(rows)
    return done.T


def iterate(gram_matrix, basis_set):
    for sweep_index in range(ITERS):
        basis_set = orthonormal(jnp.dot(gram_matrix, basis_set, precision=highest))
    return basis_set


def cross_gram(left_rows, right_rows):
    return lax.dot_general(left_rows, right_rows, (((0,), (0,)), ((), ())), precision=high)


def self_gram(rows):
    upper = lax.reduce_precision(rows, exponent_bits=8, mantissa_bits=7)
    lower = lax.reduce_precision(rows - upper, exponent_bits=8, mantissa_bits=7)
    missing = jnp.sum(lower * lower, axis=0)
    return cross_gram(rows, rows) + jnp.diag(missing)


def on_device(snapshots, coefficient, start_first, start_merge):
    halo_low, halo_high = halos(snapshots, "tx", 2)
    rows_here = snapshots.shape[0] * snapshots.shape[1]
    order_size = snapshots.shape[2]
    modes_count = start_first.shape[1]
    share_count = modes_count // lax.axis_size("run")
    cells_total = rows_here * lax.axis_size("tx")
    member = lax.axis_index("run")
    is_first = member == 0
    own_start = lax.dynamic_slice_in_dim(start_first, member * order_size, order_size, 0)
    own_start = own_start.astype(jnp.float32)
    merge_start = start_merge.astype(jnp.float32)
    if lax.axis_size("tx") % 2:
        first_basis = orthonormal(own_start)
        merge_basis = orthonormal(merge_start)
    else:
        is_even = lax.axis_index("tx") % 2 == 0
        mine = orthonormal(jnp.where(is_even, own_start, merge_start))
        theirs = partner(mine, "tx", 0)
        first_basis = jnp.where(is_even, mine, theirs)
        merge_basis = jnp.where(is_even, theirs, mine)
    own_flux = fluxes(halo_low, snapshots, halo_high, coefficient).reshape(rows_here, order_size)
    half_rows = rows_here // 2
    half_start = member * half_rows
    sent_rows = lax.dynamic_slice_in_dim(own_flux, (1 - member) * half_rows, half_rows, 0)
    other_rows = partner(sent_rows, "run", 0)
    mixed_half = cross_gram(
        lax.dynamic_slice_in_dim(own_flux, half_start, half_rows, 0), other_rows
    )
    mixed_half = jnp.where(is_first, mixed_half, mixed_half.T)
    gram_hops = butterfly_steps("tx")
    own_gram = self_gram(own_flux)
    if gram_hops:
        received = lax.ppermute(own_gram, "tx", gram_hops.pop(0))
        received, mixed_half = lax.optimization_barrier((received, mixed_half))
        own_gram = own_gram + received
    for route in gram_hops:
        own_gram = own_gram + lax.ppermute(own_gram, "tx", route)
    own_gram = own_gram / cells_total
    own_gram, mixed_sum = lax.optimization_barrier((own_gram, mixed_half))
    hops = butterfly_steps("tx")
    own_basis = first_basis
    for sweep_index in range(ITERS):
        product = jnp.dot(own_gram, own_basis, precision=highest)
        if hops:
            received = lax.ppermute(mixed_sum, "tx", hops.pop(0))
            own_basis = orthonormal(product)
            own_basis, received = lax.optimization_barrier((own_basis, received))
            mixed_sum = mixed_sum + received
        else:
            own_basis = orthonormal(product)
    if hops:
        received = lax.ppermute(mixed_sum, "tx", hops.pop(0))
        own_modes = jnp.dot(own_flux, own_basis, precision=high)
        own_modes, received = lax.optimization_barrier((own_modes, received))
        mixed_sum = mixed_sum + received
    else:
        own_modes = jnp.dot(own_flux, own_basis, precision=high)
    for route in hops:
        mixed_sum = mixed_sum + lax.ppermute(mixed_sum, "tx", route)
    mixed_gram = mixed_sum + partner(mixed_sum, "run", 0)
    own_block = jnp.dot(own_basis.T, jnp.dot(own_gram, own_basis, precision=highest), precision=highest)
    other_block, other_basis = partner((own_block, own_basis), "run", 0)
    own_modes, mixed_gram, other_block, other_basis = lax.optimization_barrier(
        (own_modes, mixed_gram, other_block, other_basis)
    )
    other_modes = partner(own_modes, "run", 0)
    first_basis_set = jnp.where(is_first, own_basis, other_basis)
    last_basis_set = jnp.where(is_first, other_basis, own_basis)
    mixed_block = jnp.dot(
        first_basis_set.T,
        jnp.dot(mixed_gram / cells_total, last_basis_set, precision=highest),
        precision=highest,
    )
    first_block = jnp.where(is_first, own_block, other_block)
    last_block = jnp.where(is_first, other_block, own_block)
    merge_gram = jnp.concatenate(
        [
            jnp.concatenate([first_block, mixed_block], axis=1),
            jnp.concatenate([mixed_block.T, last_block], axis=1),
        ],
        axis=0,
    )
    rotation = iterate(merge_gram, merge_basis)
    rotation_share = lax.dynamic_slice_in_dim(rotation, member * share_count, share_count, 1)
    top_rows = rotation_share[:modes_count]
    bottom_rows = rotation_share[modes_count:]
    own_rotation = jnp.where(is_first, top_rows, bottom_rows)
    other_rotation = jnp.where(is_first, bottom_rows, top_rows)
    result = jnp.dot(own_modes, own_rotation, precision=high) + jnp.dot(
        other_modes, other_rotation, precision=high
    )
    return result.reshape(snapshots.shape[0], snapshots.shape[1], share_count)


def solution(mesh):
    in_specs = (P(("slab", "tx"), None, "run"), P(("slab", "tx"), None), P(), P())
    out_specs = P(("slab", "tx"), None, "run")
    return jax.shard_map(
        on_device, mesh=mesh, in_specs=in_specs, out_specs=out_specs, check_vma=False
    )
```

```python
import jax
import jax.numpy as jnp
from jax import lax
from jax.sharding import PartitionSpec as P
import functools
from jax.experimental import pallas as pl
from jax.experimental.pallas import tpu as pltpu

ITERS = 2


highest = lax.Precision.HIGHEST
high = lax.Precision.HIGH


def halos(block, axis, width):
    count = lax.axis_size(axis)
    forward = [(i, i + 1) for i in range(count - 1)]
    backward = [(target, source) for source, target in forward]
    low = lax.ppermute(lax.slice_in_dim(block, block.shape[0] - width, None, axis=0), axis, forward)
    high = lax.ppermute(lax.slice_in_dim(block, 0, width, axis=0), axis, backward)
    return low, high


def partner(block, axis, stride):
    count = lax.axis_size(axis)
    route = []
    for low in range(count):
        high = low | 1 << stride
        if high != low and high < count:
            route += [(low, high), (high, low)]
    return lax.ppermute(block, axis, route)


def tree_sum(value, axis):
    count = lax.axis_size(axis)
    if count & (count - 1):
        return lax.psum(value, axis)
    step = 1
    while step < count:
        route = [(i, i ^ step) for i in range(count)]
        value = value + lax.ppermute(value, axis, route)
        step *= 2
    return value


def butterfly_steps(axis):
    count = lax.axis_size(axis)
    assert count & (count - 1) == 0
    routes = []
    step = 1
    while step < count:
        routes.append([(i, i ^ step) for i in range(count)])
        step *= 2
    return routes


def fourth_order(values, axis_dim):
    length_kept = values.shape[axis_dim] - 4

    def shifted(offset):
        return lax.slice_in_dim(values, offset, offset + length_kept, axis=axis_dim)

    return (8.0 * (shifted(3) - shifted(1)) - (shifted(4) - shifted(0))) / 12.0


def flux_kernel(count, low_ref, high_ref, prev_ref, main_ref, next_ref, coef_ref, out_ref):
    i = pl.program_id(0)
    above = jnp.where(i == 0, low_ref[...], prev_ref[-2:])
    below = jnp.where(i == count - 1, high_ref[...], next_ref[:2])
    rows = jnp.concatenate([above, main_ref[...], below], axis=0).astype(jnp.float32)
    squared = 0.5 * jnp.square(rows)
    along_rows = fourth_order(squared, 0)
    mid = squared[2:-2]
    cols = mid.shape[1]
    ids = lax.broadcasted_iota(jnp.int32, mid.shape, 1)

    def shift(offset):
        moved = pltpu.roll(mid, (-offset) % cols, 1)
        inside = (ids + offset >= 0) & (ids + offset < cols)
        return jnp.where(inside, moved, 0.0)

    along_cols = (8.0 * (shift(1) - shift(-1)) - (shift(2) - shift(-2))) / 12.0
    central = rows[2:-2]
    out_ref[...] = central - coef_ref[...][:, :, None] * (along_rows + along_cols)


def fluxes(low, block, high, coefficient):
    nx, ny, ns = block.shape
    bx = 8 if nx % 8 == 0 else nx
    count = nx // bx

    def spec(index):
        return pl.BlockSpec((bx, ny, ns), index)

    return pl.pallas_call(
        functools.partial(flux_kernel, count),
        grid=(count,),
        in_specs=[
            pl.BlockSpec(low.shape, lambda i: (0, 0, 0)),
            pl.BlockSpec(high.shape, lambda i: (0, 0, 0)),
            spec(lambda i: (jnp.maximum(i - 1, 0), 0, 0)),
            spec(lambda i: (i, 0, 0)),
            spec(lambda i: (jnp.minimum(i + 1, count - 1), 0, 0)),
            pl.BlockSpec((bx, ny), lambda i: (i, 0)),
        ],
        out_specs=spec(lambda i: (i, 0, 0)),
        out_shape=jax.ShapeDtypeStruct((nx, ny, ns), jnp.float32),
    )(low, high, block, block, block, coefficient)


def gram_schmidt_kernel(rows_ref, out_ref, work):
    count, width = rows_ref.shape
    blocks = count // 8
    group = 2 if blocks % 2 == 0 else 1
    work[...] = rows_ref[...]
    for first in range(0, blocks, group):

        def sweep(block, carry, first=first):
            base = pl.multiple_of(block * 8, 8)
            for lane_row in range(8):
                j = base + lane_row
                vector = work[pl.ds(j, 1), :]
                inverse = 1.0 / jnp.sum(vector * vector, axis=1, keepdims=True)
                for i in range(first, blocks):
                    rows = work[i * 8:(i + 1) * 8, :]
                    weight = jnp.sum(rows * vector, axis=1, keepdims=True) * inverse
                    ids = lax.broadcasted_iota(jnp.int32, weight.shape, 0) + i * 8
                    weight = jnp.where(ids > j, weight, 0.0)
                    work[i * 8:(i + 1) * 8, :] = rows - weight * vector
            return carry

        lax.fori_loop(first, first + group, sweep, 0)
    for i in range(blocks):
        rows = work[i * 8:(i + 1) * 8, :]
        norm = jnp.sqrt(jnp.sum(rows * rows, axis=1, keepdims=True))
        out_ref[i * 8:(i + 1) * 8, :] = rows / norm


def orthonormal(matrix):
    rows = matrix.T
    done = pl.pallas_call(
        gram_schmidt_kernel,
        out_shape=jax.ShapeDtypeStruct(rows.shape, jnp.float32),
        scratch_shapes=[pltpu.VMEM(rows.shape, jnp.float32)],
    )(rows)
    return done.T


def iterate(gram_matrix, basis_set):
    for sweep_index in range(ITERS):
        basis_set = orthonormal(jnp.dot(gram_matrix, basis_set, precision=highest))
    return basis_set


def cross_gram(left_rows, right_rows):
    return lax.dot_general(left_rows, right_rows, (((0,), (0,)), ((), ())), precision=high)


def self_gram(rows):
    upper = lax.reduce_precision(rows, exponent_bits=8, mantissa_bits=7)
    lower = lax.reduce_precision(rows - upper, exponent_bits=8, mantissa_bits=7)
    missing = jnp.sum(lower * lower, axis=0)
    return cross_gram(rows, rows) + jnp.diag(missing)


def on_device(snapshots, coefficient, start_first, start_merge):
    halo_low, halo_high = halos(snapshots, "tx", 2)
    rows_here = snapshots.shape[0] * snapshots.shape[1]
    order_size = snapshots.shape[2]
    modes_count = start_first.shape[1]
    share_count = modes_count // lax.axis_size("run")
    cells_total = rows_here * lax.axis_size("tx")
    member = lax.axis_index("run")
    is_first = member == 0
    own_start = lax.dynamic_slice_in_dim(start_first, member * order_size, order_size, 0)
    own_start = own_start.astype(jnp.float32)
    merge_start = start_merge.astype(jnp.float32)
    if lax.axis_size("tx") % 2:
        first_basis = orthonormal(own_start)
        merge_basis = orthonormal(merge_start)
    else:
        is_even = lax.axis_index("tx") % 2 == 0
        mine = orthonormal(jnp.where(is_even, own_start, merge_start))
        theirs = partner(mine, "tx", 0)
        first_basis = jnp.where(is_even, mine, theirs)
        merge_basis = jnp.where(is_even, theirs, mine)
    own_flux = fluxes(halo_low, snapshots, halo_high, coefficient).reshape(rows_here, order_size)
    half_rows = rows_here // 2
    half_start = member * half_rows
    sent_rows = lax.dynamic_slice_in_dim(own_flux, (1 - member) * half_rows, half_rows, 0)
    other_rows = partner(sent_rows, "run", 0)
    mixed_half = cross_gram(
        lax.dynamic_slice_in_dim(own_flux, half_start, half_rows, 0), other_rows
    )
    mixed_half = jnp.where(is_first, mixed_half, mixed_half.T)
    own_gram = tree_sum(self_gram(own_flux), "tx") / cells_total
    own_gram, mixed_sum = lax.optimization_barrier((own_gram, mixed_half))
    hops = butterfly_steps("tx")
    own_basis = first_basis
    for sweep_index in range(ITERS):
        product = jnp.dot(own_gram, own_basis, precision=highest)
        if hops:
            received = lax.ppermute(mixed_sum, "tx", hops.pop(0))
            own_basis = orthonormal(product)
            own_basis, received = lax.optimization_barrier((own_basis, received))
            mixed_sum = mixed_sum + received
        else:
            own_basis = orthonormal(product)
    if hops:
        received = lax.ppermute(mixed_sum, "tx", hops.pop(0))
        own_modes = jnp.dot(own_flux, own_basis, precision=high)
        own_modes, received = lax.optimization_barrier((own_modes, received))
        mixed_sum = mixed_sum + received
    else:
        own_modes = jnp.dot(own_flux, own_basis, precision=high)
    for route in hops:
        mixed_sum = mixed_sum + lax.ppermute(mixed_sum, "tx", route)
    mixed_gram = mixed_sum + partner(mixed_sum, "run", 0)
    own_block = jnp.dot(own_basis.T, jnp.dot(own_gram, own_basis, precision=highest), precision=highest)
    other_block, other_basis = partner((own_block, own_basis), "run", 0)
    own_modes, mixed_gram, other_block, other_basis = lax.optimization_barrier(
        (own_modes, mixed_gram, other_block, other_basis)
    )
    other_modes = partner(own_modes, "run", 0)
    first_basis_set = jnp.where(is_first, own_basis, other_basis)
    last_basis_set = jnp.where(is_first, other_basis, own_basis)
    mixed_block = jnp.dot(
        first_basis_set.T,
        jnp.dot(mixed_gram / cells_total, last_basis_set, precision=highest),
        precision=highest,
    )
    first_block = jnp.where(is_first, own_block, other_block)
    last_block = jnp.where(is_first, other_block, own_block)
    merge_gram = jnp.concatenate(
        [
            jnp.concatenate([first_block, mixed_block], axis=1),
            jnp.concatenate([mixed_block.T, last_block], axis=1),
        ],
        axis=0,
    )
    rotation = iterate(merge_gram, merge_basis)
    rotation_share = lax.dynamic_slice_in_dim(rotation, member * share_count, share_count, 1)
    top_rows = rotation_share[:modes_count]
    bottom_rows = rotation_share[modes_count:]
    own_rotation = jnp.where(is_first, top_rows, bottom_rows)
    other_rotation = jnp.where(is_first, bottom_rows, top_rows)
    result = jnp.dot(own_modes, own_rotation, precision=high) + jnp.dot(
        other_modes, other_rotation, precision=high
    )
    return result.reshape(snapshots.shape[0], snapshots.shape[1], share_count)


def solution(mesh):
    in_specs = (P(("slab", "tx"), None, "run"), P(("slab", "tx"), None), P(), P())
    out_specs = P(("slab", "tx"), None, "run")
    return jax.shard_map(
        on_device, mesh=mesh, in_specs=in_specs, out_specs=out_specs, check_vma=False
    )
```

```python
import jax
import jax.numpy as jnp
from jax import lax
from jax.sharding import PartitionSpec as P
import functools
from jax.experimental import pallas as pl
from jax.experimental.pallas import tpu as pltpu

ITERS = 2


highest = lax.Precision.HIGHEST
high = lax.Precision.HIGH


def halos(block, axis, width):
    count = lax.axis_size(axis)
    forward = [(i, i + 1) for i in range(count - 1)]
    backward = [(target, source) for source, target in forward]
    low = lax.ppermute(lax.slice_in_dim(block, block.shape[0] - width, None, axis=0), axis, forward)
    high = lax.ppermute(lax.slice_in_dim(block, 0, width, axis=0), axis, backward)
    return low, high


def partner(block, axis, stride):
    count = lax.axis_size(axis)
    route = []
    for low in range(count):
        high = low | 1 << stride
        if high != low and high < count:
            route += [(low, high), (high, low)]
    return lax.ppermute(block, axis, route)


def tree_sum(value, axis):
    count = lax.axis_size(axis)
    if count & (count - 1):
        return lax.psum(value, axis)
    step = 1
    while step < count:
        route = [(i, i ^ step) for i in range(count)]
        value = value + lax.ppermute(value, axis, route)
        step *= 2
    return value


def butterfly_steps(axis):
    count = lax.axis_size(axis)
    assert count & (count - 1) == 0
    routes = []
    step = 1
    while step < count:
        routes.append([(i, i ^ step) for i in range(count)])
        step *= 2
    return routes


def fourth_order(values, axis_dim):
    length_kept = values.shape[axis_dim] - 4

    def shifted(offset):
        return lax.slice_in_dim(values, offset, offset + length_kept, axis=axis_dim)

    return (8.0 * (shifted(3) - shifted(1)) - (shifted(4) - shifted(0))) / 12.0


def flux_kernel(count, low_ref, high_ref, prev_ref, main_ref, next_ref, coef_ref, out_ref):
    i = pl.program_id(0)
    above = jnp.where(i == 0, low_ref[...], prev_ref[-2:])
    below = jnp.where(i == count - 1, high_ref[...], next_ref[:2])
    rows = jnp.concatenate([above, main_ref[...], below], axis=0).astype(jnp.float32)
    squared = 0.5 * jnp.square(rows)
    along_rows = fourth_order(squared, 0)
    mid = squared[2:-2]
    cols = mid.shape[1]
    ids = lax.broadcasted_iota(jnp.int32, mid.shape, 1)

    def shift(offset):
        moved = pltpu.roll(mid, (-offset) % cols, 1)
        inside = (ids + offset >= 0) & (ids + offset < cols)
        return jnp.where(inside, moved, 0.0)

    along_cols = (8.0 * (shift(1) - shift(-1)) - (shift(2) - shift(-2))) / 12.0
    central = rows[2:-2]
    out_ref[...] = central - coef_ref[...][:, :, None] * (along_rows + along_cols)


def fluxes(low, block, high, coefficient):
    nx, ny, ns = block.shape
    bx = 8 if nx % 8 == 0 else nx
    count = nx // bx

    def spec(index):
        return pl.BlockSpec((bx, ny, ns), index)

    return pl.pallas_call(
        functools.partial(flux_kernel, count),
        grid=(count,),
        in_specs=[
            pl.BlockSpec(low.shape, lambda i: (0, 0, 0)),
            pl.BlockSpec(high.shape, lambda i: (0, 0, 0)),
            spec(lambda i: (jnp.maximum(i - 1, 0), 0, 0)),
            spec(lambda i: (i, 0, 0)),
            spec(lambda i: (jnp.minimum(i + 1, count - 1), 0, 0)),
            pl.BlockSpec((bx, ny), lambda i: (i, 0)),
        ],
        out_specs=spec(lambda i: (i, 0, 0)),
        out_shape=jax.ShapeDtypeStruct((nx, ny, ns), jnp.float32),
    )(low, high, block, block, block, coefficient)


def gram_schmidt_kernel(rows_ref, out_ref, work):
    count, width = rows_ref.shape
    blocks = count // 8
    group = 4 if blocks % 4 == 0 else 1
    work[...] = rows_ref[...]
    for first in range(0, blocks, group):

        def sweep(block, carry, first=first):
            base = pl.multiple_of(block * 8, 8)
            pivot_rows = work[pl.ds(base, 8), :]
            for lane_row in range(8):
                j = base + lane_row
                vector = pivot_rows[lane_row:lane_row + 1, :]
                inverse = 1.0 / jnp.sum(vector * vector, axis=1, keepdims=True)
                weight = jnp.sum(pivot_rows * vector, axis=1, keepdims=True) * inverse
                ids = lax.broadcasted_iota(jnp.int32, weight.shape, 0)
                weight = jnp.where(ids > lane_row, weight, 0.0)
                pivot_rows = pivot_rows - weight * vector
                for i in range(first, blocks):
                    rows = work[i * 8:(i + 1) * 8, :]
                    weight = jnp.sum(rows * vector, axis=1, keepdims=True) * inverse
                    ids = lax.broadcasted_iota(jnp.int32, weight.shape, 0) + i * 8
                    weight = jnp.where(ids > j, weight, 0.0)
                    work[i * 8:(i + 1) * 8, :] = rows - weight * vector
            work[pl.ds(base, 8), :] = pivot_rows
            return carry

        lax.fori_loop(first, first + group, sweep, 0)
    for i in range(blocks):
        rows = work[i * 8:(i + 1) * 8, :]
        norm = jnp.sqrt(jnp.sum(rows * rows, axis=1, keepdims=True))
        out_ref[i * 8:(i + 1) * 8, :] = rows / norm


def orthonormal(matrix):
    rows = matrix.T
    done = pl.pallas_call(
        gram_schmidt_kernel,
        out_shape=jax.ShapeDtypeStruct(rows.shape, jnp.float32),
        scratch_shapes=[pltpu.VMEM(rows.shape, jnp.float32)],
    )(rows)
    return done.T


def iterate(gram_matrix, basis_set):
    for sweep_index in range(ITERS):
        basis_set = orthonormal(jnp.dot(gram_matrix, basis_set, precision=highest))
    return basis_set


def cross_gram(left_rows, right_rows):
    return lax.dot_general(left_rows, right_rows, (((0,), (0,)), ((), ())), precision=high)


def self_gram(rows):
    upper = lax.reduce_precision(rows, exponent_bits=8, mantissa_bits=7)
    lower = lax.reduce_precision(rows - upper, exponent_bits=8, mantissa_bits=7)
    missing = jnp.sum(lower * lower, axis=0)
    return cross_gram(rows, rows) + jnp.diag(missing)


def on_device(snapshots, coefficient, start_first, start_merge):
    halo_low, halo_high = halos(snapshots, "tx", 2)
    rows_here = snapshots.shape[0] * snapshots.shape[1]
    order_size = snapshots.shape[2]
    modes_count = start_first.shape[1]
    share_count = modes_count // lax.axis_size("run")
    cells_total = rows_here * lax.axis_size("tx")
    member = lax.axis_index("run")
    is_first = member == 0
    own_start = lax.dynamic_slice_in_dim(start_first, member * order_size, order_size, 0)
    own_start = own_start.astype(jnp.float32)
    merge_start = start_merge.astype(jnp.float32)
    if lax.axis_size("tx") % 2:
        first_basis = orthonormal(own_start)
        merge_basis = orthonormal(merge_start)
    else:
        is_even = lax.axis_index("tx") % 2 == 0
        mine = orthonormal(jnp.where(is_even, own_start, merge_start))
        theirs = partner(mine, "tx", 0)
        first_basis = jnp.where(is_even, mine, theirs)
        merge_basis = jnp.where(is_even, theirs, mine)
    own_flux = fluxes(halo_low, snapshots, halo_high, coefficient).reshape(rows_here, order_size)
    half_rows = rows_here // 2
    half_start = member * half_rows
    sent_rows = lax.dynamic_slice_in_dim(own_flux, (1 - member) * half_rows, half_rows, 0)
    other_rows = partner(sent_rows, "run", 0)
    mixed_half = cross_gram(
        lax.dynamic_slice_in_dim(own_flux, half_start, half_rows, 0), other_rows
    )
    mixed_half = jnp.where(is_first, mixed_half, mixed_half.T)
    own_gram = tree_sum(self_gram(own_flux), "tx") / cells_total
    own_gram, mixed_sum = lax.optimization_barrier((own_gram, mixed_half))
    hops = butterfly_steps("tx")
    own_basis = first_basis
    for sweep_index in range(ITERS):
        product = jnp.dot(own_gram, own_basis, precision=highest)
        if hops:
            received = lax.ppermute(mixed_sum, "tx", hops.pop(0))
            own_basis = orthonormal(product)
            own_basis, received = lax.optimization_barrier((own_basis, received))
            mixed_sum = mixed_sum + received
        else:
            own_basis = orthonormal(product)
    if hops:
        received = lax.ppermute(mixed_sum, "tx", hops.pop(0))
        own_modes = jnp.dot(own_flux, own_basis, precision=high)
        own_modes, received = lax.optimization_barrier((own_modes, received))
        mixed_sum = mixed_sum + received
    else:
        own_modes = jnp.dot(own_flux, own_basis, precision=high)
    for route in hops:
        mixed_sum = mixed_sum + lax.ppermute(mixed_sum, "tx", route)
    mixed_gram = mixed_sum + partner(mixed_sum, "run", 0)
    own_block = jnp.dot(own_basis.T, jnp.dot(own_gram, own_basis, precision=highest), precision=highest)
    other_block, other_basis = partner((own_block, own_basis), "run", 0)
    own_modes, mixed_gram, other_block, other_basis = lax.optimization_barrier(
        (own_modes, mixed_gram, other_block, other_basis)
    )
    other_modes = partner(own_modes, "run", 0)
    first_basis_set = jnp.where(is_first, own_basis, other_basis)
    last_basis_set = jnp.where(is_first, other_basis, own_basis)
    mixed_block = jnp.dot(
        first_basis_set.T,
        jnp.dot(mixed_gram / cells_total, last_basis_set, precision=highest),
        precision=highest,
    )
    first_block = jnp.where(is_first, own_block, other_block)
    last_block = jnp.where(is_first, other_block, own_block)
    merge_gram = jnp.concatenate(
        [
            jnp.concatenate([first_block, mixed_block], axis=1),
            jnp.concatenate([mixed_block.T, last_block], axis=1),
        ],
        axis=0,
    )
    rotation = iterate(merge_gram, merge_basis)
    rotation_share = lax.dynamic_slice_in_dim(rotation, member * share_count, share_count, 1)
    top_rows = rotation_share[:modes_count]
    bottom_rows = rotation_share[modes_count:]
    own_rotation = jnp.where(is_first, top_rows, bottom_rows)
    other_rotation = jnp.where(is_first, bottom_rows, top_rows)
    result = jnp.dot(own_modes, own_rotation, precision=high) + jnp.dot(
        other_modes, other_rotation, precision=high
    )
    return result.reshape(snapshots.shape[0], snapshots.shape[1], share_count)


def solution(mesh):
    in_specs = (P(("slab", "tx"), None, "run"), P(("slab", "tx"), None), P(), P())
    out_specs = P(("slab", "tx"), None, "run")
    return jax.shard_map(
        on_device, mesh=mesh, in_specs=in_specs, out_specs=out_specs, check_vma=False
    )
```

```python
import jax
import jax.numpy as jnp
from jax import lax
from jax.sharding import PartitionSpec as P
import functools
from jax.experimental import pallas as pl
from jax.experimental.pallas import tpu as pltpu

ITERS = 2


highest = lax.Precision.HIGHEST
high = lax.Precision.HIGH


def halos(block, axis, width):
    count = lax.axis_size(axis)
    forward = [(i, i + 1) for i in range(count - 1)]
    backward = [(target, source) for source, target in forward]
    low = lax.ppermute(lax.slice_in_dim(block, block.shape[0] - width, None, axis=0), axis, forward)
    high = lax.ppermute(lax.slice_in_dim(block, 0, width, axis=0), axis, backward)
    return low, high


def partner(block, axis, stride):
    count = lax.axis_size(axis)
    route = []
    for low in range(count):
        high = low | 1 << stride
        if high != low and high < count:
            route += [(low, high), (high, low)]
    return lax.ppermute(block, axis, route)


def tree_sum(value, axis):
    count = lax.axis_size(axis)
    if count & (count - 1):
        return lax.psum(value, axis)
    step = 1
    while step < count:
        route = [(i, i ^ step) for i in range(count)]
        value = value + lax.ppermute(value, axis, route)
        step *= 2
    return value


def butterfly_steps(axis):
    count = lax.axis_size(axis)
    assert count & (count - 1) == 0
    routes = []
    step = 1
    while step < count:
        routes.append([(i, i ^ step) for i in range(count)])
        step *= 2
    return routes


def fourth_order(values, axis_dim):
    length_kept = values.shape[axis_dim] - 4

    def shifted(offset):
        return lax.slice_in_dim(values, offset, offset + length_kept, axis=axis_dim)

    return (8.0 * (shifted(3) - shifted(1)) - (shifted(4) - shifted(0))) / 12.0


def flux_kernel(count, low_ref, high_ref, prev_ref, main_ref, next_ref, coef_ref, out_ref):
    i = pl.program_id(0)
    above = jnp.where(i == 0, low_ref[...], prev_ref[-2:])
    below = jnp.where(i == count - 1, high_ref[...], next_ref[:2])
    rows = jnp.concatenate([above, main_ref[...], below], axis=0).astype(jnp.float32)
    squared = 0.5 * jnp.square(rows)
    along_rows = fourth_order(squared, 0)
    mid = squared[2:-2]
    cols = mid.shape[1]
    ids = lax.broadcasted_iota(jnp.int32, mid.shape, 1)

    def shift(offset):
        moved = pltpu.roll(mid, (-offset) % cols, 1)
        inside = (ids + offset >= 0) & (ids + offset < cols)
        return jnp.where(inside, moved, 0.0)

    along_cols = (8.0 * (shift(1) - shift(-1)) - (shift(2) - shift(-2))) / 12.0
    central = rows[2:-2]
    out_ref[...] = central - coef_ref[...][:, :, None] * (along_rows + along_cols)


def fluxes(low, block, high, coefficient):
    nx, ny, ns = block.shape
    bx = 8 if nx % 8 == 0 else nx
    count = nx // bx

    def spec(index):
        return pl.BlockSpec((bx, ny, ns), index)

    return pl.pallas_call(
        functools.partial(flux_kernel, count),
        grid=(count,),
        in_specs=[
            pl.BlockSpec(low.shape, lambda i: (0, 0, 0)),
            pl.BlockSpec(high.shape, lambda i: (0, 0, 0)),
            spec(lambda i: (jnp.maximum(i - 1, 0), 0, 0)),
            spec(lambda i: (i, 0, 0)),
            spec(lambda i: (jnp.minimum(i + 1, count - 1), 0, 0)),
            pl.BlockSpec((bx, ny), lambda i: (i, 0)),
        ],
        out_specs=spec(lambda i: (i, 0, 0)),
        out_shape=jax.ShapeDtypeStruct((nx, ny, ns), jnp.float32),
    )(low, high, block, block, block, coefficient)


def gram_schmidt_kernel(rows_ref, out_ref, work):
    count, width = rows_ref.shape
    blocks = count // 8
    group = 4 if blocks % 4 == 0 else 1
    work[...] = rows_ref[...]
    for first in range(0, blocks, group):

        def sweep(block, carry, first=first):
            base = pl.multiple_of(block * 8, 8)
            pivot_rows = work[pl.ds(base, 8), :]
            for lane_row in range(8):
                j = base + lane_row
                vector = pivot_rows[lane_row:lane_row + 1, :]
                inverse = 1.0 / jnp.sum(vector * vector, axis=1, keepdims=True)
                weight = jnp.sum(pivot_rows * vector, axis=1, keepdims=True) * inverse
                ids = lax.broadcasted_iota(jnp.int32, weight.shape, 0)
                weight = jnp.where(ids > lane_row, weight, 0.0)
                pivot_rows = pivot_rows - weight * vector
                for i in range(first, blocks):
                    rows = work[i * 8:(i + 1) * 8, :]
                    weight = jnp.sum(rows * vector, axis=1, keepdims=True) * inverse
                    ids = lax.broadcasted_iota(jnp.int32, weight.shape, 0) + i * 8
                    weight = jnp.where(ids > j, weight, 0.0)
                    work[i * 8:(i + 1) * 8, :] = rows - weight * vector
            work[pl.ds(base, 8), :] = pivot_rows
            return carry

        lax.fori_loop(first, first + group, sweep, 0)
    for i in range(blocks):
        rows = work[i * 8:(i + 1) * 8, :]
        norm = jnp.sqrt(jnp.sum(rows * rows, axis=1, keepdims=True))
        out_ref[i * 8:(i + 1) * 8, :] = rows / norm


def orthonormal(matrix):
    rows = matrix.T
    done = pl.pallas_call(
        gram_schmidt_kernel,
        out_shape=jax.ShapeDtypeStruct(rows.shape, jnp.float32),
        scratch_shapes=[pltpu.VMEM(rows.shape, jnp.float32)],
    )(rows)
    return done.T


def iterate(gram_matrix, basis_set):
    for sweep_index in range(ITERS):
        basis_set = orthonormal(jnp.dot(gram_matrix, basis_set, precision=highest))
    return basis_set


def cross_gram(left_rows, right_rows):
    return lax.dot_general(left_rows, right_rows, (((0,), (0,)), ((), ())), precision=high)


def self_gram(rows):
    upper = lax.reduce_precision(rows, exponent_bits=8, mantissa_bits=7)
    lower = lax.reduce_precision(rows - upper, exponent_bits=8, mantissa_bits=7)
    missing = jnp.sum(lower * lower, axis=0)
    return cross_gram(rows, rows) + jnp.diag(missing)


def on_device(snapshots, coefficient, start_first, start_merge):
    halo_low, halo_high = halos(snapshots, "tx", 2)
    rows_here = snapshots.shape[0] * snapshots.shape[1]
    order_size = snapshots.shape[2]
    modes_count = start_first.shape[1]
    share_count = modes_count // lax.axis_size("run")
    cells_total = rows_here * lax.axis_size("tx")
    member = lax.axis_index("run")
    is_first = member == 0
    own_start = lax.dynamic_slice_in_dim(start_first, member * order_size, order_size, 0)
    own_start = own_start.astype(jnp.float32)
    merge_start = start_merge.astype(jnp.float32)
    if lax.axis_size("tx") % 2:
        first_basis = orthonormal(own_start)
        merge_basis = orthonormal(merge_start)
    else:
        is_even = lax.axis_index("tx") % 2 == 0
        mine = orthonormal(jnp.where(is_even, own_start, merge_start))
        theirs = partner(mine, "tx", 0)
        first_basis = jnp.where(is_even, mine, theirs)
        merge_basis = jnp.where(is_even, theirs, mine)
    own_flux = fluxes(halo_low, snapshots, halo_high, coefficient).reshape(rows_here, order_size)
    half_rows = rows_here // 2
    half_start = member * half_rows
    sent_rows = lax.dynamic_slice_in_dim(own_flux, (1 - member) * half_rows, half_rows, 0)
    other_rows = partner(sent_rows, "run", 0)
    mixed_half = cross_gram(
        lax.dynamic_slice_in_dim(own_flux, half_start, half_rows, 0), other_rows
    )
    mixed_half = jnp.where(is_first, mixed_half, mixed_half.T)
    partial_gram = self_gram(own_flux)
    split = order_size // 2
    packed = jnp.concatenate([partial_gram[:split], partial_gram[split:, split:]], axis=1)
    packed = tree_sum(packed, "tx") / cells_total
    upper = packed[:, split:order_size]
    own_gram = jnp.concatenate(
        [
            jnp.concatenate([packed[:, :split], upper], axis=1),
            jnp.concatenate([upper.T, packed[:, order_size:]], axis=1),
        ],
        axis=0,
    )
    own_gram, mixed_sum = lax.optimization_barrier((own_gram, mixed_half))
    hops = butterfly_steps("tx")
    own_basis = first_basis
    for sweep_index in range(ITERS):
        product = jnp.dot(own_gram, own_basis, precision=highest)
        if hops:
            received = lax.ppermute(mixed_sum, "tx", hops.pop(0))
            own_basis = orthonormal(product)
            own_basis, received = lax.optimization_barrier((own_basis, received))
            mixed_sum = mixed_sum + received
        else:
            own_basis = orthonormal(product)
    if hops:
        received = lax.ppermute(mixed_sum, "tx", hops.pop(0))
        own_modes = jnp.dot(own_flux, own_basis, precision=high)
        own_modes, received = lax.optimization_barrier((own_modes, received))
        mixed_sum = mixed_sum + received
    else:
        own_modes = jnp.dot(own_flux, own_basis, precision=high)
    for route in hops:
        mixed_sum = mixed_sum + lax.ppermute(mixed_sum, "tx", route)
    mixed_gram = mixed_sum + partner(mixed_sum, "run", 0)
    own_block = jnp.dot(own_basis.T, jnp.dot(own_gram, own_basis, precision=highest), precision=highest)
    other_block, other_basis = partner((own_block, own_basis), "run", 0)
    own_modes, mixed_gram, other_block, other_basis = lax.optimization_barrier(
        (own_modes, mixed_gram, other_block, other_basis)
    )
    other_modes = partner(own_modes, "run", 0)
    first_basis_set = jnp.where(is_first, own_basis, other_basis)
    last_basis_set = jnp.where(is_first, other_basis, own_basis)
    mixed_block = jnp.dot(
        first_basis_set.T,
        jnp.dot(mixed_gram / cells_total, last_basis_set, precision=highest),
        precision=highest,
    )
    first_block = jnp.where(is_first, own_block, other_block)
    last_block = jnp.where(is_first, other_block, own_block)
    merge_gram = jnp.concatenate(
        [
            jnp.concatenate([first_block, mixed_block], axis=1),
            jnp.concatenate([mixed_block.T, last_block], axis=1),
        ],
        axis=0,
    )
    rotation = iterate(merge_gram, merge_basis)
    rotation_share = lax.dynamic_slice_in_dim(rotation, member * share_count, share_count, 1)
    top_rows = rotation_share[:modes_count]
    bottom_rows = rotation_share[modes_count:]
    own_rotation = jnp.where(is_first, top_rows, bottom_rows)
    other_rotation = jnp.where(is_first, bottom_rows, top_rows)
    result = jnp.dot(own_modes, own_rotation, precision=high) + jnp.dot(
        other_modes, other_rotation, precision=high
    )
    return result.reshape(snapshots.shape[0], snapshots.shape[1], share_count)


def solution(mesh):
    in_specs = (P(("slab", "tx"), None, "run"), P(("slab", "tx"), None), P(), P())
    out_specs = P(("slab", "tx"), None, "run")
    return jax.shard_map(
        on_device, mesh=mesh, in_specs=in_specs, out_specs=out_specs, check_vma=False
    )
```

```python
import jax
import jax.numpy as jnp
from jax import lax
from jax.sharding import PartitionSpec as P
import functools
from jax.experimental import pallas as pl
from jax.experimental.pallas import tpu as pltpu

ITERS = 2


highest = lax.Precision.HIGHEST
high = lax.Precision.HIGH


def halos(block, axis, width):
    count = lax.axis_size(axis)
    forward = [(i, i + 1) for i in range(count - 1)]
    backward = [(target, source) for source, target in forward]
    low = lax.ppermute(lax.slice_in_dim(block, block.shape[0] - width, None, axis=0), axis, forward)
    high = lax.ppermute(lax.slice_in_dim(block, 0, width, axis=0), axis, backward)
    return low, high


def partner(block, axis, stride):
    count = lax.axis_size(axis)
    route = []
    for low in range(count):
        high = low | 1 << stride
        if high != low and high < count:
            route += [(low, high), (high, low)]
    return lax.ppermute(block, axis, route)


def tree_sum(value, axis):
    count = lax.axis_size(axis)
    if count & (count - 1):
        return lax.psum(value, axis)
    step = 1
    while step < count:
        route = [(i, i ^ step) for i in range(count)]
        value = value + lax.ppermute(value, axis, route)
        step *= 2
    return value


def butterfly_steps(axis):
    count = lax.axis_size(axis)
    assert count & (count - 1) == 0
    routes = []
    step = 1
    while step < count:
        routes.append([(i, i ^ step) for i in range(count)])
        step *= 2
    return routes


def fourth_order(values, axis_dim):
    length_kept = values.shape[axis_dim] - 4

    def shifted(offset):
        return lax.slice_in_dim(values, offset, offset + length_kept, axis=axis_dim)

    return (8.0 * (shifted(3) - shifted(1)) - (shifted(4) - shifted(0))) / 12.0


def flux_kernel(count, member_ref, low_ref, high_ref, prev_ref, main_ref, next_ref, coef_ref, out_ref, sent_ref):
    i = pl.program_id(0)
    above = jnp.where(i == 0, low_ref[...], prev_ref[-2:])
    below = jnp.where(i == count - 1, high_ref[...], next_ref[:2])
    rows = jnp.concatenate([above, main_ref[...], below], axis=0).astype(jnp.float32)
    squared = 0.5 * jnp.square(rows)
    along_rows = fourth_order(squared, 0)
    mid = squared[2:-2]
    cols = mid.shape[1]
    ids = lax.broadcasted_iota(jnp.int32, mid.shape, 1)

    def shift(offset):
        moved = pltpu.roll(mid, (-offset) % cols, 1)
        inside = (ids + offset >= 0) & (ids + offset < cols)
        return jnp.where(inside, moved, 0.0)

    along_cols = (8.0 * (shift(1) - shift(-1)) - (shift(2) - shift(-2))) / 12.0
    central = rows[2:-2]
    result = central - coef_ref[...][:, :, None] * (along_rows + along_cols)
    out_ref[...] = result
    first_sent = (1 - member_ref[0]) * (count // 2)

    @pl.when((i >= first_sent) & (i < first_sent + count // 2))
    def _():
        sent_ref[...] = result


def fluxes(low, block, high, coefficient, member):
    nx, ny, ns = block.shape
    bx = 8 if nx % 16 == 0 else nx // 2
    count = nx // bx
    half = count // 2

    def spec(index):
        return pl.BlockSpec((bx, ny, ns), index)

    def sent_index(i, member_ref):
        return (jnp.clip(i - (1 - member_ref[0]) * half, 0, half - 1), 0, 0)

    grid_spec = pltpu.PrefetchScalarGridSpec(
        num_scalar_prefetch=1,
        grid=(count,),
        in_specs=[
            pl.BlockSpec(low.shape, lambda i, m: (0, 0, 0)),
            pl.BlockSpec(high.shape, lambda i, m: (0, 0, 0)),
            spec(lambda i, m: (jnp.maximum(i - 1, 0), 0, 0)),
            spec(lambda i, m: (i, 0, 0)),
            spec(lambda i, m: (jnp.minimum(i + 1, count - 1), 0, 0)),
            pl.BlockSpec((bx, ny), lambda i, m: (i, 0)),
        ],
        out_specs=[spec(lambda i, m: (i, 0, 0)), spec(sent_index)],
    )
    return pl.pallas_call(
        functools.partial(flux_kernel, count),
        grid_spec=grid_spec,
        out_shape=[
            jax.ShapeDtypeStruct((nx, ny, ns), jnp.float32),
            jax.ShapeDtypeStruct((nx // 2, ny, ns), jnp.float32),
        ],
    )(jnp.reshape(member, (1,)).astype(jnp.int32), low, high, block, block, block, coefficient)


def gram_schmidt_kernel(rows_ref, out_ref, work):
    count, width = rows_ref.shape
    blocks = count // 8
    group = 4 if blocks % 4 == 0 else 1
    work[...] = rows_ref[...]
    for first in range(0, blocks, group):

        def sweep(block, carry, first=first):
            base = pl.multiple_of(block * 8, 8)
            pivot_rows = work[pl.ds(base, 8), :]
            for lane_row in range(8):
                j = base + lane_row
                vector = pivot_rows[lane_row:lane_row + 1, :]
                inverse = 1.0 / jnp.sum(vector * vector, axis=1, keepdims=True)
                weight = jnp.sum(pivot_rows * vector, axis=1, keepdims=True) * inverse
                ids = lax.broadcasted_iota(jnp.int32, weight.shape, 0)
                weight = jnp.where(ids > lane_row, weight, 0.0)
                pivot_rows = pivot_rows - weight * vector
                for i in range(first, blocks):
                    rows = work[i * 8:(i + 1) * 8, :]
                    weight = jnp.sum(rows * vector, axis=1, keepdims=True) * inverse
                    ids = lax.broadcasted_iota(jnp.int32, weight.shape, 0) + i * 8
                    weight = jnp.where(ids > j, weight, 0.0)
                    work[i * 8:(i + 1) * 8, :] = rows - weight * vector
            work[pl.ds(base, 8), :] = pivot_rows
            return carry

        lax.fori_loop(first, first + group, sweep, 0)
    for i in range(blocks):
        rows = work[i * 8:(i + 1) * 8, :]
        norm = jnp.sqrt(jnp.sum(rows * rows, axis=1, keepdims=True))
        out_ref[i * 8:(i + 1) * 8, :] = rows / norm


def orthonormal(matrix):
    rows = matrix.T
    done = pl.pallas_call(
        gram_schmidt_kernel,
        out_shape=jax.ShapeDtypeStruct(rows.shape, jnp.float32),
        scratch_shapes=[pltpu.VMEM(rows.shape, jnp.float32)],
    )(rows)
    return done.T


def iterate(gram_matrix, basis_set):
    for sweep_index in range(ITERS):
        basis_set = orthonormal(jnp.dot(gram_matrix, basis_set, precision=highest))
    return basis_set


def cross_gram(left_rows, right_rows):
    return lax.dot_general(left_rows, right_rows, (((0,), (0,)), ((), ())), precision=high)


def self_gram(rows):
    upper = lax.reduce_precision(rows, exponent_bits=8, mantissa_bits=7)
    lower = lax.reduce_precision(rows - upper, exponent_bits=8, mantissa_bits=7)
    missing = jnp.sum(lower * lower, axis=0)
    return cross_gram(rows, rows) + jnp.diag(missing)


def on_device(snapshots, coefficient, start_first, start_merge):
    halo_low, halo_high = halos(snapshots, "tx", 2)
    rows_here = snapshots.shape[0] * snapshots.shape[1]
    order_size = snapshots.shape[2]
    modes_count = start_first.shape[1]
    share_count = modes_count // lax.axis_size("run")
    cells_total = rows_here * lax.axis_size("tx")
    member = lax.axis_index("run")
    is_first = member == 0
    own_start = lax.dynamic_slice_in_dim(start_first, member * order_size, order_size, 0)
    own_start = own_start.astype(jnp.float32)
    merge_start = start_merge.astype(jnp.float32)
    if lax.axis_size("tx") % 2:
        first_basis = orthonormal(own_start)
        merge_basis = orthonormal(merge_start)
    else:
        is_even = lax.axis_index("tx") % 2 == 0
        mine = orthonormal(jnp.where(is_even, own_start, merge_start))
        theirs = partner(mine, "tx", 0)
        first_basis = jnp.where(is_even, mine, theirs)
        merge_basis = jnp.where(is_even, theirs, mine)
    own_flux, sent_rows = fluxes(halo_low, snapshots, halo_high, coefficient, member)
    own_flux = own_flux.reshape(rows_here, order_size)
    half_rows = rows_here // 2
    half_start = member * half_rows
    other_rows = partner(sent_rows.reshape(half_rows, order_size), "run", 0)
    mixed_half = cross_gram(
        lax.dynamic_slice_in_dim(own_flux, half_start, half_rows, 0), other_rows
    )
    mixed_half = jnp.where(is_first, mixed_half, mixed_half.T)
    partial_gram = self_gram(own_flux)
    split = order_size // 2
    packed = jnp.concatenate([partial_gram[:split], partial_gram[split:, split:]], axis=1)
    packed = tree_sum(packed, "tx") / cells_total
    upper = packed[:, split:order_size]
    own_gram = jnp.concatenate(
        [
            jnp.concatenate([packed[:, :split], upper], axis=1),
            jnp.concatenate([upper.T, packed[:, order_size:]], axis=1),
        ],
        axis=0,
    )
    own_gram, mixed_sum = lax.optimization_barrier((own_gram, mixed_half))
    hops = butterfly_steps("tx")
    own_basis = first_basis
    for sweep_index in range(ITERS):
        product = jnp.dot(own_gram, own_basis, precision=highest)
        if hops:
            received = lax.ppermute(mixed_sum, "tx", hops.pop(0))
            own_basis = orthonormal(product)
            own_basis, received = lax.optimization_barrier((own_basis, received))
            mixed_sum = mixed_sum + received
        else:
            own_basis = orthonormal(product)
    if hops:
        received = lax.ppermute(mixed_sum, "tx", hops.pop(0))
        own_modes = jnp.dot(own_flux, own_basis, precision=high)
        own_modes, received = lax.optimization_barrier((own_modes, received))
        mixed_sum = mixed_sum + received
    else:
        own_modes = jnp.dot(own_flux, own_basis, precision=high)
    for route in hops:
        mixed_sum = mixed_sum + lax.ppermute(mixed_sum, "tx", route)
    mixed_gram = mixed_sum + partner(mixed_sum, "run", 0)
    own_block = jnp.dot(own_basis.T, jnp.dot(own_gram, own_basis, precision=highest), precision=highest)
    other_block, other_basis = partner((own_block, own_basis), "run", 0)
    own_modes, mixed_gram, other_block, other_basis = lax.optimization_barrier(
        (own_modes, mixed_gram, other_block, other_basis)
    )
    other_modes = partner(own_modes, "run", 0)
    first_basis_set = jnp.where(is_first, own_basis, other_basis)
    last_basis_set = jnp.where(is_first, other_basis, own_basis)
    mixed_block = jnp.dot(
        first_basis_set.T,
        jnp.dot(mixed_gram / cells_total, last_basis_set, precision=highest),
        precision=highest,
    )
    first_block = jnp.where(is_first, own_block, other_block)
    last_block = jnp.where(is_first, other_block, own_block)
    merge_gram = jnp.concatenate(
        [
            jnp.concatenate([first_block, mixed_block], axis=1),
            jnp.concatenate([mixed_block.T, last_block], axis=1),
        ],
        axis=0,
    )
    rotation = iterate(merge_gram, merge_basis)
    rotation_share = lax.dynamic_slice_in_dim(rotation, member * share_count, share_count, 1)
    top_rows = rotation_share[:modes_count]
    bottom_rows = rotation_share[modes_count:]
    own_rotation = jnp.where(is_first, top_rows, bottom_rows)
    other_rotation = jnp.where(is_first, bottom_rows, top_rows)
    result = jnp.dot(own_modes, own_rotation, precision=high) + jnp.dot(
        other_modes, other_rotation, precision=high
    )
    return result.reshape(snapshots.shape[0], snapshots.shape[1], share_count)


def solution(mesh):
    in_specs = (P(("slab", "tx"), None, "run"), P(("slab", "tx"), None), P(), P())
    out_specs = P(("slab", "tx"), None, "run")
    return jax.shard_map(
        on_device, mesh=mesh, in_specs=in_specs, out_specs=out_specs, check_vma=False
    )
```

```python
import jax
import jax.numpy as jnp
from jax import lax
from jax.sharding import PartitionSpec as P
import functools
from jax.experimental import pallas as pl
from jax.experimental.pallas import tpu as pltpu

ITERS = 2


highest = lax.Precision.HIGHEST
high = lax.Precision.HIGH


def halos(block, axis, width):
    count = lax.axis_size(axis)
    forward = [(i, i + 1) for i in range(count - 1)]
    backward = [(target, source) for source, target in forward]
    low = lax.ppermute(lax.slice_in_dim(block, block.shape[0] - width, None, axis=0), axis, forward)
    high = lax.ppermute(lax.slice_in_dim(block, 0, width, axis=0), axis, backward)
    return low, high


def partner(block, axis, stride):
    count = lax.axis_size(axis)
    route = []
    for low in range(count):
        high = low | 1 << stride
        if high != low and high < count:
            route += [(low, high), (high, low)]
    return lax.ppermute(block, axis, route)


def tree_sum(value, axis):
    count = lax.axis_size(axis)
    if count & (count - 1):
        return lax.psum(value, axis)
    step = 1
    while step < count:
        route = [(i, i ^ step) for i in range(count)]
        value = value + lax.ppermute(value, axis, route)
        step *= 2
    return value


def butterfly_steps(axis):
    count = lax.axis_size(axis)
    assert count & (count - 1) == 0
    routes = []
    step = 1
    while step < count:
        routes.append([(i, i ^ step) for i in range(count)])
        step *= 2
    return routes


def fourth_order(values, axis_dim):
    length_kept = values.shape[axis_dim] - 4

    def shifted(offset):
        return lax.slice_in_dim(values, offset, offset + length_kept, axis=axis_dim)

    return (8.0 * (shifted(3) - shifted(1)) - (shifted(4) - shifted(0))) / 12.0


def flux_kernel(count, low_ref, high_ref, prev_ref, main_ref, next_ref, coef_ref, out_ref):
    i = pl.program_id(0)
    above = jnp.where(i == 0, low_ref[...], prev_ref[-2:])
    below = jnp.where(i == count - 1, high_ref[...], next_ref[:2])
    rows = jnp.concatenate([above, main_ref[...], below], axis=0).astype(jnp.float32)
    squared = 0.5 * jnp.square(rows)
    along_rows = fourth_order(squared, 0)
    mid = squared[2:-2]
    cols = mid.shape[1]
    ids = lax.broadcasted_iota(jnp.int32, mid.shape, 1)

    def shift(offset):
        moved = pltpu.roll(mid, (-offset) % cols, 1)
        inside = (ids + offset >= 0) & (ids + offset < cols)
        return jnp.where(inside, moved, 0.0)

    along_cols = (8.0 * (shift(1) - shift(-1)) - (shift(2) - shift(-2))) / 12.0
    central = rows[2:-2]
    out_ref[...] = central - coef_ref[...][:, :, None] * (along_rows + along_cols)


def fluxes(low, block, high, coefficient):
    nx, ny, ns = block.shape
    bx = 8 if nx % 8 == 0 else nx
    count = nx // bx

    def spec(index):
        return pl.BlockSpec((bx, ny, ns), index)

    return pl.pallas_call(
        functools.partial(flux_kernel, count),
        grid=(count,),
        in_specs=[
            pl.BlockSpec(low.shape, lambda i: (0, 0, 0)),
            pl.BlockSpec(high.shape, lambda i: (0, 0, 0)),
            spec(lambda i: (jnp.maximum(i - 1, 0), 0, 0)),
            spec(lambda i: (i, 0, 0)),
            spec(lambda i: (jnp.minimum(i + 1, count - 1), 0, 0)),
            pl.BlockSpec((bx, ny), lambda i: (i, 0)),
        ],
        out_specs=spec(lambda i: (i, 0, 0)),
        out_shape=jax.ShapeDtypeStruct((nx, ny, ns), jnp.float32),
    )(low, high, block, block, block, coefficient)


def gram_schmidt_kernel(rows_ref, out_ref, work):
    count, width = rows_ref.shape
    blocks = count // 8
    group = 4 if blocks % 4 == 0 else 1
    work[...] = rows_ref[...]
    for first in range(0, blocks, group):

        def sweep(block, carry, first=first):
            base = pl.multiple_of(block * 8, 8)
            pivot_rows = work[pl.ds(base, 8), :]
            for lane_row in range(8):
                j = base + lane_row
                vector = pivot_rows[lane_row:lane_row + 1, :]
                inverse = 1.0 / jnp.sum(vector * vector, axis=1, keepdims=True)
                weight = jnp.sum(pivot_rows * vector, axis=1, keepdims=True) * inverse
                ids = lax.broadcasted_iota(jnp.int32, weight.shape, 0)
                weight = jnp.where(ids > lane_row, weight, 0.0)
                pivot_rows = pivot_rows - weight * vector
                for i in range(first, blocks):
                    rows = work[i * 8:(i + 1) * 8, :]
                    weight = jnp.sum(rows * vector, axis=1, keepdims=True) * inverse
                    ids = lax.broadcasted_iota(jnp.int32, weight.shape, 0) + i * 8
                    weight = jnp.where(ids > j, weight, 0.0)
                    work[i * 8:(i + 1) * 8, :] = rows - weight * vector
            work[pl.ds(base, 8), :] = pivot_rows
            return carry

        lax.fori_loop(first, first + group, sweep, 0)
    for i in range(blocks):
        rows = work[i * 8:(i + 1) * 8, :]
        norm = jnp.sqrt(jnp.sum(rows * rows, axis=1, keepdims=True))
        out_ref[i * 8:(i + 1) * 8, :] = rows / norm


def orthonormal(matrix):
    rows = matrix.T
    done = pl.pallas_call(
        gram_schmidt_kernel,
        out_shape=jax.ShapeDtypeStruct(rows.shape, jnp.float32),
        scratch_shapes=[pltpu.VMEM(rows.shape, jnp.float32)],
    )(rows)
    return done.T


def iterate(gram_matrix, basis_set):
    for sweep_index in range(ITERS):
        basis_set = orthonormal(jnp.dot(gram_matrix, basis_set, precision=highest))
    return basis_set


def cross_gram(left_rows, right_rows):
    return lax.dot_general(left_rows, right_rows, (((0,), (0,)), ((), ())), precision=high)


def self_gram(rows):
    upper = lax.reduce_precision(rows, exponent_bits=8, mantissa_bits=7)
    lower = lax.reduce_precision(rows - upper, exponent_bits=8, mantissa_bits=7)
    missing = jnp.sum(lower * lower, axis=0)
    return cross_gram(rows, rows) + jnp.diag(missing)


def on_device(snapshots, coefficient, start_first, start_merge):
    halo_low, halo_high = halos(snapshots, "tx", 2)
    rows_here = snapshots.shape[0] * snapshots.shape[1]
    order_size = snapshots.shape[2]
    modes_count = start_first.shape[1]
    share_count = modes_count // lax.axis_size("run")
    cells_total = rows_here * lax.axis_size("tx")
    member = lax.axis_index("run")
    is_first = member == 0
    own_start = lax.dynamic_slice_in_dim(start_first, member * order_size, order_size, 0)
    own_start = own_start.astype(jnp.float32)
    merge_start = start_merge.astype(jnp.float32)
    if lax.axis_size("tx") % 2:
        first_basis = orthonormal(own_start)
        merge_basis = orthonormal(merge_start)
    else:
        is_even = lax.axis_index("tx") % 2 == 0
        mine = orthonormal(jnp.where(is_even, own_start, merge_start))
        mine, snapshots = lax.optimization_barrier((mine, snapshots))
        theirs = partner(mine, "tx", 0)
        first_basis = jnp.where(is_even, mine, theirs)
        merge_basis = jnp.where(is_even, theirs, mine)
    own_flux = fluxes(halo_low, snapshots, halo_high, coefficient).reshape(rows_here, order_size)
    half_rows = rows_here // 2
    half_start = member * half_rows
    sent_rows = lax.dynamic_slice_in_dim(own_flux, (1 - member) * half_rows, half_rows, 0)
    other_rows = partner(sent_rows, "run", 0)
    mixed_half = cross_gram(
        lax.dynamic_slice_in_dim(own_flux, half_start, half_rows, 0), other_rows
    )
    mixed_half = jnp.where(is_first, mixed_half, mixed_half.T)
    partial_gram = self_gram(own_flux)
    split = order_size // 2
    packed = jnp.concatenate([partial_gram[:split], partial_gram[split:, split:]], axis=1)
    packed = tree_sum(packed, "tx") / cells_total
    upper = packed[:, split:order_size]
    own_gram = jnp.concatenate(
        [
            jnp.concatenate([packed[:, :split], upper], axis=1),
            jnp.concatenate([upper.T, packed[:, order_size:]], axis=1),
        ],
        axis=0,
    )
    own_gram, mixed_sum = lax.optimization_barrier((own_gram, mixed_half))
    hops = butterfly_steps("tx")
    own_basis = first_basis
    for sweep_index in range(ITERS):
        product = jnp.dot(own_gram, own_basis, precision=highest)
        if hops:
            received = lax.ppermute(mixed_sum, "tx", hops.pop(0))
            own_basis = orthonormal(product)
            own_basis, received = lax.optimization_barrier((own_basis, received))
            mixed_sum = mixed_sum + received
        else:
            own_basis = orthonormal(product)
    if hops:
        received = lax.ppermute(mixed_sum, "tx", hops.pop(0))
        own_modes = jnp.dot(own_flux, own_basis, precision=high)
        own_modes, received = lax.optimization_barrier((own_modes, received))
        mixed_sum = mixed_sum + received
    else:
        own_modes = jnp.dot(own_flux, own_basis, precision=high)
    for route in hops:
        mixed_sum = mixed_sum + lax.ppermute(mixed_sum, "tx", route)
    mixed_gram = mixed_sum + partner(mixed_sum, "run", 0)
    own_block = jnp.dot(own_basis.T, jnp.dot(own_gram, own_basis, precision=highest), precision=highest)
    other_block, other_basis = partner((own_block, own_basis), "run", 0)
    own_modes, mixed_gram, other_block, other_basis = lax.optimization_barrier(
        (own_modes, mixed_gram, other_block, other_basis)
    )
    other_modes = partner(own_modes, "run", 0)
    first_basis_set = jnp.where(is_first, own_basis, other_basis)
    last_basis_set = jnp.where(is_first, other_basis, own_basis)
    mixed_block = jnp.dot(
        first_basis_set.T,
        jnp.dot(mixed_gram / cells_total, last_basis_set, precision=highest),
        precision=highest,
    )
    first_block = jnp.where(is_first, own_block, other_block)
    last_block = jnp.where(is_first, other_block, own_block)
    merge_gram = jnp.concatenate(
        [
            jnp.concatenate([first_block, mixed_block], axis=1),
            jnp.concatenate([mixed_block.T, last_block], axis=1),
        ],
        axis=0,
    )
    rotation = iterate(merge_gram, merge_basis)
    rotation_share = lax.dynamic_slice_in_dim(rotation, member * share_count, share_count, 1)
    top_rows = rotation_share[:modes_count]
    bottom_rows = rotation_share[modes_count:]
    own_rotation = jnp.where(is_first, top_rows, bottom_rows)
    other_rotation = jnp.where(is_first, bottom_rows, top_rows)
    result = jnp.dot(own_modes, own_rotation, precision=high) + jnp.dot(
        other_modes, other_rotation, precision=high
    )
    return result.reshape(snapshots.shape[0], snapshots.shape[1], share_count)


def solution(mesh):
    in_specs = (P(("slab", "tx"), None, "run"), P(("slab", "tx"), None), P(), P())
    out_specs = P(("slab", "tx"), None, "run")
    return jax.shard_map(
        on_device, mesh=mesh, in_specs=in_specs, out_specs=out_specs, check_vma=False
    )
```

```python
import jax
import jax.numpy as jnp
from jax import lax
from jax.sharding import PartitionSpec as P
import functools
from jax.experimental import pallas as pl
from jax.experimental.pallas import tpu as pltpu

ITERS = 2


highest = lax.Precision.HIGHEST
high = lax.Precision.HIGH


def halos(block, axis, width):
    count = lax.axis_size(axis)
    forward = [(i, i + 1) for i in range(count - 1)]
    backward = [(target, source) for source, target in forward]
    low = lax.ppermute(lax.slice_in_dim(block, block.shape[0] - width, None, axis=0), axis, forward)
    high = lax.ppermute(lax.slice_in_dim(block, 0, width, axis=0), axis, backward)
    return low, high


def partner(block, axis, stride):
    count = lax.axis_size(axis)
    route = []
    for low in range(count):
        high = low | 1 << stride
        if high != low and high < count:
            route += [(low, high), (high, low)]
    return lax.ppermute(block, axis, route)


def tree_sum(value, axis):
    count = lax.axis_size(axis)
    if count & (count - 1):
        return lax.psum(value, axis)
    step = 1
    while step < count:
        route = [(i, i ^ step) for i in range(count)]
        value = value + lax.ppermute(value, axis, route)
        step *= 2
    return value


def butterfly_steps(axis):
    count = lax.axis_size(axis)
    assert count & (count - 1) == 0
    routes = []
    step = 1
    while step < count:
        routes.append([(i, i ^ step) for i in range(count)])
        step *= 2
    return routes


def fourth_order(values, axis_dim):
    length_kept = values.shape[axis_dim] - 4

    def shifted(offset):
        return lax.slice_in_dim(values, offset, offset + length_kept, axis=axis_dim)

    return (8.0 * (shifted(3) - shifted(1)) - (shifted(4) - shifted(0))) / 12.0


def flux_kernel(count, low_ref, high_ref, prev_ref, main_ref, next_ref, coef_ref, out_ref):
    i = pl.program_id(0)
    above = jnp.where(i == 0, low_ref[...], prev_ref[-2:])
    below = jnp.where(i == count - 1, high_ref[...], next_ref[:2])
    rows = jnp.concatenate([above, main_ref[...], below], axis=0).astype(jnp.float32)
    squared = 0.5 * jnp.square(rows)
    along_rows = fourth_order(squared, 0)
    mid = squared[2:-2]
    cols = mid.shape[1]
    ids = lax.broadcasted_iota(jnp.int32, mid.shape, 1)

    def shift(offset):
        moved = pltpu.roll(mid, (-offset) % cols, 1)
        inside = (ids + offset >= 0) & (ids + offset < cols)
        return jnp.where(inside, moved, 0.0)

    along_cols = (8.0 * (shift(1) - shift(-1)) - (shift(2) - shift(-2))) / 12.0
    central = rows[2:-2]
    out_ref[...] = central - coef_ref[...][:, :, None] * (along_rows + along_cols)


def fluxes(low, block, high, coefficient):
    nx, ny, ns = block.shape
    bx = 8 if nx % 8 == 0 else nx
    count = nx // bx

    def spec(index):
        return pl.BlockSpec((bx, ny, ns), index)

    return pl.pallas_call(
        functools.partial(flux_kernel, count),
        grid=(count,),
        in_specs=[
            pl.BlockSpec(low.shape, lambda i: (0, 0, 0)),
            pl.BlockSpec(high.shape, lambda i: (0, 0, 0)),
            spec(lambda i: (jnp.maximum(i - 1, 0), 0, 0)),
            spec(lambda i: (i, 0, 0)),
            spec(lambda i: (jnp.minimum(i + 1, count - 1), 0, 0)),
            pl.BlockSpec((bx, ny), lambda i: (i, 0)),
        ],
        out_specs=spec(lambda i: (i, 0, 0)),
        out_shape=jax.ShapeDtypeStruct((nx, ny, ns), jnp.float32),
    )(low, high, block, block, block, coefficient)


def gram_schmidt_kernel(rows_ref, out_ref, work):
    count, width = rows_ref.shape
    blocks = count // 8
    group = 4 if blocks % 4 == 0 else 1
    work[...] = rows_ref[...]
    for first in range(0, blocks, group):

        def sweep(block, carry, first=first):
            base = pl.multiple_of(block * 8, 8)
            pivot_rows = work[pl.ds(base, 8), :]
            for lane_row in range(8):
                j = base + lane_row
                vector = pivot_rows[lane_row:lane_row + 1, :]
                inverse = 1.0 / jnp.sum(vector * vector, axis=1, keepdims=True)
                weight = jnp.sum(pivot_rows * vector, axis=1, keepdims=True) * inverse
                ids = lax.broadcasted_iota(jnp.int32, weight.shape, 0)
                weight = jnp.where(ids > lane_row, weight, 0.0)
                pivot_rows = pivot_rows - weight * vector
                for i in range(first, blocks):
                    rows = work[i * 8:(i + 1) * 8, :]
                    weight = jnp.sum(rows * vector, axis=1, keepdims=True) * inverse
                    ids = lax.broadcasted_iota(jnp.int32, weight.shape, 0) + i * 8
                    weight = jnp.where(ids > j, weight, 0.0)
                    work[i * 8:(i + 1) * 8, :] = rows - weight * vector
            work[pl.ds(base, 8), :] = pivot_rows
            return carry

        lax.fori_loop(first, first + group, sweep, 0)
    for i in range(blocks):
        rows = work[i * 8:(i + 1) * 8, :]
        norm = jnp.sqrt(jnp.sum(rows * rows, axis=1, keepdims=True))
        out_ref[i * 8:(i + 1) * 8, :] = rows / norm


def orthonormal(matrix):
    rows = matrix.T
    done = pl.pallas_call(
        gram_schmidt_kernel,
        out_shape=jax.ShapeDtypeStruct(rows.shape, jnp.float32),
        scratch_shapes=[pltpu.VMEM(rows.shape, jnp.float32)],
    )(rows)
    return done.T


def iterate(gram_matrix, basis_set):
    for sweep_index in range(ITERS):
        basis_set = orthonormal(jnp.dot(gram_matrix, basis_set, precision=highest))
    return basis_set


def cross_gram(left_rows, right_rows):
    return lax.dot_general(left_rows, right_rows, (((0,), (0,)), ((), ())), precision=high)


def self_gram(rows):
    upper = lax.reduce_precision(rows, exponent_bits=8, mantissa_bits=7)
    lower = lax.reduce_precision(rows - upper, exponent_bits=8, mantissa_bits=7)
    missing = jnp.sum(lower * lower, axis=0)
    return cross_gram(rows, rows) + jnp.diag(missing)


def on_device(snapshots, coefficient, start_first, start_merge):
    halo_low, halo_high = halos(snapshots, "tx", 2)
    rows_here = snapshots.shape[0] * snapshots.shape[1]
    order_size = snapshots.shape[2]
    modes_count = start_first.shape[1]
    share_count = modes_count // lax.axis_size("run")
    cells_total = rows_here * lax.axis_size("tx")
    member = lax.axis_index("run")
    is_first = member == 0
    own_start = lax.dynamic_slice_in_dim(start_first, member * order_size, order_size, 0)
    own_start = own_start.astype(jnp.float32)
    merge_start = start_merge.astype(jnp.float32)
    if lax.axis_size("tx") % 2:
        first_basis = orthonormal(own_start)
        merge_basis = orthonormal(merge_start)
    else:
        is_even = lax.axis_index("tx") % 2 == 0
        mine = orthonormal(jnp.where(is_even, own_start, merge_start))
        theirs = partner(mine, "tx", 0)
        first_basis = jnp.where(is_even, mine, theirs)
        merge_basis = jnp.where(is_even, theirs, mine)
    own_flux = fluxes(halo_low, snapshots, halo_high, coefficient).reshape(rows_here, order_size)
    half_rows = rows_here // 2
    half_start = member * half_rows
    sent_rows = lax.dynamic_slice_in_dim(own_flux, (1 - member) * half_rows, half_rows, 0)
    other_rows = partner(sent_rows, "run", 0)
    mixed_half = cross_gram(
        lax.dynamic_slice_in_dim(own_flux, half_start, half_rows, 0), other_rows
    )
    mixed_half = jnp.where(is_first, mixed_half, mixed_half.T)
    partial_gram = self_gram(own_flux)
    split = order_size // 2
    packed = jnp.concatenate([partial_gram[:split], partial_gram[split:, split:]], axis=1)
    packed = tree_sum(packed, "tx") / cells_total
    upper = packed[:, split:order_size]
    own_gram = jnp.concatenate(
        [
            jnp.concatenate([packed[:, :split], upper], axis=1),
            jnp.concatenate([upper.T, packed[:, order_size:]], axis=1),
        ],
        axis=0,
    )
    own_gram, mixed_sum = lax.optimization_barrier((own_gram, mixed_half))
    hops = butterfly_steps("tx")
    own_basis = first_basis
    for sweep_index in range(ITERS):
        product = jnp.dot(own_gram, own_basis, precision=highest)
        if hops:
            received = lax.ppermute(mixed_sum, "tx", hops.pop(0))
            own_basis = orthonormal(product)
            own_basis, received = lax.optimization_barrier((own_basis, received))
            mixed_sum = mixed_sum + received
        else:
            own_basis = orthonormal(product)
    if hops:
        received = lax.ppermute(mixed_sum, "tx", hops.pop(0))
        own_modes = jnp.dot(own_flux, own_basis, precision=high)
        own_modes, received = lax.optimization_barrier((own_modes, received))
        mixed_sum = mixed_sum + received
    else:
        own_modes = jnp.dot(own_flux, own_basis, precision=high)
    for route in hops:
        mixed_sum = mixed_sum + lax.ppermute(mixed_sum, "tx", route)
    mixed_gram = mixed_sum + partner(mixed_sum, "run", 0)
    own_block = jnp.dot(own_basis.T, jnp.dot(own_gram, own_basis, precision=highest), precision=highest)
    other_block, other_basis = partner((own_block, own_basis), "run", 0)
    own_modes, mixed_gram, other_block, other_basis = lax.optimization_barrier(
        (own_modes, mixed_gram, other_block, other_basis)
    )
    other_modes = partner(own_modes, "run", 0)
    first_basis_set = jnp.where(is_first, own_basis, other_basis)
    last_basis_set = jnp.where(is_first, other_basis, own_basis)
    mixed_block = jnp.dot(
        first_basis_set.T,
        jnp.dot(mixed_gram / cells_total, last_basis_set, precision=highest),
        precision=highest,
    )
    first_block = jnp.where(is_first, own_block, other_block)
    last_block = jnp.where(is_first, other_block, own_block)
    merge_gram = jnp.concatenate(
        [
            jnp.concatenate([first_block, mixed_block], axis=1),
            jnp.concatenate([mixed_block.T, last_block], axis=1),
        ],
        axis=0,
    )
    rotation = iterate(merge_gram, merge_basis)
    rotation_share = lax.dynamic_slice_in_dim(rotation, member * share_count, share_count, 1)
    top_rows = rotation_share[:modes_count]
    bottom_rows = rotation_share[modes_count:]
    own_rotation = jnp.where(is_first, top_rows, bottom_rows)
    other_rotation = jnp.where(is_first, bottom_rows, top_rows)
    grid_shape = (snapshots.shape[0], snapshots.shape[1], modes_count)
    result = jnp.einsum(
        "xyk,km->xym", own_modes.reshape(grid_shape), own_rotation, precision=high
    ) + jnp.einsum("xyk,km->xym", other_modes.reshape(grid_shape), other_rotation, precision=high)
    return result


def solution(mesh):
    in_specs = (P(("slab", "tx"), None, "run"), P(("slab", "tx"), None), P(), P())
    out_specs = P(("slab", "tx"), None, "run")
    return jax.shard_map(
        on_device, mesh=mesh, in_specs=in_specs, out_specs=out_specs, check_vma=False
    )
```

```python
import jax
import jax.numpy as jnp
from jax import lax
from jax.sharding import PartitionSpec as P
import functools
from jax.experimental import pallas as pl
from jax.experimental.pallas import tpu as pltpu

ITERS = 2


highest = lax.Precision.HIGHEST
high = lax.Precision.HIGH


def halos(block, axis, width):
    count = lax.axis_size(axis)
    forward = [(i, i + 1) for i in range(count - 1)]
    backward = [(target, source) for source, target in forward]
    low = lax.ppermute(lax.slice_in_dim(block, block.shape[0] - width, None, axis=0), axis, forward)
    high = lax.ppermute(lax.slice_in_dim(block, 0, width, axis=0), axis, backward)
    return low, high


def partner(block, axis, stride):
    count = lax.axis_size(axis)
    route = []
    for low in range(count):
        high = low | 1 << stride
        if high != low and high < count:
            route += [(low, high), (high, low)]
    return lax.ppermute(block, axis, route)


def tree_sum(value, axis):
    count = lax.axis_size(axis)
    if count & (count - 1):
        return lax.psum(value, axis)
    step = 1
    while step < count:
        route = [(i, i ^ step) for i in range(count)]
        value = value + lax.ppermute(value, axis, route)
        step *= 2
    return value


def butterfly_steps(axis):
    count = lax.axis_size(axis)
    assert count & (count - 1) == 0
    routes = []
    step = 1
    while step < count:
        routes.append([(i, i ^ step) for i in range(count)])
        step *= 2
    return routes


def fourth_order(values, axis_dim):
    length_kept = values.shape[axis_dim] - 4

    def shifted(offset):
        return lax.slice_in_dim(values, offset, offset + length_kept, axis=axis_dim)

    return (8.0 * (shifted(3) - shifted(1)) - (shifted(4) - shifted(0))) / 12.0


def flux_kernel(count, low_ref, high_ref, prev_ref, main_ref, next_ref, coef_ref, out_ref):
    i = pl.program_id(0)
    above = jnp.where(i == 0, low_ref[...], prev_ref[-2:])
    below = jnp.where(i == count - 1, high_ref[...], next_ref[:2])
    rows = jnp.concatenate([above, main_ref[...], below], axis=0).astype(jnp.float32)
    squared = 0.5 * jnp.square(rows)
    along_rows = fourth_order(squared, 0)
    mid = squared[2:-2]
    cols = mid.shape[1]
    ids = lax.broadcasted_iota(jnp.int32, mid.shape, 1)

    def shift(offset):
        moved = pltpu.roll(mid, (-offset) % cols, 1)
        inside = (ids + offset >= 0) & (ids + offset < cols)
        return jnp.where(inside, moved, 0.0)

    along_cols = (8.0 * (shift(1) - shift(-1)) - (shift(2) - shift(-2))) / 12.0
    central = rows[2:-2]
    out_ref[...] = central - coef_ref[...][:, :, None] * (along_rows + along_cols)


def fluxes(low, block, high, coefficient):
    nx, ny, ns = block.shape
    bx = 8 if nx % 8 == 0 else nx
    count = nx // bx

    def spec(index):
        return pl.BlockSpec((bx, ny, ns), index)

    return pl.pallas_call(
        functools.partial(flux_kernel, count),
        grid=(count,),
        in_specs=[
            pl.BlockSpec(low.shape, lambda i: (0, 0, 0)),
            pl.BlockSpec(high.shape, lambda i: (0, 0, 0)),
            spec(lambda i: (jnp.maximum(i - 1, 0), 0, 0)),
            spec(lambda i: (i, 0, 0)),
            spec(lambda i: (jnp.minimum(i + 1, count - 1), 0, 0)),
            pl.BlockSpec((bx, ny), lambda i: (i, 0)),
        ],
        out_specs=spec(lambda i: (i, 0, 0)),
        out_shape=jax.ShapeDtypeStruct((nx, ny, ns), jnp.float32),
    )(low, high, block, block, block, coefficient)


def gram_schmidt_kernel(rows_ref, out_ref, work):
    count, width = rows_ref.shape
    blocks = count // 8
    group = 4 if blocks % 4 == 0 else 1
    work[...] = rows_ref[...]
    for first in range(0, blocks, group):

        def sweep(block, carry, first=first):
            base = pl.multiple_of(block * 8, 8)
            pivot_rows = work[pl.ds(base, 8), :]
            for lane_row in range(8):
                j = base + lane_row
                vector = pivot_rows[lane_row:lane_row + 1, :]
                inverse = 1.0 / jnp.sum(vector * vector, axis=1, keepdims=True)
                weight = jnp.sum(pivot_rows * vector, axis=1, keepdims=True) * inverse
                ids = lax.broadcasted_iota(jnp.int32, weight.shape, 0)
                weight = jnp.where(ids > lane_row, weight, 0.0)
                pivot_rows = pivot_rows - weight * vector
                for i in range(first, blocks):
                    rows = work[i * 8:(i + 1) * 8, :]
                    weight = jnp.sum(rows * vector, axis=1, keepdims=True) * inverse
                    ids = lax.broadcasted_iota(jnp.int32, weight.shape, 0) + i * 8
                    weight = jnp.where(ids > j, weight, 0.0)
                    work[i * 8:(i + 1) * 8, :] = rows - weight * vector
            work[pl.ds(base, 8), :] = pivot_rows
            return carry

        lax.fori_loop(first, first + group, sweep, 0)
    for i in range(blocks):
        rows = work[i * 8:(i + 1) * 8, :]
        norm = jnp.sqrt(jnp.sum(rows * rows, axis=1, keepdims=True))
        out_ref[i * 8:(i + 1) * 8, :] = rows / norm


def orthonormal(matrix):
    rows = matrix.T
    done = pl.pallas_call(
        gram_schmidt_kernel,
        out_shape=jax.ShapeDtypeStruct(rows.shape, jnp.float32),
        scratch_shapes=[pltpu.VMEM(rows.shape, jnp.float32)],
    )(rows)
    return done.T


def iterate(gram_matrix, basis_set):
    for sweep_index in range(ITERS):
        basis_set = orthonormal(jnp.dot(gram_matrix, basis_set, precision=high))
    return basis_set


def cross_gram(left_rows, right_rows):
    return lax.dot_general(left_rows, right_rows, (((0,), (0,)), ((), ())), precision=high)


def self_gram(rows):
    upper = lax.reduce_precision(rows, exponent_bits=8, mantissa_bits=7)
    lower = lax.reduce_precision(rows - upper, exponent_bits=8, mantissa_bits=7)
    missing = jnp.sum(lower * lower, axis=0)
    return cross_gram(rows, rows) + jnp.diag(missing)


def on_device(snapshots, coefficient, start_first, start_merge):
    halo_low, halo_high = halos(snapshots, "tx", 2)
    rows_here = snapshots.shape[0] * snapshots.shape[1]
    order_size = snapshots.shape[2]
    modes_count = start_first.shape[1]
    share_count = modes_count // lax.axis_size("run")
    cells_total = rows_here * lax.axis_size("tx")
    member = lax.axis_index("run")
    is_first = member == 0
    own_start = lax.dynamic_slice_in_dim(start_first, member * order_size, order_size, 0)
    own_start = own_start.astype(jnp.float32)
    merge_start = start_merge.astype(jnp.float32)
    if lax.axis_size("tx") % 2:
        first_basis = orthonormal(own_start)
        merge_basis = orthonormal(merge_start)
    else:
        is_even = lax.axis_index("tx") % 2 == 0
        mine = orthonormal(jnp.where(is_even, own_start, merge_start))
        theirs = partner(mine, "tx", 0)
        first_basis = jnp.where(is_even, mine, theirs)
        merge_basis = jnp.where(is_even, theirs, mine)
    own_flux = fluxes(halo_low, snapshots, halo_high, coefficient).reshape(rows_here, order_size)
    half_rows = rows_here // 2
    half_start = member * half_rows
    sent_rows = lax.dynamic_slice_in_dim(own_flux, (1 - member) * half_rows, half_rows, 0)
    other_rows = partner(sent_rows, "run", 0)
    mixed_half = cross_gram(
        lax.dynamic_slice_in_dim(own_flux, half_start, half_rows, 0), other_rows
    )
    mixed_half = jnp.where(is_first, mixed_half, mixed_half.T)
    partial_gram = self_gram(own_flux)
    split = order_size // 2
    packed = jnp.concatenate([partial_gram[:split], partial_gram[split:, split:]], axis=1)
    packed = tree_sum(packed, "tx") / cells_total
    upper = packed[:, split:order_size]
    own_gram = jnp.concatenate(
        [
            jnp.concatenate([packed[:, :split], upper], axis=1),
            jnp.concatenate([upper.T, packed[:, order_size:]], axis=1),
        ],
        axis=0,
    )
    own_gram, mixed_sum = lax.optimization_barrier((own_gram, mixed_half))
    hops = butterfly_steps("tx")
    own_basis = first_basis
    for sweep_index in range(ITERS):
        product = jnp.dot(own_gram, own_basis, precision=high)
        if hops:
            received = lax.ppermute(mixed_sum, "tx", hops.pop(0))
            own_basis = orthonormal(product)
            own_basis, received = lax.optimization_barrier((own_basis, received))
            mixed_sum = mixed_sum + received
        else:
            own_basis = orthonormal(product)
    if hops:
        received = lax.ppermute(mixed_sum, "tx", hops.pop(0))
        own_modes = jnp.dot(own_flux, own_basis, precision=high)
        own_modes, received = lax.optimization_barrier((own_modes, received))
        mixed_sum = mixed_sum + received
    else:
        own_modes = jnp.dot(own_flux, own_basis, precision=high)
    for route in hops:
        mixed_sum = mixed_sum + lax.ppermute(mixed_sum, "tx", route)
    mixed_gram = mixed_sum + partner(mixed_sum, "run", 0)
    own_block = jnp.dot(own_basis.T, jnp.dot(own_gram, own_basis, precision=highest), precision=highest)
    other_block, other_basis = partner((own_block, own_basis), "run", 0)
    own_modes, mixed_gram, other_block, other_basis = lax.optimization_barrier(
        (own_modes, mixed_gram, other_block, other_basis)
    )
    other_modes = partner(own_modes, "run", 0)
    first_basis_set = jnp.where(is_first, own_basis, other_basis)
    last_basis_set = jnp.where(is_first, other_basis, own_basis)
    mixed_block = jnp.dot(
        first_basis_set.T,
        jnp.dot(mixed_gram / cells_total, last_basis_set, precision=highest),
        precision=highest,
    )
    first_block = jnp.where(is_first, own_block, other_block)
    last_block = jnp.where(is_first, other_block, own_block)
    merge_gram = jnp.concatenate(
        [
            jnp.concatenate([first_block, mixed_block], axis=1),
            jnp.concatenate([mixed_block.T, last_block], axis=1),
        ],
        axis=0,
    )
    rotation = iterate(merge_gram, merge_basis)
    rotation_share = lax.dynamic_slice_in_dim(rotation, member * share_count, share_count, 1)
    top_rows = rotation_share[:modes_count]
    bottom_rows = rotation_share[modes_count:]
    own_rotation = jnp.where(is_first, top_rows, bottom_rows)
    other_rotation = jnp.where(is_first, bottom_rows, top_rows)
    grid_shape = (snapshots.shape[0], snapshots.shape[1], modes_count)
    result = jnp.einsum(
        "xyk,km->xym", own_modes.reshape(grid_shape), own_rotation, precision=high
    ) + jnp.einsum("xyk,km->xym", other_modes.reshape(grid_shape), other_rotation, precision=high)
    return result


def solution(mesh):
    in_specs = (P(("slab", "tx"), None, "run"), P(("slab", "tx"), None), P(), P())
    out_specs = P(("slab", "tx"), None, "run")
    return jax.shard_map(
        on_device, mesh=mesh, in_specs=in_specs, out_specs=out_specs, check_vma=False
    )
```

```python
import jax
import jax.numpy as jnp
from jax import lax
from jax.sharding import PartitionSpec as P
import functools
from jax.experimental import pallas as pl
from jax.experimental.pallas import tpu as pltpu

ITERS = 2


highest = lax.Precision.HIGHEST
high = lax.Precision.HIGH


def halos(block, axis, width):
    count = lax.axis_size(axis)
    forward = [(i, i + 1) for i in range(count - 1)]
    backward = [(target, source) for source, target in forward]
    low = lax.ppermute(lax.slice_in_dim(block, block.shape[0] - width, None, axis=0), axis, forward)
    high = lax.ppermute(lax.slice_in_dim(block, 0, width, axis=0), axis, backward)
    return low, high


def partner(block, axis, stride):
    count = lax.axis_size(axis)
    route = []
    for low in range(count):
        high = low | 1 << stride
        if high != low and high < count:
            route += [(low, high), (high, low)]
    return lax.ppermute(block, axis, route)


def tree_sum(value, axis):
    count = lax.axis_size(axis)
    if count & (count - 1):
        return lax.psum(value, axis)
    step = 1
    while step < count:
        route = [(i, i ^ step) for i in range(count)]
        value = value + lax.ppermute(value, axis, route)
        step *= 2
    return value


def butterfly_steps(axis):
    count = lax.axis_size(axis)
    assert count & (count - 1) == 0
    routes = []
    step = 1
    while step < count:
        routes.append([(i, i ^ step) for i in range(count)])
        step *= 2
    return routes


def fourth_order(values, axis_dim):
    length_kept = values.shape[axis_dim] - 4

    def shifted(offset):
        return lax.slice_in_dim(values, offset, offset + length_kept, axis=axis_dim)

    return (8.0 * (shifted(3) - shifted(1)) - (shifted(4) - shifted(0))) / 12.0


def flux_kernel(count, low_ref, high_ref, prev_ref, main_ref, next_ref, coef_ref, out_ref):
    i = pl.program_id(0)
    above = jnp.where(i == 0, low_ref[...], prev_ref[-2:])
    below = jnp.where(i == count - 1, high_ref[...], next_ref[:2])
    rows = jnp.concatenate([above, main_ref[...], below], axis=0).astype(jnp.float32)
    squared = 0.5 * jnp.square(rows)
    along_rows = fourth_order(squared, 0)
    mid = squared[2:-2]
    cols = mid.shape[1]
    ids = lax.broadcasted_iota(jnp.int32, mid.shape, 1)

    def shift(offset):
        moved = pltpu.roll(mid, (-offset) % cols, 1)
        inside = (ids + offset >= 0) & (ids + offset < cols)
        return jnp.where(inside, moved, 0.0)

    along_cols = (8.0 * (shift(1) - shift(-1)) - (shift(2) - shift(-2))) / 12.0
    central = rows[2:-2]
    out_ref[...] = central - coef_ref[...][:, :, None] * (along_rows + along_cols)


def fluxes(low, block, high, coefficient):
    nx, ny, ns = block.shape
    bx = 8 if nx % 8 == 0 else nx
    count = nx // bx

    def spec(index):
        return pl.BlockSpec((bx, ny, ns), index)

    return pl.pallas_call(
        functools.partial(flux_kernel, count),
        grid=(count,),
        in_specs=[
            pl.BlockSpec(low.shape, lambda i: (0, 0, 0)),
            pl.BlockSpec(high.shape, lambda i: (0, 0, 0)),
            spec(lambda i: (jnp.maximum(i - 1, 0), 0, 0)),
            spec(lambda i: (i, 0, 0)),
            spec(lambda i: (jnp.minimum(i + 1, count - 1), 0, 0)),
            pl.BlockSpec((bx, ny), lambda i: (i, 0)),
        ],
        out_specs=spec(lambda i: (i, 0, 0)),
        out_shape=jax.ShapeDtypeStruct((nx, ny, ns), jnp.float32),
    )(low, high, block, block, block, coefficient)


def gram_schmidt_kernel(rows_ref, out_ref, work):
    count, width = rows_ref.shape
    blocks = count // 8
    group = 2 if blocks % 2 == 0 else 1
    work[...] = rows_ref[...]
    for first in range(0, blocks, group):

        def sweep(block, carry, first=first):
            base = pl.multiple_of(block * 8, 8)
            pivot_rows = work[pl.ds(base, 8), :]
            for lane_row in range(8):
                j = base + lane_row
                vector = pivot_rows[lane_row:lane_row + 1, :]
                inverse = 1.0 / jnp.sum(vector * vector, axis=1, keepdims=True)
                weight = jnp.sum(pivot_rows * vector, axis=1, keepdims=True) * inverse
                ids = lax.broadcasted_iota(jnp.int32, weight.shape, 0)
                weight = jnp.where(ids > lane_row, weight, 0.0)
                pivot_rows = pivot_rows - weight * vector
                for i in range(first, blocks):
                    rows = work[i * 8:(i + 1) * 8, :]
                    weight = jnp.sum(rows * vector, axis=1, keepdims=True) * inverse
                    ids = lax.broadcasted_iota(jnp.int32, weight.shape, 0) + i * 8
                    weight = jnp.where(ids > j, weight, 0.0)
                    work[i * 8:(i + 1) * 8, :] = rows - weight * vector
            work[pl.ds(base, 8), :] = pivot_rows
            return carry

        lax.fori_loop(first, first + group, sweep, 0)
    for i in range(blocks):
        rows = work[i * 8:(i + 1) * 8, :]
        norm = jnp.sqrt(jnp.sum(rows * rows, axis=1, keepdims=True))
        out_ref[i * 8:(i + 1) * 8, :] = rows / norm


def orthonormal(matrix):
    rows = matrix.T
    done = pl.pallas_call(
        gram_schmidt_kernel,
        out_shape=jax.ShapeDtypeStruct(rows.shape, jnp.float32),
        scratch_shapes=[pltpu.VMEM(rows.shape, jnp.float32)],
    )(rows)
    return done.T


def iterate(gram_matrix, basis_set):
    for sweep_index in range(ITERS):
        basis_set = orthonormal(jnp.dot(gram_matrix, basis_set, precision=highest))
    return basis_set


def cross_gram(left_rows, right_rows):
    return lax.dot_general(left_rows, right_rows, (((0,), (0,)), ((), ())), precision=high)


def self_gram(rows):
    upper = lax.reduce_precision(rows, exponent_bits=8, mantissa_bits=7)
    lower = lax.reduce_precision(rows - upper, exponent_bits=8, mantissa_bits=7)
    missing = jnp.sum(lower * lower, axis=0)
    return cross_gram(rows, rows) + jnp.diag(missing)


def on_device(snapshots, coefficient, start_first, start_merge):
    halo_low, halo_high = halos(snapshots, "tx", 2)
    rows_here = snapshots.shape[0] * snapshots.shape[1]
    order_size = snapshots.shape[2]
    modes_count = start_first.shape[1]
    share_count = modes_count // lax.axis_size("run")
    cells_total = rows_here * lax.axis_size("tx")
    member = lax.axis_index("run")
    is_first = member == 0
    own_start = lax.dynamic_slice_in_dim(start_first, member * order_size, order_size, 0)
    own_start = own_start.astype(jnp.float32)
    merge_start = start_merge.astype(jnp.float32)
    if lax.axis_size("tx") % 2:
        first_basis = orthonormal(own_start)
        merge_basis = orthonormal(merge_start)
    else:
        is_even = lax.axis_index("tx") % 2 == 0
        mine = orthonormal(jnp.where(is_even, own_start, merge_start))
        theirs = partner(mine, "tx", 0)
        first_basis = jnp.where(is_even, mine, theirs)
        merge_basis = jnp.where(is_even, theirs, mine)
    own_flux = fluxes(halo_low, snapshots, halo_high, coefficient).reshape(rows_here, order_size)
    half_rows = rows_here // 2
    half_start = member * half_rows
    sent_rows = lax.dynamic_slice_in_dim(own_flux, (1 - member) * half_rows, half_rows, 0)
    other_rows = partner(sent_rows, "run", 0)
    mixed_half = cross_gram(
        lax.dynamic_slice_in_dim(own_flux, half_start, half_rows, 0), other_rows
    )
    mixed_half = jnp.where(is_first, mixed_half, mixed_half.T)
    partial_gram = self_gram(own_flux)
    split = order_size // 2
    packed = jnp.concatenate([partial_gram[:split], partial_gram[split:, split:]], axis=1)
    packed = tree_sum(packed, "tx") / cells_total
    upper = packed[:, split:order_size]
    own_gram = jnp.concatenate(
        [
            jnp.concatenate([packed[:, :split], upper], axis=1),
            jnp.concatenate([upper.T, packed[:, order_size:]], axis=1),
        ],
        axis=0,
    )
    own_gram, mixed_sum = lax.optimization_barrier((own_gram, mixed_half))
    hops = butterfly_steps("tx")
    own_basis = first_basis
    for sweep_index in range(ITERS):
        product = jnp.dot(own_gram, own_basis, precision=highest)
        if hops:
            received = lax.ppermute(mixed_sum, "tx", hops.pop(0))
            own_basis = orthonormal(product)
            own_basis, received = lax.optimization_barrier((own_basis, received))
            mixed_sum = mixed_sum + received
        else:
            own_basis = orthonormal(product)
    if hops:
        received = lax.ppermute(mixed_sum, "tx", hops.pop(0))
        own_modes = jnp.dot(own_flux, own_basis, precision=high)
        own_modes, received = lax.optimization_barrier((own_modes, received))
        mixed_sum = mixed_sum + received
    else:
        own_modes = jnp.dot(own_flux, own_basis, precision=high)
    for route in hops:
        mixed_sum = mixed_sum + lax.ppermute(mixed_sum, "tx", route)
    mixed_gram = mixed_sum + partner(mixed_sum, "run", 0)
    own_block = jnp.dot(own_basis.T, jnp.dot(own_gram, own_basis, precision=highest), precision=highest)
    other_block, other_basis = partner((own_block, own_basis), "run", 0)
    own_modes, mixed_gram, other_block, other_basis = lax.optimization_barrier(
        (own_modes, mixed_gram, other_block, other_basis)
    )
    other_modes = partner(own_modes, "run", 0)
    first_basis_set = jnp.where(is_first, own_basis, other_basis)
    last_basis_set = jnp.where(is_first, other_basis, own_basis)
    mixed_block = jnp.dot(
        first_basis_set.T,
        jnp.dot(mixed_gram / cells_total, last_basis_set, precision=highest),
        precision=highest,
    )
    first_block = jnp.where(is_first, own_block, other_block)
    last_block = jnp.where(is_first, other_block, own_block)
    merge_gram = jnp.concatenate(
        [
            jnp.concatenate([first_block, mixed_block], axis=1),
            jnp.concatenate([mixed_block.T, last_block], axis=1),
        ],
        axis=0,
    )
    rotation = iterate(merge_gram, merge_basis)
    rotation_share = lax.dynamic_slice_in_dim(rotation, member * share_count, share_count, 1)
    top_rows = rotation_share[:modes_count]
    bottom_rows = rotation_share[modes_count:]
    own_rotation = jnp.where(is_first, top_rows, bottom_rows)
    other_rotation = jnp.where(is_first, bottom_rows, top_rows)
    result = jnp.dot(own_modes, own_rotation, precision=high) + jnp.dot(
        other_modes, other_rotation, precision=high
    )
    return result.reshape(snapshots.shape[0], snapshots.shape[1], share_count)


def solution(mesh):
    in_specs = (P(("slab", "tx"), None, "run"), P(("slab", "tx"), None), P(), P())
    out_specs = P(("slab", "tx"), None, "run")
    return jax.shard_map(
        on_device, mesh=mesh, in_specs=in_specs, out_specs=out_specs, check_vma=False
    )
```

```python
import jax
import jax.numpy as jnp
from jax import lax
from jax.sharding import PartitionSpec as P
import functools
from jax.experimental import pallas as pl
from jax.experimental.pallas import tpu as pltpu

ITERS = 2


highest = lax.Precision.HIGHEST
high = lax.Precision.HIGH


def halos(block, axis, width):
    count = lax.axis_size(axis)
    forward = [(i, i + 1) for i in range(count - 1)]
    backward = [(target, source) for source, target in forward]
    low = lax.ppermute(lax.slice_in_dim(block, block.shape[0] - width, None, axis=0), axis, forward)
    high = lax.ppermute(lax.slice_in_dim(block, 0, width, axis=0), axis, backward)
    return low, high


def partner(block, axis, stride):
    count = lax.axis_size(axis)
    route = []
    for low in range(count):
        high = low | 1 << stride
        if high != low and high < count:
            route += [(low, high), (high, low)]
    return lax.ppermute(block, axis, route)


def tree_sum(value, axis):
    count = lax.axis_size(axis)
    if count & (count - 1):
        return lax.psum(value, axis)
    step = 1
    while step < count:
        route = [(i, i ^ step) for i in range(count)]
        value = value + lax.ppermute(value, axis, route)
        step *= 2
    return value


def butterfly_steps(axis):
    count = lax.axis_size(axis)
    assert count & (count - 1) == 0
    routes = []
    step = 1
    while step < count:
        routes.append([(i, i ^ step) for i in range(count)])
        step *= 2
    return routes


def fourth_order(values, axis_dim):
    length_kept = values.shape[axis_dim] - 4

    def shifted(offset):
        return lax.slice_in_dim(values, offset, offset + length_kept, axis=axis_dim)

    return (8.0 * (shifted(3) - shifted(1)) - (shifted(4) - shifted(0))) / 12.0


def flux_kernel(count, low_ref, high_ref, prev_ref, main_ref, next_ref, coef_ref, out_ref):
    i = pl.program_id(0)
    above = jnp.where(i == 0, low_ref[...], prev_ref[-2:])
    below = jnp.where(i == count - 1, high_ref[...], next_ref[:2])
    rows = jnp.concatenate([above, main_ref[...], below], axis=0).astype(jnp.float32)
    squared = 0.5 * jnp.square(rows)
    along_rows = fourth_order(squared, 0)
    mid = squared[2:-2]
    cols = mid.shape[1]
    ids = lax.broadcasted_iota(jnp.int32, mid.shape, 1)

    def shift(offset):
        moved = pltpu.roll(mid, (-offset) % cols, 1)
        inside = (ids + offset >= 0) & (ids + offset < cols)
        return jnp.where(inside, moved, 0.0)

    along_cols = (8.0 * (shift(1) - shift(-1)) - (shift(2) - shift(-2))) / 12.0
    central = rows[2:-2]
    out_ref[...] = central - coef_ref[...][:, :, None] * (along_rows + along_cols)


def fluxes(low, block, high, coefficient):
    nx, ny, ns = block.shape
    bx = 16 if nx % 16 == 0 else nx
    count = nx // bx

    def spec(index):
        return pl.BlockSpec((bx, ny, ns), index)

    return pl.pallas_call(
        functools.partial(flux_kernel, count),
        grid=(count,),
        in_specs=[
            pl.BlockSpec(low.shape, lambda i: (0, 0, 0)),
            pl.BlockSpec(high.shape, lambda i: (0, 0, 0)),
            spec(lambda i: (jnp.maximum(i - 1, 0), 0, 0)),
            spec(lambda i: (i, 0, 0)),
            spec(lambda i: (jnp.minimum(i + 1, count - 1), 0, 0)),
            pl.BlockSpec((bx, ny), lambda i: (i, 0)),
        ],
        out_specs=spec(lambda i: (i, 0, 0)),
        out_shape=jax.ShapeDtypeStruct((nx, ny, ns), jnp.float32),
    )(low, high, block, block, block, coefficient)


def gram_schmidt_kernel(rows_ref, out_ref, work):
    count, width = rows_ref.shape
    blocks = count // 8
    group = 4 if blocks % 4 == 0 else 1
    work[...] = rows_ref[...]
    for first in range(0, blocks, group):

        def sweep(block, carry, first=first):
            base = pl.multiple_of(block * 8, 8)
            pivot_rows = work[pl.ds(base, 8), :]
            for lane_row in range(8):
                j = base + lane_row
                vector = pivot_rows[lane_row:lane_row + 1, :]
                inverse = 1.0 / jnp.sum(vector * vector, axis=1, keepdims=True)
                weight = jnp.sum(pivot_rows * vector, axis=1, keepdims=True) * inverse
                ids = lax.broadcasted_iota(jnp.int32, weight.shape, 0)
                weight = jnp.where(ids > lane_row, weight, 0.0)
                pivot_rows = pivot_rows - weight * vector
                for i in range(first, blocks):
                    rows = work[i * 8:(i + 1) * 8, :]
                    weight = jnp.sum(rows * vector, axis=1, keepdims=True) * inverse
                    ids = lax.broadcasted_iota(jnp.int32, weight.shape, 0) + i * 8
                    weight = jnp.where(ids > j, weight, 0.0)
                    work[i * 8:(i + 1) * 8, :] = rows - weight * vector
            work[pl.ds(base, 8), :] = pivot_rows
            return carry

        lax.fori_loop(first, first + group, sweep, 0)
    for i in range(blocks):
        rows = work[i * 8:(i + 1) * 8, :]
        norm = jnp.sqrt(jnp.sum(rows * rows, axis=1, keepdims=True))
        out_ref[i * 8:(i + 1) * 8, :] = rows / norm


def orthonormal(matrix):
    rows = matrix.T
    done = pl.pallas_call(
        gram_schmidt_kernel,
        out_shape=jax.ShapeDtypeStruct(rows.shape, jnp.float32),
        scratch_shapes=[pltpu.VMEM(rows.shape, jnp.float32)],
    )(rows)
    return done.T


def iterate(gram_matrix, basis_set):
    for sweep_index in range(ITERS):
        basis_set = orthonormal(jnp.dot(gram_matrix, basis_set, precision=highest))
    return basis_set


def cross_gram(left_rows, right_rows):
    return lax.dot_general(left_rows, right_rows, (((0,), (0,)), ((), ())), precision=high)


def self_gram(rows):
    upper = lax.reduce_precision(rows, exponent_bits=8, mantissa_bits=7)
    lower = lax.reduce_precision(rows - upper, exponent_bits=8, mantissa_bits=7)
    missing = jnp.sum(lower * lower, axis=0)
    return cross_gram(rows, rows) + jnp.diag(missing)


def on_device(snapshots, coefficient, start_first, start_merge):
    halo_low, halo_high = halos(snapshots, "tx", 2)
    rows_here = snapshots.shape[0] * snapshots.shape[1]
    order_size = snapshots.shape[2]
    modes_count = start_first.shape[1]
    share_count = modes_count // lax.axis_size("run")
    cells_total = rows_here * lax.axis_size("tx")
    member = lax.axis_index("run")
    is_first = member == 0
    own_start = lax.dynamic_slice_in_dim(start_first, member * order_size, order_size, 0)
    own_start = own_start.astype(jnp.float32)
    merge_start = start_merge.astype(jnp.float32)
    if lax.axis_size("tx") % 2:
        first_basis = orthonormal(own_start)
        merge_basis = orthonormal(merge_start)
    else:
        is_even = lax.axis_index("tx") % 2 == 0
        mine = orthonormal(jnp.where(is_even, own_start, merge_start))
        theirs = partner(mine, "tx", 0)
        first_basis = jnp.where(is_even, mine, theirs)
        merge_basis = jnp.where(is_even, theirs, mine)
    own_flux = fluxes(halo_low, snapshots, halo_high, coefficient).reshape(rows_here, order_size)
    half_rows = rows_here // 2
    half_start = member * half_rows
    sent_rows = lax.dynamic_slice_in_dim(own_flux, (1 - member) * half_rows, half_rows, 0)
    other_rows = partner(sent_rows, "run", 0)
    mixed_half = cross_gram(
        lax.dynamic_slice_in_dim(own_flux, half_start, half_rows, 0), other_rows
    )
    mixed_half = jnp.where(is_first, mixed_half, mixed_half.T)
    partial_gram = self_gram(own_flux)
    split = order_size // 2
    packed = jnp.concatenate([partial_gram[:split], partial_gram[split:, split:]], axis=1)
    packed = tree_sum(packed, "tx") / cells_total
    upper = packed[:, split:order_size]
    own_gram = jnp.concatenate(
        [
            jnp.concatenate([packed[:, :split], upper], axis=1),
            jnp.concatenate([upper.T, packed[:, order_size:]], axis=1),
        ],
        axis=0,
    )
    own_gram, mixed_sum = lax.optimization_barrier((own_gram, mixed_half))
    hops = butterfly_steps("tx")
    own_basis = first_basis
    for sweep_index in range(ITERS):
        product = jnp.dot(own_gram, own_basis, precision=highest)
        if hops:
            received = lax.ppermute(mixed_sum, "tx", hops.pop(0))
            own_basis = orthonormal(product)
            own_basis, received = lax.optimization_barrier((own_basis, received))
            mixed_sum = mixed_sum + received
        else:
            own_basis = orthonormal(product)
    if hops:
        received = lax.ppermute(mixed_sum, "tx", hops.pop(0))
        own_modes = jnp.dot(own_flux, own_basis, precision=high)
        own_modes, received = lax.optimization_barrier((own_modes, received))
        mixed_sum = mixed_sum + received
    else:
        own_modes = jnp.dot(own_flux, own_basis, precision=high)
    for route in hops:
        mixed_sum = mixed_sum + lax.ppermute(mixed_sum, "tx", route)
    mixed_gram = mixed_sum + partner(mixed_sum, "run", 0)
    own_block = jnp.dot(own_basis.T, jnp.dot(own_gram, own_basis, precision=highest), precision=highest)
    other_block, other_basis = partner((own_block, own_basis), "run", 0)
    own_modes, mixed_gram, other_block, other_basis = lax.optimization_barrier(
        (own_modes, mixed_gram, other_block, other_basis)
    )
    other_modes = partner(own_modes, "run", 0)
    first_basis_set = jnp.where(is_first, own_basis, other_basis)
    last_basis_set = jnp.where(is_first, other_basis, own_basis)
    mixed_block = jnp.dot(
        first_basis_set.T,
        jnp.dot(mixed_gram / cells_total, last_basis_set, precision=highest),
        precision=highest,
    )
    first_block = jnp.where(is_first, own_block, other_block)
    last_block = jnp.where(is_first, other_block, own_block)
    merge_gram = jnp.concatenate(
        [
            jnp.concatenate([first_block, mixed_block], axis=1),
            jnp.concatenate([mixed_block.T, last_block], axis=1),
        ],
        axis=0,
    )
    rotation = iterate(merge_gram, merge_basis)
    rotation_share = lax.dynamic_slice_in_dim(rotation, member * share_count, share_count, 1)
    top_rows = rotation_share[:modes_count]
    bottom_rows = rotation_share[modes_count:]
    own_rotation = jnp.where(is_first, top_rows, bottom_rows)
    other_rotation = jnp.where(is_first, bottom_rows, top_rows)
    result = jnp.dot(own_modes, own_rotation, precision=high) + jnp.dot(
        other_modes, other_rotation, precision=high
    )
    return result.reshape(snapshots.shape[0], snapshots.shape[1], share_count)


def solution(mesh):
    in_specs = (P(("slab", "tx"), None, "run"), P(("slab", "tx"), None), P(), P())
    out_specs = P(("slab", "tx"), None, "run")
    return jax.shard_map(
        on_device, mesh=mesh, in_specs=in_specs, out_specs=out_specs, check_vma=False
    )
```

```python
import jax
import jax.numpy as jnp
from jax import lax
from jax.sharding import PartitionSpec as P
import functools
from jax.experimental import pallas as pl
from jax.experimental.pallas import tpu as pltpu

ITERS = 2


highest = lax.Precision.HIGHEST
high = lax.Precision.HIGH


def halos(block, axis, width):
    count = lax.axis_size(axis)
    forward = [(i, i + 1) for i in range(count - 1)]
    backward = [(target, source) for source, target in forward]
    low = lax.ppermute(lax.slice_in_dim(block, block.shape[0] - width, None, axis=0), axis, forward)
    high = lax.ppermute(lax.slice_in_dim(block, 0, width, axis=0), axis, backward)
    return low, high


def partner(block, axis, stride):
    count = lax.axis_size(axis)
    route = []
    for low in range(count):
        high = low | 1 << stride
        if high != low and high < count:
            route += [(low, high), (high, low)]
    return lax.ppermute(block, axis, route)


def tree_sum(value, axis):
    count = lax.axis_size(axis)
    if count & (count - 1):
        return lax.psum(value, axis)
    step = 1
    while step < count:
        route = [(i, i ^ step) for i in range(count)]
        value = value + lax.ppermute(value, axis, route)
        step *= 2
    return value


def butterfly_steps(axis):
    count = lax.axis_size(axis)
    assert count & (count - 1) == 0
    routes = []
    step = 1
    while step < count:
        routes.append([(i, i ^ step) for i in range(count)])
        step *= 2
    return routes


def fourth_order(values, axis_dim):
    length_kept = values.shape[axis_dim] - 4

    def shifted(offset):
        return lax.slice_in_dim(values, offset, offset + length_kept, axis=axis_dim)

    return (8.0 * (shifted(3) - shifted(1)) - (shifted(4) - shifted(0))) / 12.0


def flux_kernel(count, low_ref, high_ref, prev_ref, main_ref, next_ref, coef_ref, out_ref):
    i = pl.program_id(0)
    above = jnp.where(i == 0, low_ref[...], prev_ref[-2:])
    below = jnp.where(i == count - 1, high_ref[...], next_ref[:2])
    rows = jnp.concatenate([above, main_ref[...], below], axis=0).astype(jnp.float32)
    squared = 0.5 * jnp.square(rows)
    along_rows = fourth_order(squared, 0)
    mid = squared[2:-2]
    cols = mid.shape[1]
    ids = lax.broadcasted_iota(jnp.int32, mid.shape, 1)

    def shift(offset):
        moved = pltpu.roll(mid, (-offset) % cols, 1)
        inside = (ids + offset >= 0) & (ids + offset < cols)
        return jnp.where(inside, moved, 0.0)

    along_cols = (8.0 * (shift(1) - shift(-1)) - (shift(2) - shift(-2))) / 12.0
    central = rows[2:-2]
    out_ref[...] = central - coef_ref[...][:, :, None] * (along_rows + along_cols)


def fluxes(low, block, high, coefficient):
    nx, ny, ns = block.shape
    bx = 32 if nx % 32 == 0 else nx
    count = nx // bx

    def spec(index):
        return pl.BlockSpec((bx, ny, ns), index)

    return pl.pallas_call(
        functools.partial(flux_kernel, count),
        grid=(count,),
        in_specs=[
            pl.BlockSpec(low.shape, lambda i: (0, 0, 0)),
            pl.BlockSpec(high.shape, lambda i: (0, 0, 0)),
            spec(lambda i: (jnp.maximum(i - 1, 0), 0, 0)),
            spec(lambda i: (i, 0, 0)),
            spec(lambda i: (jnp.minimum(i + 1, count - 1), 0, 0)),
            pl.BlockSpec((bx, ny), lambda i: (i, 0)),
        ],
        out_specs=spec(lambda i: (i, 0, 0)),
        out_shape=jax.ShapeDtypeStruct((nx, ny, ns), jnp.float32),
    )(low, high, block, block, block, coefficient)


def gram_schmidt_kernel(rows_ref, out_ref, work):
    count, width = rows_ref.shape
    blocks = count // 8
    group = 4 if blocks % 4 == 0 else 1
    work[...] = rows_ref[...]
    for first in range(0, blocks, group):

        def sweep(block, carry, first=first):
            base = pl.multiple_of(block * 8, 8)
            pivot_rows = work[pl.ds(base, 8), :]
            for lane_row in range(8):
                j = base + lane_row
                vector = pivot_rows[lane_row:lane_row + 1, :]
                inverse = 1.0 / jnp.sum(vector * vector, axis=1, keepdims=True)
                weight = jnp.sum(pivot_rows * vector, axis=1, keepdims=True) * inverse
                ids = lax.broadcasted_iota(jnp.int32, weight.shape, 0)
                weight = jnp.where(ids > lane_row, weight, 0.0)
                pivot_rows = pivot_rows - weight * vector
                for i in range(first, blocks):
                    rows = work[i * 8:(i + 1) * 8, :]
                    weight = jnp.sum(rows * vector, axis=1, keepdims=True) * inverse
                    ids = lax.broadcasted_iota(jnp.int32, weight.shape, 0) + i * 8
                    weight = jnp.where(ids > j, weight, 0.0)
                    work[i * 8:(i + 1) * 8, :] = rows - weight * vector
            work[pl.ds(base, 8), :] = pivot_rows
            return carry

        lax.fori_loop(first, first + group, sweep, 0)
    for i in range(blocks):
        rows = work[i * 8:(i + 1) * 8, :]
        norm = jnp.sqrt(jnp.sum(rows * rows, axis=1, keepdims=True))
        out_ref[i * 8:(i + 1) * 8, :] = rows / norm


def orthonormal(matrix):
    rows = matrix.T
    done = pl.pallas_call(
        gram_schmidt_kernel,
        out_shape=jax.ShapeDtypeStruct(rows.shape, jnp.float32),
        scratch_shapes=[pltpu.VMEM(rows.shape, jnp.float32)],
    )(rows)
    return done.T


def iterate(gram_matrix, basis_set):
    for sweep_index in range(ITERS):
        basis_set = orthonormal(jnp.dot(gram_matrix, basis_set, precision=highest))
    return basis_set


def cross_gram(left_rows, right_rows):
    return lax.dot_general(left_rows, right_rows, (((0,), (0,)), ((), ())), precision=high)


def self_gram(rows):
    upper = lax.reduce_precision(rows, exponent_bits=8, mantissa_bits=7)
    lower = lax.reduce_precision(rows - upper, exponent_bits=8, mantissa_bits=7)
    missing = jnp.sum(lower * lower, axis=0)
    return cross_gram(rows, rows) + jnp.diag(missing)


def on_device(snapshots, coefficient, start_first, start_merge):
    halo_low, halo_high = halos(snapshots, "tx", 2)
    rows_here = snapshots.shape[0] * snapshots.shape[1]
    order_size = snapshots.shape[2]
    modes_count = start_first.shape[1]
    share_count = modes_count // lax.axis_size("run")
    cells_total = rows_here * lax.axis_size("tx")
    member = lax.axis_index("run")
    is_first = member == 0
    own_start = lax.dynamic_slice_in_dim(start_first, member * order_size, order_size, 0)
    own_start = own_start.astype(jnp.float32)
    merge_start = start_merge.astype(jnp.float32)
    if lax.axis_size("tx") % 2:
        first_basis = orthonormal(own_start)
        merge_basis = orthonormal(merge_start)
    else:
        is_even = lax.axis_index("tx") % 2 == 0
        mine = orthonormal(jnp.where(is_even, own_start, merge_start))
        theirs = partner(mine, "tx", 0)
        first_basis = jnp.where(is_even, mine, theirs)
        merge_basis = jnp.where(is_even, theirs, mine)
    own_flux = fluxes(halo_low, snapshots, halo_high, coefficient).reshape(rows_here, order_size)
    half_rows = rows_here // 2
    half_start = member * half_rows
    sent_rows = lax.dynamic_slice_in_dim(own_flux, (1 - member) * half_rows, half_rows, 0)
    other_rows = partner(sent_rows, "run", 0)
    mixed_half = cross_gram(
        lax.dynamic_slice_in_dim(own_flux, half_start, half_rows, 0), other_rows
    )
    mixed_half = jnp.where(is_first, mixed_half, mixed_half.T)
    partial_gram = self_gram(own_flux)
    split = order_size // 2
    packed = jnp.concatenate([partial_gram[:split], partial_gram[split:, split:]], axis=1)
    packed = tree_sum(packed, "tx") / cells_total
    upper = packed[:, split:order_size]
    own_gram = jnp.concatenate(
        [
            jnp.concatenate([packed[:, :split], upper], axis=1),
            jnp.concatenate([upper.T, packed[:, order_size:]], axis=1),
        ],
        axis=0,
    )
    own_gram, mixed_sum = lax.optimization_barrier((own_gram, mixed_half))
    hops = butterfly_steps("tx")
    own_basis = first_basis
    for sweep_index in range(ITERS):
        product = jnp.dot(own_gram, own_basis, precision=highest)
        if hops:
            received = lax.ppermute(mixed_sum, "tx", hops.pop(0))
            own_basis = orthonormal(product)
            own_basis, received = lax.optimization_barrier((own_basis, received))
            mixed_sum = mixed_sum + received
        else:
            own_basis = orthonormal(product)
    if hops:
        received = lax.ppermute(mixed_sum, "tx", hops.pop(0))
        own_modes = jnp.dot(own_flux, own_basis, precision=high)
        own_modes, received = lax.optimization_barrier((own_modes, received))
        mixed_sum = mixed_sum + received
    else:
        own_modes = jnp.dot(own_flux, own_basis, precision=high)
    for route in hops:
        mixed_sum = mixed_sum + lax.ppermute(mixed_sum, "tx", route)
    mixed_gram = mixed_sum + partner(mixed_sum, "run", 0)
    own_block = jnp.dot(own_basis.T, jnp.dot(own_gram, own_basis, precision=highest), precision=highest)
    other_block, other_basis = partner((own_block, own_basis), "run", 0)
    own_modes, mixed_gram, other_block, other_basis = lax.optimization_barrier(
        (own_modes, mixed_gram, other_block, other_basis)
    )
    other_modes = partner(own_modes, "run", 0)
    first_basis_set = jnp.where(is_first, own_basis, other_basis)
    last_basis_set = jnp.where(is_first, other_basis, own_basis)
    mixed_block = jnp.dot(
        first_basis_set.T,
        jnp.dot(mixed_gram / cells_total, last_basis_set, precision=highest),
        precision=highest,
    )
    first_block = jnp.where(is_first, own_block, other_block)
    last_block = jnp.where(is_first, other_block, own_block)
    merge_gram = jnp.concatenate(
        [
            jnp.concatenate([first_block, mixed_block], axis=1),
            jnp.concatenate([mixed_block.T, last_block], axis=1),
        ],
        axis=0,
    )
    rotation = iterate(merge_gram, merge_basis)
    rotation_share = lax.dynamic_slice_in_dim(rotation, member * share_count, share_count, 1)
    top_rows = rotation_share[:modes_count]
    bottom_rows = rotation_share[modes_count:]
    own_rotation = jnp.where(is_first, top_rows, bottom_rows)
    other_rotation = jnp.where(is_first, bottom_rows, top_rows)
    result = jnp.dot(own_modes, own_rotation, precision=high) + jnp.dot(
        other_modes, other_rotation, precision=high
    )
    return result.reshape(snapshots.shape[0], snapshots.shape[1], share_count)


def solution(mesh):
    in_specs = (P(("slab", "tx"), None, "run"), P(("slab", "tx"), None), P(), P())
    out_specs = P(("slab", "tx"), None, "run")
    return jax.shard_map(
        on_device, mesh=mesh, in_specs=in_specs, out_specs=out_specs, check_vma=False
    )
```

```python
import jax
import jax.numpy as jnp
from jax import lax
from jax.sharding import PartitionSpec as P
import functools
from jax.experimental import pallas as pl
from jax.experimental.pallas import tpu as pltpu

ITERS = 2


highest = lax.Precision.HIGHEST
high = lax.Precision.HIGH


def halos(block, axis, width):
    count = lax.axis_size(axis)
    forward = [(i, i + 1) for i in range(count - 1)]
    backward = [(target, source) for source, target in forward]
    low = lax.ppermute(lax.slice_in_dim(block, block.shape[0] - width, None, axis=0), axis, forward)
    high = lax.ppermute(lax.slice_in_dim(block, 0, width, axis=0), axis, backward)
    return low, high


def partner(block, axis, stride):
    count = lax.axis_size(axis)
    route = []
    for low in range(count):
        high = low | 1 << stride
        if high != low and high < count:
            route += [(low, high), (high, low)]
    return lax.ppermute(block, axis, route)


def tree_sum(value, axis):
    count = lax.axis_size(axis)
    if count & (count - 1):
        return lax.psum(value, axis)
    step = 1
    while step < count:
        route = [(i, i ^ step) for i in range(count)]
        value = value + lax.ppermute(value, axis, route)
        step *= 2
    return value


def butterfly_steps(axis):
    count = lax.axis_size(axis)
    assert count & (count - 1) == 0
    routes = []
    step = 1
    while step < count:
        routes.append([(i, i ^ step) for i in range(count)])
        step *= 2
    return routes


def fourth_order(values, axis_dim):
    length_kept = values.shape[axis_dim] - 4

    def shifted(offset):
        return lax.slice_in_dim(values, offset, offset + length_kept, axis=axis_dim)

    return (8.0 * (shifted(3) - shifted(1)) - (shifted(4) - shifted(0))) / 12.0


def flux_kernel(count, low_ref, high_ref, prev_ref, main_ref, next_ref, coef_ref, out_ref):
    i = pl.program_id(0)
    above = jnp.where(i == 0, low_ref[...], prev_ref[-2:])
    below = jnp.where(i == count - 1, high_ref[...], next_ref[:2])
    rows = jnp.concatenate([above, main_ref[...], below], axis=0).astype(jnp.float32)
    squared = 0.5 * jnp.square(rows)
    along_rows = fourth_order(squared, 0)
    mid = squared[2:-2]
    cols = mid.shape[1]
    ids = lax.broadcasted_iota(jnp.int32, mid.shape, 1)

    def shift(offset):
        moved = pltpu.roll(mid, (-offset) % cols, 1)
        inside = (ids + offset >= 0) & (ids + offset < cols)
        return jnp.where(inside, moved, 0.0)

    along_cols = (8.0 * (shift(1) - shift(-1)) - (shift(2) - shift(-2))) / 12.0
    central = rows[2:-2]
    out_ref[...] = central - coef_ref[...][:, :, None] * (along_rows + along_cols)


def fluxes(low, block, high, coefficient):
    nx, ny, ns = block.shape
    bx = 16 if nx % 16 == 0 else nx
    count = nx // bx

    def spec(index):
        return pl.BlockSpec((bx, ny, ns), index)

    return pl.pallas_call(
        functools.partial(flux_kernel, count),
        grid=(count,),
        in_specs=[
            pl.BlockSpec(low.shape, lambda i: (0, 0, 0)),
            pl.BlockSpec(high.shape, lambda i: (0, 0, 0)),
            spec(lambda i: (jnp.maximum(i - 1, 0), 0, 0)),
            spec(lambda i: (i, 0, 0)),
            spec(lambda i: (jnp.minimum(i + 1, count - 1), 0, 0)),
            pl.BlockSpec((bx, ny), lambda i: (i, 0)),
        ],
        out_specs=spec(lambda i: (i, 0, 0)),
        out_shape=jax.ShapeDtypeStruct((nx, ny, ns), jnp.float32),
    )(low, high, block, block, block, coefficient)


def gram_schmidt_kernel(rows_ref, out_ref, work):
    count, width = rows_ref.shape
    blocks = count // 8
    group = 4 if blocks % 4 == 0 else 1
    work[...] = rows_ref[...]
    for first in range(0, blocks, group):

        def sweep(block, carry, first=first):
            base = pl.multiple_of(block * 8, 8)
            pivot_rows = work[pl.ds(base, 8), :]
            for lane_row in range(8):
                j = base + lane_row
                vector = pivot_rows[lane_row:lane_row + 1, :]
                inverse = 1.0 / jnp.sum(vector * vector, axis=1, keepdims=True)
                weight = jnp.sum(pivot_rows * vector, axis=1, keepdims=True) * inverse
                ids = lax.broadcasted_iota(jnp.int32, weight.shape, 0)
                weight = jnp.where(ids > lane_row, weight, 0.0)
                pivot_rows = pivot_rows - weight * vector
                for i in range(first, blocks):
                    rows = work[i * 8:(i + 1) * 8, :]
                    weight = jnp.sum(rows * vector, axis=1, keepdims=True) * inverse
                    ids = lax.broadcasted_iota(jnp.int32, weight.shape, 0) + i * 8
                    weight = jnp.where(ids > j, weight, 0.0)
                    work[i * 8:(i + 1) * 8, :] = rows - weight * vector
            work[pl.ds(base, 8), :] = pivot_rows
            return carry

        lax.fori_loop(first, first + group, sweep, 0)
    for i in range(blocks):
        rows = work[i * 8:(i + 1) * 8, :]
        norm = jnp.sqrt(jnp.sum(rows * rows, axis=1, keepdims=True))
        out_ref[i * 8:(i + 1) * 8, :] = rows / norm


def orthonormal(matrix):
    rows = matrix.T
    done = pl.pallas_call(
        gram_schmidt_kernel,
        out_shape=jax.ShapeDtypeStruct(rows.shape, jnp.float32),
        scratch_shapes=[pltpu.VMEM(rows.shape, jnp.float32)],
    )(rows)
    return done.T


def iterate(gram_matrix, basis_set):
    for sweep_index in range(ITERS):
        basis_set = orthonormal(jnp.dot(gram_matrix, basis_set, precision=highest))
    return basis_set


def cross_gram(left_rows, right_rows):
    return lax.dot_general(left_rows, right_rows, (((0,), (0,)), ((), ())), precision=high)


def self_gram(rows):
    upper = lax.reduce_precision(rows, exponent_bits=8, mantissa_bits=7)
    lower = lax.reduce_precision(rows - upper, exponent_bits=8, mantissa_bits=7)
    missing = jnp.sum(lower * lower, axis=0)
    return cross_gram(rows, rows) + jnp.diag(missing)


def on_device(snapshots, coefficient, start_first, start_merge):
    halo_low, halo_high = halos(snapshots, "tx", 2)
    rows_here = snapshots.shape[0] * snapshots.shape[1]
    order_size = snapshots.shape[2]
    modes_count = start_first.shape[1]
    share_count = modes_count // lax.axis_size("run")
    cells_total = rows_here * lax.axis_size("tx")
    member = lax.axis_index("run")
    is_first = member == 0
    own_start = lax.dynamic_slice_in_dim(start_first, member * order_size, order_size, 0)
    own_start = own_start.astype(jnp.float32)
    merge_start = start_merge.astype(jnp.float32)
    if lax.axis_size("tx") % 2:
        first_basis = orthonormal(own_start)
        merge_basis = orthonormal(merge_start)
    else:
        is_even = lax.axis_index("tx") % 2 == 0
        mine = orthonormal(jnp.where(is_even, own_start, merge_start))
        theirs = partner(mine, "tx", 0)
        first_basis = jnp.where(is_even, mine, theirs)
        merge_basis = jnp.where(is_even, theirs, mine)
    own_flux = fluxes(halo_low, snapshots, halo_high, coefficient).reshape(rows_here, order_size)
    half_rows = rows_here // 2
    half_start = member * half_rows
    sent_rows = lax.dynamic_slice_in_dim(own_flux, (1 - member) * half_rows, half_rows, 0)
    other_rows = partner(sent_rows, "run", 0)
    mixed_half = cross_gram(
        lax.dynamic_slice_in_dim(own_flux, half_start, half_rows, 0), other_rows
    )
    mixed_half = jnp.where(is_first, mixed_half, mixed_half.T)
    partial_gram = self_gram(own_flux)
    split = order_size // 2
    packed = jnp.concatenate([partial_gram[:split], partial_gram[split:, split:]], axis=1)
    packed = tree_sum(packed, "tx") / cells_total
    upper = packed[:, split:order_size]
    own_gram = jnp.concatenate(
        [
            jnp.concatenate([packed[:, :split], upper], axis=1),
            jnp.concatenate([upper.T, packed[:, order_size:]], axis=1),
        ],
        axis=0,
    )
    own_gram, mixed_sum = lax.optimization_barrier((own_gram, mixed_half))
    hops = butterfly_steps("tx")
    own_basis = first_basis
    for sweep_index in range(ITERS):
        product = jnp.dot(own_gram, own_basis, precision=highest)
        if hops:
            received = lax.ppermute(mixed_sum, "tx", hops.pop(0))
            own_basis = orthonormal(product)
            own_basis, received = lax.optimization_barrier((own_basis, received))
            mixed_sum = mixed_sum + received
        else:
            own_basis = orthonormal(product)
    if hops:
        received = lax.ppermute(mixed_sum, "tx", hops.pop(0))
        own_modes = jnp.dot(own_flux, own_basis, precision=high)
        own_modes, received = lax.optimization_barrier((own_modes, received))
        mixed_sum = mixed_sum + received
    else:
        own_modes = jnp.dot(own_flux, own_basis, precision=high)
    for route in hops:
        mixed_sum = mixed_sum + lax.ppermute(mixed_sum, "tx", route)
    mixed_gram = mixed_sum + partner(mixed_sum, "run", 0)
    own_block = jnp.dot(own_basis.T, jnp.dot(own_gram, own_basis, precision=highest), precision=highest)
    other_block, other_basis = partner((own_block, own_basis), "run", 0)
    own_modes, mixed_gram, other_block, other_basis = lax.optimization_barrier(
        (own_modes, mixed_gram, other_block, other_basis)
    )
    other_modes = partner(own_modes, "run", 0)
    first_basis_set = jnp.where(is_first, own_basis, other_basis)
    last_basis_set = jnp.where(is_first, other_basis, own_basis)
    mixed_block = jnp.dot(
        first_basis_set.T,
        jnp.dot(mixed_gram / cells_total, last_basis_set, precision=highest),
        precision=highest,
    )
    first_block = jnp.where(is_first, own_block, other_block)
    last_block = jnp.where(is_first, other_block, own_block)
    merge_gram = jnp.concatenate(
        [
            jnp.concatenate([first_block, mixed_block], axis=1),
            jnp.concatenate([mixed_block.T, last_block], axis=1),
        ],
        axis=0,
    )
    rotation = iterate(merge_gram, merge_basis)
    rotation_share = lax.dynamic_slice_in_dim(rotation, member * share_count, share_count, 1)
    top_rows = rotation_share[:modes_count]
    bottom_rows = rotation_share[modes_count:]
    own_rotation = jnp.where(is_first, top_rows, bottom_rows)
    other_rotation = jnp.where(is_first, bottom_rows, top_rows)
    grid_shape = (snapshots.shape[0], snapshots.shape[1], modes_count)
    result = jnp.einsum(
        "xyk,km->xym", own_modes.reshape(grid_shape), own_rotation, precision=high
    ) + jnp.einsum("xyk,km->xym", other_modes.reshape(grid_shape), other_rotation, precision=high)
    return result


def solution(mesh):
    in_specs = (P(("slab", "tx"), None, "run"), P(("slab", "tx"), None), P(), P())
    out_specs = P(("slab", "tx"), None, "run")
    return jax.shard_map(
        on_device, mesh=mesh, in_specs=in_specs, out_specs=out_specs, check_vma=False
    )
```
